128 devices in a mesh: chain: 2 (over core), slab: 64 (over z, y, x).
Axes of the slice: x: 4, y: 4, z: 4, core: 2. Of those that a mesh axis runs over, the one named last changes fastest.
Arguments:
- coarse_states: bfloat16 [8, 4, 256, 64, 128], P('chain', None, 'slab'), may hold values from -3 to 3
- accept_flags: int32 [8, 3], P('chain'), may hold values 0 or 1
- owners: int32 [2], replicated, may hold values from 0 to 7, as said below
- kl_coeffs: float32 [2, 32, 16, 64], P('chain'), may hold values from -0.02 to 0.02
- source: float32 [512, 128, 256], P('slab'), may hold values from -18 to 18
Outputs:
- pressure: float32 [2, 512, 128, 256], P('chain', 'slab')
The draws below stay inside these ranges and needn't reach their ends.
Inputs may be any that keep to these rules, and one draw needn't show every extreme that they name: `accept_flags`: 1 means accepted. The owners of different fine chain groups are different coarse chains.
All inputs are finite; a program needn't handle non-finite values. No bound on the sum of `accept_flags` on one device may be relied on, other than what follows from the above.
Results may differ from the reference program's by a relative error of at most 0.0007.
Values may be sent and summed in bfloat16 or wider, within the bound.
No kernel may reach another device: no remote copies, remote signals or barrier semaphores. Data moves between devices by JAX's collectives and lax.ppermute only.
A program may use at most 192 MiB of HBM per device.

```python
import jax
import jax.numpy as jnp
from jax import lax

CY = 64
CX = 128
STEPS = 4
MZ = 32
MY = 16
MX = 64
LEVELS = 4
SWEEPS = 2
BOTTOM = 4
CHAINS = 2
COARSE = 8
CZG = 256
FZG = 512
FY = 128
FX = 256


def draw_owners(key, part):
    order = jax.random.permutation(jax.random.fold_in(key, 7), COARSE - 1)[:CHAINS].astype(jnp.int32)
    marked = jax.random.randint(jax.random.fold_in(key, 11), (), 0, CHAINS, dtype=jnp.int32)
    places = jnp.arange(CHAINS, dtype=jnp.int32)
    return jnp.where(places == marked, COARSE - 1, order).astype(jnp.int32)


def touch_ends(entries, own_key, low, high):
    dims = entries.shape
    spot = [jax.random.randint(jax.random.fold_in(own_key, axis), (), 0, dims[axis]) for axis in range(len(dims))]
    entries = entries.at[tuple(spot)].set(low)
    longest = dims.index(max(dims))
    spot[longest] = (spot[longest] + 1) % dims[longest]
    return entries.at[tuple(spot)].set(high)


def steps_of(key, extent, cuts, least, high):
    def one(axis_at, blocks):
        steps = jax.random.uniform(jax.random.fold_in(jax.random.fold_in(key, 6), axis_at), (blocks,), jnp.float32, least / len(cuts), high / len(cuts))
        return jnp.repeat(jnp.exp(steps), extent[axis_at] // blocks).reshape((-1,) + (1,) * (len(extent) - axis_at - 1))

    loudness = one(*cuts[0])
    for cut in cuts[1:]:
        loudness = loudness * one(*cut)
    return loudness


def normal_values(stream_key, extent, deviation, reach, pieces=(), kind=jnp.bfloat16):
    gain = steps_of(stream_key, extent, pieces, -0.22, 0.18) if pieces else 1.0
    drawn = jax.random.normal(stream_key, extent, jnp.float32) * deviation * gain
    return jnp.minimum(jnp.maximum(drawn, -reach), reach).astype(kind)


def setup_inputs(seed: int = 0) -> dict:
    splits = jax.random.split(jax.random.key(seed), 6)
    return {
        "coarse_states": normal_values(splits[0], (COARSE, STEPS, CZG, CY, CX), 0.5, 3.0, ((0, 2), (2, 64))),
        "accept_flags": touch_ends((jax.random.randint(splits[1], (COARSE, STEPS - 1), 0, 2) < 1).astype(jnp.int32), jax.random.fold_in(splits[1], 1), 0, 1),
        "owners": draw_owners(jax.random.fold_in(splits[5], 71), 0),
        "kl_coeffs": normal_values(splits[3], (CHAINS, MZ, MY, MX), 0.008, 0.02, ((0, 2),), jnp.float32),
        "source": normal_values(splits[4], (FZG, FY, FX), 3.0, 18.0, ((0, 64),), jnp.float32),
    }


OMEGA = 0.8


def pad_axis(values, dim_index):
    widths = [(0, 0), (0, 0), (0, 0)]
    widths[dim_index] = (1, 1)
    return jnp.pad(values, widths)


def local_rims(values):
    return pad_axis(values, 0)


def face_weights(depth_padded, permeability):
    faces_depth = 0.5 * (depth_padded[1:] + depth_padded[:-1])
    rows_padded = pad_axis(permeability, 1)
    faces_rows = 0.5 * (rows_padded[:, 1:] + rows_padded[:, :-1])
    cols_padded = pad_axis(permeability, 2)
    faces_cols = 0.5 * (cols_padded[:, :, 1:] + cols_padded[:, :, :-1])
    diagonal = faces_depth[1:] + faces_depth[:-1] + faces_rows[:, 1:] + faces_rows[:, :-1]
    diagonal = diagonal + faces_cols[:, :, 1:] + faces_cols[:, :, :-1]
    return faces_depth, faces_rows, faces_cols, diagonal


def operate(iterate, coefficients, extender):
    faces_depth, faces_rows, faces_cols, diagonal = coefficients
    deep_pad = extender(iterate)
    rows_pad = pad_axis(iterate, 1)
    cols_pad = pad_axis(iterate, 2)
    neighbours = faces_depth[1:] * deep_pad[2:] + faces_depth[:-1] * deep_pad[:-2]
    neighbours = neighbours + faces_rows[:, 1:] * rows_pad[:, 2:] + faces_rows[:, :-1] * rows_pad[:, :-2]
    neighbours = neighbours + faces_cols[:, :, 1:] * cols_pad[:, :, 2:] + faces_cols[:, :, :-1] * cols_pad[:, :, :-2]
    return diagonal * iterate - neighbours


def jacobi_sweep(iterate, forcing, coefficients, extender):
    return iterate + OMEGA * (forcing - operate(iterate, coefficients, extender)) / coefficients[3]


def smooth_from_zero(forcing, coefficients, extender, sweep_count):
    iterate = OMEGA * forcing / coefficients[3]
    for repeat in range(sweep_count - 1):
        iterate = jacobi_sweep(iterate, forcing, coefficients, extender)
    return iterate


def restrict_sum(values):
    size_z, size_y, size_x = values.shape
    return values.reshape(size_z // 2, 2, size_y // 2, 2, size_x // 2, 2).sum(axis=(1, 3, 5))


def copy_up(values):
    return jnp.repeat(jnp.repeat(jnp.repeat(values, 2, axis=0), 2, axis=1), 2, axis=2)


def vcycle(forcing, permeability, depth_level):
    coefficients = face_weights(local_rims(permeability), permeability)
    if depth_level == LEVELS - 1:
        return smooth_from_zero(forcing, coefficients, local_rims, BOTTOM)
    iterate = smooth_from_zero(forcing, coefficients, local_rims, SWEEPS)
    residual = forcing - operate(iterate, coefficients, local_rims)
    coarse_forcing = 0.5 * restrict_sum(residual)
    coarse_perm = 0.125 * restrict_sum(permeability)
    correction = vcycle(coarse_forcing, coarse_perm, depth_level + 1)
    iterate = iterate + copy_up(correction)
    for repeat in range(SWEEPS):
        iterate = jacobi_sweep(iterate, forcing, coefficients, local_rims)
    return iterate


def prolong_axis(values, low_edge, high_edge, dim_index):
    length_now = values.shape[dim_index]
    leading = jnp.concatenate([low_edge, lax.slice_in_dim(values, 0, length_now - 1, axis=dim_index)], axis=dim_index)
    trailing = jnp.concatenate([lax.slice_in_dim(values, 1, length_now, axis=dim_index), high_edge], axis=dim_index)
    even_cells = 0.75 * values + 0.25 * leading
    odd_cells = 0.75 * values + 0.25 * trailing
    new_shape = list(values.shape)
    new_shape[dim_index] = 2 * length_now
    return jnp.stack((even_cells, odd_cells), axis=dim_index + 1).reshape(new_shape)


def prolong_edges(values, dim_index):
    length_now = values.shape[dim_index]
    low_edge = lax.slice_in_dim(values, 0, 1, axis=dim_index)
    high_edge = lax.slice_in_dim(values, length_now - 1, length_now, axis=dim_index)
    return prolong_axis(values, low_edge, high_edge, dim_index)


def mode_table(mode_count, length, positions):
    frequency = length // 2 + jnp.arange(mode_count, dtype=jnp.int32)
    phases = (frequency[:, None] * (2 * positions[None, :] + 1)) % (4 * length)
    return jnp.cos(jnp.pi * phases.astype(jnp.float32) / (2 * length))


def kl_field(coefficients, depth_table, rows_table, cols_table):
    highest = lax.Precision.HIGHEST
    along_cols = jnp.einsum("abc,cx->abx", coefficients, cols_table, precision=highest)
    along_rows = jnp.einsum("abx,by->ayx", along_cols, rows_table, precision=highest)
    return jnp.einsum("ayx,az->zyx", along_rows, depth_table, precision=highest)


def reference(coarse_states, accept_flags, owners, kl_coeffs, source):
    step_numbers = jnp.arange(1, STEPS, dtype=jnp.int32)
    chosen = jnp.max(jnp.where(accept_flags == 1, step_numbers[None, :], 0), axis=1).astype(jnp.int32)
    depth_table = mode_table(MZ, FZG, jnp.arange(FZG, dtype=jnp.int32))
    rows_table = mode_table(MY, FY, jnp.arange(FY, dtype=jnp.int32))
    cols_table = mode_table(MX, FX, jnp.arange(FX, dtype=jnp.int32))

    def one_group(group_index):
        owner_index = owners[group_index]
        coarse = coarse_states[owner_index, chosen[owner_index]].astype(jnp.float32)
        log_perm = prolong_edges(coarse, 0)
        log_perm = prolong_edges(log_perm, 1)
        log_perm = prolong_edges(log_perm, 2)
        log_perm = log_perm + kl_field(kl_coeffs[group_index], depth_table, rows_table, cols_table)
        return vcycle(source, jnp.exp(log_perm), 0)

    return lax.map(one_group, jnp.arange(CHAINS, dtype=jnp.int32))
```

```python
import numpy as np
import jax
import jax.numpy as jnp
from jax import lax
from jax.sharding import PartitionSpec as P

STEPS = 4
MZ = 32
MY = 16
MX = 64
LEVELS = 4
SWEEPS = 2
BOTTOM = 4

OMEGA = 0.8
HI = lax.Precision.HIGHEST

K0_HALO = 10
F0_HALO = 3
F1_HALO = 4
COARSE_HALO = 6


def pair_sum_matrix(n):
    m = np.zeros((n, n // 2), np.float32)
    m[np.arange(n), np.arange(n) // 2] = 1.0
    return m


def repeat_matrix(n):
    return np.ascontiguousarray(pair_sum_matrix(2 * n).T)


def prolong_matrix(n):
    m = np.zeros((n, 2 * n), np.float32)
    for i in range(n):
        m[i, 2 * i] += 0.75
        m[max(i - 1, 0), 2 * i] += 0.25
        m[i, 2 * i + 1] += 0.75
        m[min(i + 1, n - 1), 2 * i + 1] += 0.25
    return m


def along_x(values, matrix, precision=HI):
    return jnp.einsum("zyx,xw->zyw", values, jnp.asarray(matrix), precision=precision,
                      preferred_element_type=jnp.float32)


def along_y(values, matrix, precision=HI):
    return jnp.einsum("zyx,yv->zvx", values, jnp.asarray(matrix), precision=precision,
                      preferred_element_type=jnp.float32)


def restrict_sum(values):
    nz, ny, nx = values.shape
    values = values.reshape(nz // 2, 2, ny, nx).sum(axis=1)
    values = along_y(values, pair_sum_matrix(ny))
    return along_x(values, pair_sum_matrix(nx))


def copy_up(values):
    nz, ny, nx = values.shape
    values = along_x(values, repeat_matrix(nx))
    values = along_y(values, repeat_matrix(ny))
    return jnp.repeat(values, 2, axis=0)


def shift_from(block, offset):
    count = lax.axis_size("slab")
    pairs = [(i, i + offset) for i in range(count) if 0 <= i + offset < count]
    return lax.ppermute(block, "slab", pairs)


def plane_mask(first_global, planes, total):
    g = first_global + jnp.arange(planes, dtype=jnp.int32)
    return ((g >= 0) & (g < total))[:, None, None]


class Level:
    def __init__(self, k, k_halo, own, first_global, total):
        self.own = own
        self.halo = k_halo - 1
        self.first = first_global + 1
        self.total = total
        faces_z = 0.5 * (k[1:] + k[:-1])
        kc = k[1:-1]
        rows = jnp.pad(kc, ((0, 0), (1, 1), (0, 0)))
        self.fy = 0.5 * (rows[:, 1:] + rows[:, :-1])
        cols = jnp.pad(kc, ((0, 0), (0, 0), (1, 1)))
        self.fx = 0.5 * (cols[:, :, 1:] + cols[:, :, :-1])
        self.fzl = faces_z[:-1]
        self.fzu = faces_z[1:]
        diag = self.fzl + self.fzu + self.fy[:, 1:] + self.fy[:, :-1]
        self.diag = diag + self.fx[:, :, 1:] + self.fx[:, :, :-1]

    def cut(self, arr, h, have):
        n = self.own + 2 * h
        return arr[have - h: have - h + n]

    def coef(self, h):
        c = self.cut
        H = self.halo
        return c(self.fzl, h, H), c(self.fzu, h, H), c(self.fy, h, H), c(self.fx, h, H), c(self.diag, h, H)

    def mask(self, u, h):
        return jnp.where(plane_mask(self.first + self.halo - h, u.shape[0], self.total), u, 0.0)

    def operate(self, u, h):
        fzl, fzu, fy, fx, diag = self.coef(h - 1)
        uc = u[1:-1]
        rows = jnp.pad(uc, ((0, 0), (1, 1), (0, 0)))
        cols = jnp.pad(uc, ((0, 0), (0, 0), (1, 1)))
        nb = fzu * u[2:] + fzl * u[:-2]
        nb = nb + fy[:, 1:] * rows[:, 2:] + fy[:, :-1] * rows[:, :-2]
        nb = nb + fx[:, :, 1:] * cols[:, :, 2:] + fx[:, :, :-1] * cols[:, :, :-2]
        return diag * uc - nb

    def sweep(self, u, f, h):
        diag = self.coef(h - 1)[4]
        new = u[1:-1] + OMEGA * (f - self.operate(u, h)) / diag
        return self.mask(new, h - 1)

    def start(self, f, h):
        return self.mask(OMEGA * f / self.coef(h)[4], h)


def full_face_weights(k):
    depth = jnp.pad(k, ((1, 1), (0, 0), (0, 0)))
    return Level(depth, 1, k.shape[0], -1, k.shape[0])


def full_vcycle(f, k, depth_level):
    lvl = full_face_weights(k)

    def ext(u):
        return jnp.pad(u, ((1, 1), (0, 0), (0, 0)))

    if depth_level == LEVELS - 1:
        u = lvl.start(f, 0)
        for _ in range(BOTTOM - 1):
            u = lvl.sweep(ext(u), f, 1)
        return u
    u = lvl.start(f, 0)
    for _ in range(SWEEPS - 1):
        u = lvl.sweep(ext(u), f, 1)
    residual = f - lvl.operate(ext(u), 1)
    e = full_vcycle(0.5 * restrict_sum(residual), 0.125 * restrict_sum(k), depth_level + 1)
    u = u + copy_up(e)
    for _ in range(SWEEPS):
        u = lvl.sweep(ext(u), f, 1)
    return u


def mode_table(mode_count, length, positions):
    frequency = length // 2 + jnp.arange(mode_count, dtype=jnp.int32)
    phases = frequency[:, None] * (2 * positions[None, :] + 1) % (4 * length)
    return jnp.cos(jnp.pi * phases.astype(jnp.float32) / (2 * length))


def on_device(coarse_states, accept_flags, owners, kl_coeffs, source):
    slabs = lax.axis_size("slab")
    chain_index = lax.axis_index("chain")
    s = lax.axis_index("slab")
    step_numbers = jnp.arange(1, STEPS, dtype=jnp.int32)
    chosen = jnp.max(jnp.where(accept_flags == 1, step_numbers[None, :], 0), axis=1)
    local_count = coarse_states.shape[0]
    accepted = coarse_states[jnp.arange(local_count, dtype=jnp.int32), chosen]
    every_field = lax.all_gather(accepted, "chain", axis=0, tiled=True)
    own = lax.dynamic_index_in_dim(every_field, owners[chain_index], 0, keepdims=False)

    cz, cy, cx = own.shape
    fz = source.shape[0]
    fy, fx = 2 * cy, 2 * cx
    coarse_total = cz * slabs
    fine_total = fz * slabs

    far = COARSE_HALO - cz
    parts = [shift_from(own[cz - far:], 2), shift_from(own, 1), own,
             shift_from(own, -1), shift_from(own[:far], -2)]
    ext = jnp.concatenate(parts, axis=0)
    n_ext = ext.shape[0]
    g0 = s * cz - COARSE_HALO
    gidx = g0 + jnp.arange(n_ext, dtype=jnp.int32)
    lo_plane = lax.dynamic_index_in_dim(ext, jnp.maximum(-g0, 0), 0, keepdims=True)
    hi_plane = lax.dynamic_index_in_dim(ext, jnp.minimum(coarse_total - 1 - g0, n_ext - 1), 0, keepdims=True)
    ext = jnp.where((gidx < 0)[:, None, None], lo_plane, ext)
    ext = jnp.where((gidx >= coarse_total)[:, None, None], hi_plane, ext)

    pro = along_x(ext, prolong_matrix(cx).astype(jnp.bfloat16), precision=lax.Precision.DEFAULT)
    pro = along_y(pro, prolong_matrix(cy))
    inner = pro[1:-1]
    even = 0.75 * inner + 0.25 * pro[:-2]
    odd = 0.75 * inner + 0.25 * pro[2:]
    log_perm = jnp.stack((even, odd), axis=1).reshape(2 * (n_ext - 2), fy, fx)
    k0_first = 2 * (g0 + 1)
    k0_planes = log_perm.shape[0]

    positions = k0_first + jnp.arange(k0_planes, dtype=jnp.int32)
    depth_table = mode_table(MZ, fine_total, positions)
    rows_table = mode_table(MY, fy, jnp.arange(fy, dtype=jnp.int32))
    cols_table = mode_table(MX, fx, jnp.arange(fx, dtype=jnp.int32))
    along_cols = jnp.einsum("abc,cx->abx", kl_coeffs[0], cols_table, precision=HI)
    along_rows = jnp.einsum("abx,by->ayx", along_cols, rows_table, precision=HI)
    kl = jnp.einsum("ayx,az->zyx", along_rows, depth_table, precision=HI)
    k0 = jnp.exp(log_perm + kl)
    k0 = jnp.where(plane_mask(k0_first, k0_planes, fine_total), k0, 0.0)
    k0_halo = (k0_planes - fz) // 2

    k1 = 0.125 * restrict_sum(k0)
    k1_halo = k0_halo // 2
    own1 = fz // 2
    k2_own = 0.125 * restrict_sum(k1[k1_halo:k1_halo + own1])
    k2 = lax.all_gather(k2_own, "slab", axis=0, tiled=True)

    h0k = F0_HALO + 1
    lvl0 = Level(k0[k0_halo - h0k: k0_halo + fz + h0k], h0k, fz, s * fz - h0k, fine_total)
    f0 = jnp.concatenate([shift_from(source[fz - F0_HALO:], 1), source,
                          shift_from(source[:F0_HALO], -1)], axis=0)
    u = lvl0.start(f0, F0_HALO)
    u1 = lvl0.sweep(u, lvl0.cut(f0, F0_HALO - 1, F0_HALO), F0_HALO)
    res0 = f0[F0_HALO:F0_HALO + fz] - lvl0.operate(u1[1:-1], 1)
    f1_own = 0.5 * restrict_sum(res0)

    h1k = F1_HALO + 1
    lvl1 = Level(k1[k1_halo - h1k: k1_halo + own1 + h1k], h1k, own1, s * own1 - h1k,
                 fine_total // 2)
    f1 = jnp.concatenate([shift_from(f1_own, 1), f1_own, shift_from(f1_own, -1)], axis=0)
    v = lvl1.start(f1, F1_HALO)
    v1 = lvl1.sweep(v, lvl1.cut(f1, F1_HALO - 1, F1_HALO), F1_HALO)
    res1 = f1_own - lvl1.operate(v1[2:-2], 1)
    f2 = lax.all_gather(0.5 * restrict_sum(res1), "slab", axis=0, tiled=True)

    e2 = full_vcycle(f2, k2, 2)
    own2 = own1 // 2
    e2 = jnp.pad(e2, ((2, 2), (0, 0), (0, 0)))
    e2 = lax.dynamic_slice_in_dim(e2, s * own2, own2 + 4, axis=0)

    v = v1 + copy_up(e2)[1:-1]
    v = lvl1.sweep(v, lvl1.cut(f1, 2, F1_HALO), 3)
    e1 = lvl1.sweep(v, lvl1.cut(f1, 1, F1_HALO), 2)

    u = u1 + copy_up(e1)
    u = lvl0.sweep(u, lvl0.cut(f0, 1, F0_HALO), 2)
    u = lvl0.sweep(u, source, 1)
    return u[None]


def solution(mesh):
    return jax.shard_map(
        on_device,
        mesh=mesh,
        in_specs=(
            P("chain", None, "slab", None, None),
            P("chain", None),
            P(),
            P("chain", None, None, None),
            P("slab", None, None),
        ),
        out_specs=P("chain", "slab", None, None),
        check_vma=False,
    )
```

```python
import numpy as np
import jax
import jax.numpy as jnp
from jax import lax
from jax.sharding import PartitionSpec as P

STEPS = 4
MZ = 32
MY = 16
MX = 64
LEVELS = 4
SWEEPS = 2
BOTTOM = 4

OMEGA = 0.8
HI = lax.Precision.HIGHEST

K0_HALO = 10
F0_HALO = 3
F1_HALO = 4
COARSE_HALO = 6


def pair_sum_matrix(n):
    m = np.zeros((n, n // 2), np.float32)
    m[np.arange(n), np.arange(n) // 2] = 1.0
    return m


def repeat_matrix(n):
    return np.ascontiguousarray(pair_sum_matrix(2 * n).T)


def prolong_matrix(n):
    m = np.zeros((n, 2 * n), np.float32)
    for i in range(n):
        m[i, 2 * i] += 0.75
        m[max(i - 1, 0), 2 * i] += 0.25
        m[i, 2 * i + 1] += 0.75
        m[min(i + 1, n - 1), 2 * i + 1] += 0.25
    return m


def along_x(values, matrix, precision=HI):
    return jnp.einsum("zyx,xw->zyw", values, jnp.asarray(matrix), precision=precision,
                      preferred_element_type=jnp.float32)


def along_y(values, matrix, precision=HI):
    return jnp.einsum("zyx,yv->zvx", values, jnp.asarray(matrix), precision=precision,
                      preferred_element_type=jnp.float32)


def restrict_sum(values):
    nz, ny, nx = values.shape
    values = values.reshape(nz // 2, 2, ny, nx).sum(axis=1)
    values = along_y(values, pair_sum_matrix(ny))
    return along_x(values, pair_sum_matrix(nx))


def copy_up(values):
    nz, ny, nx = values.shape
    values = along_x(values, repeat_matrix(nx))
    values = along_y(values, repeat_matrix(ny))
    return jnp.repeat(values, 2, axis=0)


def shift_from(block, offset):
    count = lax.axis_size("slab")
    pairs = [(i, i + offset) for i in range(count) if 0 <= i + offset < count]
    return lax.ppermute(block, "slab", pairs)


def gather_slabs(block):
    count = lax.axis_size("slab")
    spread = jnp.broadcast_to(block[None], (count,) + block.shape)
    return lax.all_to_all(spread, "slab", 0, 0, tiled=False).reshape((-1,) + block.shape[1:])


def plane_mask(first_global, planes, total):
    g = first_global + jnp.arange(planes, dtype=jnp.int32)
    return ((g >= 0) & (g < total))[:, None, None]


class Level:
    def __init__(self, k, k_halo, own, first_global, total):
        self.own = own
        self.halo = k_halo - 1
        self.first = first_global + 1
        self.total = total
        faces_z = 0.5 * (k[1:] + k[:-1])
        kc = k[1:-1]
        rows = jnp.pad(kc, ((0, 0), (1, 1), (0, 0)))
        self.fy = 0.5 * (rows[:, 1:] + rows[:, :-1])
        cols = jnp.pad(kc, ((0, 0), (0, 0), (1, 1)))
        self.fx = 0.5 * (cols[:, :, 1:] + cols[:, :, :-1])
        self.fzl = faces_z[:-1]
        self.fzu = faces_z[1:]
        diag = self.fzl + self.fzu + self.fy[:, 1:] + self.fy[:, :-1]
        self.diag = diag + self.fx[:, :, 1:] + self.fx[:, :, :-1]

    def cut(self, arr, h, have):
        n = self.own + 2 * h
        return arr[have - h: have - h + n]

    def coef(self, h):
        c = self.cut
        H = self.halo
        return c(self.fzl, h, H), c(self.fzu, h, H), c(self.fy, h, H), c(self.fx, h, H), c(self.diag, h, H)

    def mask(self, u, h):
        return jnp.where(plane_mask(self.first + self.halo - h, u.shape[0], self.total), u, 0.0)

    def operate(self, u, h):
        fzl, fzu, fy, fx, diag = self.coef(h - 1)
        uc = u[1:-1]
        rows = jnp.pad(uc, ((0, 0), (1, 1), (0, 0)))
        cols = jnp.pad(uc, ((0, 0), (0, 0), (1, 1)))
        nb = fzu * u[2:] + fzl * u[:-2]
        nb = nb + fy[:, 1:] * rows[:, 2:] + fy[:, :-1] * rows[:, :-2]
        nb = nb + fx[:, :, 1:] * cols[:, :, 2:] + fx[:, :, :-1] * cols[:, :, :-2]
        return diag * uc - nb

    def sweep(self, u, f, h):
        diag = self.coef(h - 1)[4]
        new = u[1:-1] + OMEGA * (f - self.operate(u, h)) / diag
        return self.mask(new, h - 1)

    def start(self, f, h):
        return self.mask(OMEGA * f / self.coef(h)[4], h)


def full_face_weights(k):
    depth = jnp.pad(k, ((1, 1), (0, 0), (0, 0)))
    return Level(depth, 1, k.shape[0], -1, k.shape[0])


def full_vcycle(f, k, depth_level):
    lvl = full_face_weights(k)

    def ext(u):
        return jnp.pad(u, ((1, 1), (0, 0), (0, 0)))

    if depth_level == LEVELS - 1:
        u = lvl.start(f, 0)
        for _ in range(BOTTOM - 1):
            u = lvl.sweep(ext(u), f, 1)
        return u
    u = lvl.start(f, 0)
    for _ in range(SWEEPS - 1):
        u = lvl.sweep(ext(u), f, 1)
    residual = f - lvl.operate(ext(u), 1)
    e = full_vcycle(0.5 * restrict_sum(residual), 0.125 * restrict_sum(k), depth_level + 1)
    u = u + copy_up(e)
    for _ in range(SWEEPS):
        u = lvl.sweep(ext(u), f, 1)
    return u


def mode_table(mode_count, length, positions):
    frequency = length // 2 + jnp.arange(mode_count, dtype=jnp.int32)
    phases = frequency[:, None] * (2 * positions[None, :] + 1) % (4 * length)
    return jnp.cos(jnp.pi * phases.astype(jnp.float32) / (2 * length))


def on_device(coarse_states, accept_flags, owners, kl_coeffs, source):
    slabs = lax.axis_size("slab")
    chain_index = lax.axis_index("chain")
    s = lax.axis_index("slab")
    step_numbers = jnp.arange(1, STEPS, dtype=jnp.int32)
    chosen = jnp.max(jnp.where(accept_flags == 1, step_numbers[None, :], 0), axis=1)
    local_count = coarse_states.shape[0]
    accepted = coarse_states[jnp.arange(local_count, dtype=jnp.int32), chosen]
    every_field = lax.all_gather(accepted, "chain", axis=0, tiled=True)
    own = lax.dynamic_index_in_dim(every_field, owners[chain_index], 0, keepdims=False)

    cz, cy, cx = own.shape
    fz = source.shape[0]
    fy, fx = 2 * cy, 2 * cx
    coarse_total = cz * slabs
    fine_total = fz * slabs

    far = COARSE_HALO - cz
    parts = [shift_from(own[cz - far:], 2), shift_from(own, 1), own,
             shift_from(own, -1), shift_from(own[:far], -2)]
    ext = jnp.concatenate(parts, axis=0)
    n_ext = ext.shape[0]
    g0 = s * cz - COARSE_HALO
    gidx = g0 + jnp.arange(n_ext, dtype=jnp.int32)
    lo_plane = lax.dynamic_index_in_dim(ext, jnp.maximum(-g0, 0), 0, keepdims=True)
    hi_plane = lax.dynamic_index_in_dim(ext, jnp.minimum(coarse_total - 1 - g0, n_ext - 1), 0, keepdims=True)
    ext = jnp.where((gidx < 0)[:, None, None], lo_plane, ext)
    ext = jnp.where((gidx >= coarse_total)[:, None, None], hi_plane, ext)

    pro = along_x(ext, prolong_matrix(cx).astype(jnp.bfloat16), precision=lax.Precision.DEFAULT)
    pro = along_y(pro, prolong_matrix(cy))
    inner = pro[1:-1]
    even = 0.75 * inner + 0.25 * pro[:-2]
    odd = 0.75 * inner + 0.25 * pro[2:]
    log_perm = jnp.stack((even, odd), axis=1).reshape(2 * (n_ext - 2), fy, fx)
    k0_first = 2 * (g0 + 1)
    k0_planes = log_perm.shape[0]

    positions = k0_first + jnp.arange(k0_planes, dtype=jnp.int32)
    depth_table = mode_table(MZ, fine_total, positions)
    rows_table = mode_table(MY, fy, jnp.arange(fy, dtype=jnp.int32))
    cols_table = mode_table(MX, fx, jnp.arange(fx, dtype=jnp.int32))
    along_depth = jnp.einsum("abe,az->zbe", kl_coeffs[0], depth_table, precision=HI)
    along_rows = jnp.einsum("zbe,by->zye", along_depth, rows_table, precision=HI)
    kl = jnp.dot(along_rows.reshape(k0_planes * fy, MX), cols_table,
                 precision=HI).reshape(k0_planes, fy, fx)
    k0 = jnp.exp(log_perm + kl)
    k0 = jnp.where(plane_mask(k0_first, k0_planes, fine_total), k0, 0.0)
    k0_halo = (k0_planes - fz) // 2

    k1 = 0.125 * restrict_sum(k0)
    k1_halo = k0_halo // 2
    own1 = fz // 2
    k2_own = 0.125 * restrict_sum(k1[k1_halo:k1_halo + own1])
    k2 = lax.all_gather(k2_own, "slab", axis=0, tiled=True)

    h0k = F0_HALO + 1
    lvl0 = Level(k0[k0_halo - h0k: k0_halo + fz + h0k], h0k, fz, s * fz - h0k, fine_total)
    f0 = jnp.concatenate([shift_from(source[fz - F0_HALO:], 1), source,
                          shift_from(source[:F0_HALO], -1)], axis=0)
    u = lvl0.start(f0, F0_HALO)
    u1 = lvl0.sweep(u, lvl0.cut(f0, F0_HALO - 1, F0_HALO), F0_HALO)
    res0 = f0[F0_HALO:F0_HALO + fz] - lvl0.operate(u1[1:-1], 1)
    f1_own = 0.5 * restrict_sum(res0)

    h1k = F1_HALO + 1
    lvl1 = Level(k1[k1_halo - h1k: k1_halo + own1 + h1k], h1k, own1, s * own1 - h1k,
                 fine_total // 2)
    f1 = jnp.concatenate([shift_from(f1_own, 1), f1_own, shift_from(f1_own, -1)], axis=0)
    v = lvl1.start(f1, F1_HALO)
    v1 = lvl1.sweep(v, lvl1.cut(f1, F1_HALO - 1, F1_HALO), F1_HALO)
    res1 = f1_own - lvl1.operate(v1[2:-2], 1)
    f2 = gather_slabs(0.5 * restrict_sum(res1))

    e2 = full_vcycle(f2, k2, 2)
    own2 = own1 // 2
    e2 = jnp.pad(e2, ((2, 2), (0, 0), (0, 0)))
    e2 = lax.dynamic_slice_in_dim(e2, s * own2, own2 + 4, axis=0)

    v = v1 + copy_up(e2)[1:-1]
    v = lvl1.sweep(v, lvl1.cut(f1, 2, F1_HALO), 3)
    e1 = lvl1.sweep(v, lvl1.cut(f1, 1, F1_HALO), 2)

    u = u1 + copy_up(e1)
    u = lvl0.sweep(u, lvl0.cut(f0, 1, F0_HALO), 2)
    u = lvl0.sweep(u, source, 1)
    return u[None]


def solution(mesh):
    return jax.shard_map(
        on_device,
        mesh=mesh,
        in_specs=(
            P("chain", None, "slab", None, None),
            P("chain", None),
            P(),
            P("chain", None, None, None),
            P("slab", None, None),
        ),
        out_specs=P("chain", "slab", None, None),
        check_vma=False,
    )
```

```python
import numpy as np
import jax
import jax.numpy as jnp
from jax import lax
from jax.sharding import PartitionSpec as P

STEPS = 4
MZ = 32
MY = 16
MX = 64
LEVELS = 4
SWEEPS = 2
BOTTOM = 4

OMEGA = 0.8
HI = lax.Precision.HIGHEST

K0_HALO = 10
F0_HALO = 3
F1_HALO = 4
COARSE_HALO = 6


def pair_sum_matrix(n):
    m = np.zeros((n, n // 2), np.float32)
    m[np.arange(n), np.arange(n) // 2] = 1.0
    return m


def repeat_matrix(n):
    return np.ascontiguousarray(pair_sum_matrix(2 * n).T)


def prolong_matrix(n):
    m = np.zeros((n, 2 * n), np.float32)
    for i in range(n):
        m[i, 2 * i] += 0.75
        m[max(i - 1, 0), 2 * i] += 0.25
        m[i, 2 * i + 1] += 0.75
        m[min(i + 1, n - 1), 2 * i + 1] += 0.25
    return m


def along_x(values, matrix, precision=HI):
    return jnp.einsum("zyx,xw->zyw", values, jnp.asarray(matrix), precision=precision,
                      preferred_element_type=jnp.float32)


def along_y(values, matrix, precision=HI):
    return jnp.einsum("zyx,yv->zvx", values, jnp.asarray(matrix), precision=precision,
                      preferred_element_type=jnp.float32)


def restrict_sum(values):
    nz, ny, nx = values.shape
    values = values.reshape(nz // 2, 2, ny, nx).sum(axis=1)
    values = along_y(values, pair_sum_matrix(ny))
    return along_x(values, pair_sum_matrix(nx))


def copy_up(values):
    nz, ny, nx = values.shape
    values = along_x(values, repeat_matrix(nx))
    values = along_y(values, repeat_matrix(ny))
    return jnp.repeat(values, 2, axis=0)


def shift_from(block, offset):
    count = lax.axis_size("slab")
    pairs = [(i, i + offset) for i in range(count) if 0 <= i + offset < count]
    return lax.ppermute(block, "slab", pairs)


def gather_slabs(block):
    count = lax.axis_size("slab")
    flat = block.reshape(block.size // 128, 128)
    spread = jnp.broadcast_to(flat[None], (count,) + flat.shape)
    got = lax.all_to_all(spread, "slab", 0, 0, tiled=False)
    return got.reshape((count * block.shape[0],) + block.shape[1:])


def plane_mask(first_global, planes, total):
    g = first_global + jnp.arange(planes, dtype=jnp.int32)
    return ((g >= 0) & (g < total))[:, None, None]


class Level:
    def __init__(self, k, k_halo, own, first_global, total):
        self.own = own
        self.halo = k_halo - 1
        self.first = first_global + 1
        self.total = total
        faces_z = 0.5 * (k[1:] + k[:-1])
        kc = k[1:-1]
        rows = jnp.pad(kc, ((0, 0), (1, 1), (0, 0)))
        self.fy = 0.5 * (rows[:, 1:] + rows[:, :-1])
        cols = jnp.pad(kc, ((0, 0), (0, 0), (1, 1)))
        self.fx = 0.5 * (cols[:, :, 1:] + cols[:, :, :-1])
        self.fzl = faces_z[:-1]
        self.fzu = faces_z[1:]
        diag = self.fzl + self.fzu + self.fy[:, 1:] + self.fy[:, :-1]
        self.diag = diag + self.fx[:, :, 1:] + self.fx[:, :, :-1]

    def cut(self, arr, h, have):
        n = self.own + 2 * h
        return arr[have - h: have - h + n]

    def coef(self, h):
        c = self.cut
        H = self.halo
        return c(self.fzl, h, H), c(self.fzu, h, H), c(self.fy, h, H), c(self.fx, h, H), c(self.diag, h, H)

    def mask(self, u, h):
        return jnp.where(plane_mask(self.first + self.halo - h, u.shape[0], self.total), u, 0.0)

    def operate(self, u, h):
        fzl, fzu, fy, fx, diag = self.coef(h - 1)
        uc = u[1:-1]
        rows = jnp.pad(uc, ((0, 0), (1, 1), (0, 0)))
        cols = jnp.pad(uc, ((0, 0), (0, 0), (1, 1)))
        nb = fzu * u[2:] + fzl * u[:-2]
        nb = nb + fy[:, 1:] * rows[:, 2:] + fy[:, :-1] * rows[:, :-2]
        nb = nb + fx[:, :, 1:] * cols[:, :, 2:] + fx[:, :, :-1] * cols[:, :, :-2]
        return diag * uc - nb

    def sweep(self, u, f, h):
        diag = self.coef(h - 1)[4]
        new = u[1:-1] + OMEGA * (f - self.operate(u, h)) / diag
        return self.mask(new, h - 1)

    def start(self, f, h):
        return self.mask(OMEGA * f / self.coef(h)[4], h)


def mode_table(mode_count, length, positions):
    frequency = length // 2 + jnp.arange(mode_count, dtype=jnp.int32)
    phases = frequency[:, None] * (2 * positions[None, :] + 1) % (4 * length)
    return jnp.cos(jnp.pi * phases.astype(jnp.float32) / (2 * length))


def on_device(coarse_states, accept_flags, owners, kl_coeffs, source):
    slabs = lax.axis_size("slab")
    chain_index = lax.axis_index("chain")
    s = lax.axis_index("slab")
    step_numbers = jnp.arange(1, STEPS, dtype=jnp.int32)
    chosen = jnp.max(jnp.where(accept_flags == 1, step_numbers[None, :], 0), axis=1)
    local_count = coarse_states.shape[0]
    accepted = coarse_states[jnp.arange(local_count, dtype=jnp.int32), chosen]
    every_field = lax.all_gather(accepted, "chain", axis=0, tiled=True)
    own = lax.dynamic_index_in_dim(every_field, owners[chain_index], 0, keepdims=False)

    cz, cy, cx = own.shape
    fz = source.shape[0]
    fy, fx = 2 * cy, 2 * cx
    coarse_total = cz * slabs
    fine_total = fz * slabs

    far = COARSE_HALO - cz
    parts = [shift_from(own[cz - far:], 2), shift_from(own, 1), own,
             shift_from(own, -1), shift_from(own[:far], -2)]
    ext = jnp.concatenate(parts, axis=0)
    n_ext = ext.shape[0]
    g0 = s * cz - COARSE_HALO
    gidx = g0 + jnp.arange(n_ext, dtype=jnp.int32)
    lo_plane = lax.dynamic_index_in_dim(ext, jnp.maximum(-g0, 0), 0, keepdims=True)
    hi_plane = lax.dynamic_index_in_dim(ext, jnp.minimum(coarse_total - 1 - g0, n_ext - 1), 0, keepdims=True)
    ext = jnp.where((gidx < 0)[:, None, None], lo_plane, ext)
    ext = jnp.where((gidx >= coarse_total)[:, None, None], hi_plane, ext)

    pro = along_x(ext, prolong_matrix(cx).astype(jnp.bfloat16), precision=lax.Precision.DEFAULT)
    pro = along_y(pro, prolong_matrix(cy))
    inner = pro[1:-1]
    even = 0.75 * inner + 0.25 * pro[:-2]
    odd = 0.75 * inner + 0.25 * pro[2:]
    log_perm = jnp.stack((even, odd), axis=1).reshape(2 * (n_ext - 2), fy, fx)
    k0_first = 2 * (g0 + 1)
    k0_planes = log_perm.shape[0]

    positions = k0_first + jnp.arange(k0_planes, dtype=jnp.int32)
    depth_table = mode_table(MZ, fine_total, positions)
    rows_table = mode_table(MY, fy, jnp.arange(fy, dtype=jnp.int32))
    cols_table = mode_table(MX, fx, jnp.arange(fx, dtype=jnp.int32))
    along_depth = jnp.einsum("abe,az->zbe", kl_coeffs[0], depth_table, precision=HI)
    along_rows = jnp.einsum("zbe,by->zye", along_depth, rows_table, precision=HI)
    kl = jnp.dot(along_rows.reshape(k0_planes * fy, MX), cols_table,
                 precision=HI).reshape(k0_planes, fy, fx)
    k0 = jnp.exp(log_perm + kl)
    k0 = jnp.where(plane_mask(k0_first, k0_planes, fine_total), k0, 0.0)
    k0_halo = (k0_planes - fz) // 2

    k1 = 0.125 * restrict_sum(k0)
    k1_halo = k0_halo // 2
    own1 = fz // 2
    k2_own = 0.125 * restrict_sum(k1[k1_halo:k1_halo + own1])
    k2 = lax.all_gather(k2_own, "slab", axis=0, tiled=True)

    h0k = F0_HALO + 1
    lvl0 = Level(k0[k0_halo - h0k: k0_halo + fz + h0k], h0k, fz, s * fz - h0k, fine_total)
    f0 = jnp.concatenate([shift_from(source[fz - F0_HALO:], 1), source,
                          shift_from(source[:F0_HALO], -1)], axis=0)
    u = lvl0.start(f0, F0_HALO)
    u1 = lvl0.sweep(u, lvl0.cut(f0, F0_HALO - 1, F0_HALO), F0_HALO)
    res0 = f0[F0_HALO:F0_HALO + fz] - lvl0.operate(u1[1:-1], 1)
    f1_own = 0.5 * restrict_sum(res0)

    h1k = F1_HALO + 1
    lvl1 = Level(k1[k1_halo - h1k: k1_halo + own1 + h1k], h1k, own1, s * own1 - h1k,
                 fine_total // 2)
    f1 = jnp.concatenate([shift_from(f1_own, 1), f1_own, shift_from(f1_own, -1)], axis=0)
    v = lvl1.start(f1, F1_HALO)
    v1 = lvl1.sweep(v, lvl1.cut(f1, F1_HALO - 1, F1_HALO), F1_HALO)
    res1 = f1_own - lvl1.operate(v1[2:-2], 1)
    f2 = gather_slabs(0.5 * restrict_sum(res1))

    own2 = own1 // 2
    total2 = fine_total // 4
    k2_halo = 13
    f2_halo = k2_halo - 1
    pad2 = ((k2_halo, k2_halo), (0, 0), (0, 0))
    k2w = lax.dynamic_slice_in_dim(jnp.pad(k2, pad2), s * own2, own2 + 2 * k2_halo, axis=0)
    f2w = lax.dynamic_slice_in_dim(jnp.pad(f2, pad2), s * own2 + 1, own2 + 2 * f2_halo, axis=0)
    lvl2 = Level(k2w, k2_halo, own2, s * own2 - k2_halo, total2)
    w = lvl2.start(f2w, f2_halo)
    w1 = lvl2.sweep(w, lvl2.cut(f2w, f2_halo - 1, f2_halo), f2_halo)
    res2 = lvl2.cut(f2w, f2_halo - 2, f2_halo) - lvl2.operate(w1, f2_halo - 1)
    f3 = 0.5 * restrict_sum(res2)
    f3_halo = (f2_halo - 2) // 2
    k3 = 0.125 * restrict_sum(k2w[1:-1])
    lvl3 = Level(k3, f3_halo + 1, own2 // 2, s * (own2 // 2) - f3_halo - 1, total2 // 2)
    b = lvl3.start(f3, f3_halo)
    for step in range(BOTTOM - 1):
        h = f3_halo - step
        b = lvl3.sweep(b, lvl3.cut(f3, h - 1, f3_halo), h)
    e3_halo = f3_halo - (BOTTOM - 1)
    cut2 = (f2_halo - 1) - 2 * e3_halo
    w = w1[cut2:w1.shape[0] - cut2] + copy_up(b)
    h = 2 * e3_halo
    for _ in range(SWEEPS):
        w = lvl2.sweep(w, lvl2.cut(f2w, h - 1, f2_halo), h)
        h -= 1
    e2 = w

    v = v1 + copy_up(e2)[1:-1]
    v = lvl1.sweep(v, lvl1.cut(f1, 2, F1_HALO), 3)
    e1 = lvl1.sweep(v, lvl1.cut(f1, 1, F1_HALO), 2)

    u = u1 + copy_up(e1)
    u = lvl0.sweep(u, lvl0.cut(f0, 1, F0_HALO), 2)
    u = lvl0.sweep(u, source, 1)
    return u[None]


def solution(mesh):
    return jax.shard_map(
        on_device,
        mesh=mesh,
        in_specs=(
            P("chain", None, "slab", None, None),
            P("chain", None),
            P(),
            P("chain", None, None, None),
            P("slab", None, None),
        ),
        out_specs=P("chain", "slab", None, None),
        check_vma=False,
    )
```

```python
import numpy as np
import jax
import jax.numpy as jnp
from jax import lax
from jax.sharding import PartitionSpec as P

STEPS = 4
MZ = 32
MY = 16
MX = 64
LEVELS = 4
SWEEPS = 2
BOTTOM = 4

OMEGA = 0.8
HI = lax.Precision.HIGHEST

K0_HALO = 10
F0_HALO = 3
F1_HALO = 4
COARSE_HALO = 6


def pair_sum_matrix(n):
    m = np.zeros((n, n // 2), np.float32)
    m[np.arange(n), np.arange(n) // 2] = 1.0
    return m


def repeat_matrix(n):
    return np.ascontiguousarray(pair_sum_matrix(2 * n).T)


def prolong_matrix(n):
    m = np.zeros((n, 2 * n), np.float32)
    for i in range(n):
        m[i, 2 * i] += 0.75
        m[max(i - 1, 0), 2 * i] += 0.25
        m[i, 2 * i + 1] += 0.75
        m[min(i + 1, n - 1), 2 * i + 1] += 0.25
    return m


def along_x(values, matrix, precision=HI):
    return jnp.einsum("zyx,xw->zyw", values, jnp.asarray(matrix), precision=precision,
                      preferred_element_type=jnp.float32)


def along_y(values, matrix, precision=HI):
    return jnp.einsum("zyx,yv->zvx", values, jnp.asarray(matrix), precision=precision,
                      preferred_element_type=jnp.float32)


def restrict_sum(values):
    nz, ny, nx = values.shape
    values = values.reshape(nz // 2, 2, ny, nx).sum(axis=1)
    values = along_y(values, pair_sum_matrix(ny))
    return along_x(values, pair_sum_matrix(nx))


def copy_up(values):
    nz, ny, nx = values.shape
    values = along_x(values, repeat_matrix(nx))
    values = along_y(values, repeat_matrix(ny))
    return jnp.repeat(values, 2, axis=0)


def shift_from(block, offset):
    count = lax.axis_size("slab")
    pairs = [(i, i + offset) for i in range(count) if 0 <= i + offset < count]
    return lax.ppermute(block, "slab", pairs)


def gather_slabs(*blocks):
    count = lax.axis_size("slab")
    flat = jnp.concatenate([b.reshape(b.size // 128, 128) for b in blocks], axis=0)
    spread = jnp.broadcast_to(flat[None], (count,) + flat.shape)
    got = lax.all_to_all(spread, "slab", 0, 0, tiled=False)
    outs = []
    row = 0
    for b in blocks:
        rows = b.size // 128
        part = got[:, row:row + rows]
        outs.append(part.reshape((count * b.shape[0],) + b.shape[1:]))
        row += rows
    return outs


def plane_mask(first_global, planes, total):
    g = first_global + jnp.arange(planes, dtype=jnp.int32)
    return ((g >= 0) & (g < total))[:, None, None]


class Level:
    def __init__(self, k, k_halo, own, first_global, total):
        self.own = own
        self.halo = k_halo - 1
        self.first = first_global + 1
        self.total = total
        faces_z = 0.5 * (k[1:] + k[:-1])
        kc = k[1:-1]
        rows = jnp.pad(kc, ((0, 0), (1, 1), (0, 0)))
        self.fy = 0.5 * (rows[:, 1:] + rows[:, :-1])
        cols = jnp.pad(kc, ((0, 0), (0, 0), (1, 1)))
        self.fx = 0.5 * (cols[:, :, 1:] + cols[:, :, :-1])
        self.fzl = faces_z[:-1]
        self.fzu = faces_z[1:]
        diag = self.fzl + self.fzu + self.fy[:, 1:] + self.fy[:, :-1]
        self.diag = diag + self.fx[:, :, 1:] + self.fx[:, :, :-1]

    def cut(self, arr, h, have):
        n = self.own + 2 * h
        return arr[have - h: have - h + n]

    def coef(self, h):
        c = self.cut
        H = self.halo
        return c(self.fzl, h, H), c(self.fzu, h, H), c(self.fy, h, H), c(self.fx, h, H), c(self.diag, h, H)

    def mask(self, u, h):
        return jnp.where(plane_mask(self.first + self.halo - h, u.shape[0], self.total), u, 0.0)

    def operate(self, u, h):
        fzl, fzu, fy, fx, diag = self.coef(h - 1)
        uc = u[1:-1]
        rows = jnp.pad(uc, ((0, 0), (1, 1), (0, 0)))
        cols = jnp.pad(uc, ((0, 0), (0, 0), (1, 1)))
        nb = fzu * u[2:] + fzl * u[:-2]
        nb = nb + fy[:, 1:] * rows[:, 2:] + fy[:, :-1] * rows[:, :-2]
        nb = nb + fx[:, :, 1:] * cols[:, :, 2:] + fx[:, :, :-1] * cols[:, :, :-2]
        return diag * uc - nb

    def sweep(self, u, f, h):
        diag = self.coef(h - 1)[4]
        new = u[1:-1] + OMEGA * (f - self.operate(u, h)) / diag
        return self.mask(new, h - 1)

    def start(self, f, h):
        return self.mask(OMEGA * f / self.coef(h)[4], h)


def mode_table(mode_count, length, positions):
    frequency = length // 2 + jnp.arange(mode_count, dtype=jnp.int32)
    phases = frequency[:, None] * (2 * positions[None, :] + 1) % (4 * length)
    return jnp.cos(jnp.pi * phases.astype(jnp.float32) / (2 * length))


def on_device(coarse_states, accept_flags, owners, kl_coeffs, source):
    slabs = lax.axis_size("slab")
    chain_index = lax.axis_index("chain")
    s = lax.axis_index("slab")
    step_numbers = jnp.arange(1, STEPS, dtype=jnp.int32)
    chosen = jnp.max(jnp.where(accept_flags == 1, step_numbers[None, :], 0), axis=1)
    local_count = coarse_states.shape[0]
    accepted = coarse_states[jnp.arange(local_count, dtype=jnp.int32), chosen]
    every_field = lax.all_gather(accepted, "chain", axis=0, tiled=True)
    own = lax.dynamic_index_in_dim(every_field, owners[chain_index], 0, keepdims=False)

    cz, cy, cx = own.shape
    fz = source.shape[0]
    fy, fx = 2 * cy, 2 * cx
    coarse_total = cz * slabs
    fine_total = fz * slabs

    far = COARSE_HALO - cz
    parts = [shift_from(own[cz - far:], 2), shift_from(own, 1), own,
             shift_from(own, -1), shift_from(own[:far], -2)]
    ext = jnp.concatenate(parts, axis=0)
    n_ext = ext.shape[0]
    g0 = s * cz - COARSE_HALO
    gidx = g0 + jnp.arange(n_ext, dtype=jnp.int32)
    lo_plane = lax.dynamic_index_in_dim(ext, jnp.maximum(-g0, 0), 0, keepdims=True)
    hi_plane = lax.dynamic_index_in_dim(ext, jnp.minimum(coarse_total - 1 - g0, n_ext - 1), 0, keepdims=True)
    ext = jnp.where((gidx < 0)[:, None, None], lo_plane, ext)
    ext = jnp.where((gidx >= coarse_total)[:, None, None], hi_plane, ext)

    pro = along_x(ext, prolong_matrix(cx).astype(jnp.bfloat16), precision=lax.Precision.DEFAULT)
    pro = along_y(pro, prolong_matrix(cy))
    inner = pro[1:-1]
    even = 0.75 * inner + 0.25 * pro[:-2]
    odd = 0.75 * inner + 0.25 * pro[2:]
    log_perm = jnp.stack((even, odd), axis=1).reshape(2 * (n_ext - 2), fy, fx)
    k0_first = 2 * (g0 + 1)
    k0_planes = log_perm.shape[0]

    positions = k0_first + jnp.arange(k0_planes, dtype=jnp.int32)
    depth_table = mode_table(MZ, fine_total, positions)
    rows_table = mode_table(MY, fy, jnp.arange(fy, dtype=jnp.int32))
    cols_table = mode_table(MX, fx, jnp.arange(fx, dtype=jnp.int32))
    along_depth = jnp.einsum("abe,az->zbe", kl_coeffs[0], depth_table, precision=HI)
    along_rows = jnp.einsum("zbe,by->zye", along_depth, rows_table, precision=HI)
    kl = jnp.dot(along_rows.reshape(k0_planes * fy, MX), cols_table,
                 precision=HI).reshape(k0_planes, fy, fx)
    k0 = jnp.exp(log_perm + kl)
    k0 = jnp.where(plane_mask(k0_first, k0_planes, fine_total), k0, 0.0)
    k0_halo = (k0_planes - fz) // 2

    k1 = 0.125 * restrict_sum(k0)
    k1_halo = k0_halo // 2
    own1 = fz // 2
    k2_own = 0.125 * restrict_sum(k1[k1_halo:k1_halo + own1])

    h0k = F0_HALO + 1
    lvl0 = Level(k0[k0_halo - h0k: k0_halo + fz + h0k], h0k, fz, s * fz - h0k, fine_total)
    f0 = jnp.concatenate([shift_from(source[fz - F0_HALO:], 1), source,
                          shift_from(source[:F0_HALO], -1)], axis=0)
    u = lvl0.start(f0, F0_HALO)
    u1 = lvl0.sweep(u, lvl0.cut(f0, F0_HALO - 1, F0_HALO), F0_HALO)
    res0 = f0[F0_HALO:F0_HALO + fz] - lvl0.operate(u1[1:-1], 1)
    f1_own = 0.5 * restrict_sum(res0)

    h1k = F1_HALO + 1
    lvl1 = Level(k1[k1_halo - h1k: k1_halo + own1 + h1k], h1k, own1, s * own1 - h1k,
                 fine_total // 2)
    f1 = jnp.concatenate([shift_from(f1_own, 1), f1_own, shift_from(f1_own, -1)], axis=0)
    v = lvl1.start(f1, F1_HALO)
    v1 = lvl1.sweep(v, lvl1.cut(f1, F1_HALO - 1, F1_HALO), F1_HALO)
    res1 = f1_own - lvl1.operate(v1[2:-2], 1)
    f2, k2 = gather_slabs(0.5 * restrict_sum(res1), k2_own)

    own2 = own1 // 2
    total2 = fine_total // 4
    k2_halo = 13
    f2_halo = k2_halo - 1
    pad2 = ((k2_halo, k2_halo), (0, 0), (0, 0))
    k2w = lax.dynamic_slice_in_dim(jnp.pad(k2, pad2), s * own2, own2 + 2 * k2_halo, axis=0)
    f2w = lax.dynamic_slice_in_dim(jnp.pad(f2, pad2), s * own2 + 1, own2 + 2 * f2_halo, axis=0)
    lvl2 = Level(k2w, k2_halo, own2, s * own2 - k2_halo, total2)
    w = lvl2.start(f2w, f2_halo)
    w1 = lvl2.sweep(w, lvl2.cut(f2w, f2_halo - 1, f2_halo), f2_halo)
    res2 = lvl2.cut(f2w, f2_halo - 2, f2_halo) - lvl2.operate(w1, f2_halo - 1)
    f3 = 0.5 * restrict_sum(res2)
    f3_halo = (f2_halo - 2) // 2
    k3 = 0.125 * restrict_sum(k2w[1:-1])
    lvl3 = Level(k3, f3_halo + 1, own2 // 2, s * (own2 // 2) - f3_halo - 1, total2 // 2)
    b = lvl3.start(f3, f3_halo)
    for step in range(BOTTOM - 1):
        h = f3_halo - step
        b = lvl3.sweep(b, lvl3.cut(f3, h - 1, f3_halo), h)
    e3_halo = f3_halo - (BOTTOM - 1)
    cut2 = (f2_halo - 1) - 2 * e3_halo
    w = w1[cut2:w1.shape[0] - cut2] + copy_up(b)
    h = 2 * e3_halo
    for _ in range(SWEEPS):
        w = lvl2.sweep(w, lvl2.cut(f2w, h - 1, f2_halo), h)
        h -= 1
    e2 = w

    v = v1 + copy_up(e2)[1:-1]
    v = lvl1.sweep(v, lvl1.cut(f1, 2, F1_HALO), 3)
    e1 = lvl1.sweep(v, lvl1.cut(f1, 1, F1_HALO), 2)

    u = u1 + copy_up(e1)
    u = lvl0.sweep(u, lvl0.cut(f0, 1, F0_HALO), 2)
    u = lvl0.sweep(u, source, 1)
    return u[None]


def solution(mesh):
    return jax.shard_map(
        on_device,
        mesh=mesh,
        in_specs=(
            P("chain", None, "slab", None, None),
            P("chain", None),
            P(),
            P("chain", None, None, None),
            P("slab", None, None),
        ),
        out_specs=P("chain", "slab", None, None),
        check_vma=False,
    )
```

```python
import numpy as np
import jax
import jax.numpy as jnp
from jax import lax
from jax.sharding import PartitionSpec as P

STEPS = 4
MZ = 32
MY = 16
MX = 64
LEVELS = 4
SWEEPS = 2
BOTTOM = 4

OMEGA = 0.8
HI = lax.Precision.HIGHEST

K0_HALO = 10
F0_HALO = 3
F1_HALO = 4
COARSE_HALO = 6


def pair_sum_matrix(n):
    m = np.zeros((n, n // 2), np.float32)
    m[np.arange(n), np.arange(n) // 2] = 1.0
    return m


def repeat_matrix(n):
    return np.ascontiguousarray(pair_sum_matrix(2 * n).T)


def prolong_matrix(n):
    m = np.zeros((n, 2 * n), np.float32)
    for i in range(n):
        m[i, 2 * i] += 0.75
        m[max(i - 1, 0), 2 * i] += 0.25
        m[i, 2 * i + 1] += 0.75
        m[min(i + 1, n - 1), 2 * i + 1] += 0.25
    return m


def along_x(values, matrix, precision=HI):
    return jnp.einsum("zyx,xw->zyw", values, jnp.asarray(matrix), precision=precision,
                      preferred_element_type=jnp.float32)


def along_y(values, matrix, precision=HI):
    return jnp.einsum("zyx,yv->zvx", values, jnp.asarray(matrix), precision=precision,
                      preferred_element_type=jnp.float32)


def restrict_sum(values):
    nz, ny, nx = values.shape
    values = values.reshape(nz // 2, 2, ny, nx).sum(axis=1)
    values = along_y(values, pair_sum_matrix(ny))
    return along_x(values, pair_sum_matrix(nx))


def copy_up(values):
    nz, ny, nx = values.shape
    values = along_x(values, repeat_matrix(nx))
    values = along_y(values, repeat_matrix(ny))
    return jnp.repeat(values, 2, axis=0)


def shift_from(block, offset):
    count = lax.axis_size("slab")
    pairs = [(i, i + offset) for i in range(count) if 0 <= i + offset < count]
    return lax.ppermute(block, "slab", pairs)


def gather_window(block):
    got = jnp.concatenate([shift_from(block[None], 1), block[None], shift_from(block[None], -1)])
    got = jnp.concatenate([shift_from(got[:2], 2), got, shift_from(got[1:], -2)])
    return jnp.concatenate([shift_from(got[:4], 4), got, shift_from(got[3:], -4)])


def plane_mask(first_global, planes, total):
    g = first_global + jnp.arange(planes, dtype=jnp.int32)
    return ((g >= 0) & (g < total))[:, None, None]


class Level:
    def __init__(self, k, k_halo, own, first_global, total):
        self.own = own
        self.halo = k_halo - 1
        self.first = first_global + 1
        self.total = total
        faces_z = 0.5 * (k[1:] + k[:-1])
        kc = k[1:-1]
        rows = jnp.pad(kc, ((0, 0), (1, 1), (0, 0)))
        self.fy = 0.5 * (rows[:, 1:] + rows[:, :-1])
        cols = jnp.pad(kc, ((0, 0), (0, 0), (1, 1)))
        self.fx = 0.5 * (cols[:, :, 1:] + cols[:, :, :-1])
        self.fzl = faces_z[:-1]
        self.fzu = faces_z[1:]
        diag = self.fzl + self.fzu + self.fy[:, 1:] + self.fy[:, :-1]
        self.diag = diag + self.fx[:, :, 1:] + self.fx[:, :, :-1]

    def cut(self, arr, h, have):
        n = self.own + 2 * h
        return arr[have - h: have - h + n]

    def coef(self, h):
        c = self.cut
        H = self.halo
        return c(self.fzl, h, H), c(self.fzu, h, H), c(self.fy, h, H), c(self.fx, h, H), c(self.diag, h, H)

    def mask(self, u, h):
        return jnp.where(plane_mask(self.first + self.halo - h, u.shape[0], self.total), u, 0.0)

    def operate(self, u, h):
        fzl, fzu, fy, fx, diag = self.coef(h - 1)
        uc = u[1:-1]
        rows = jnp.pad(uc, ((0, 0), (1, 1), (0, 0)))
        cols = jnp.pad(uc, ((0, 0), (0, 0), (1, 1)))
        nb = fzu * u[2:] + fzl * u[:-2]
        nb = nb + fy[:, 1:] * rows[:, 2:] + fy[:, :-1] * rows[:, :-2]
        nb = nb + fx[:, :, 1:] * cols[:, :, 2:] + fx[:, :, :-1] * cols[:, :, :-2]
        return diag * uc - nb

    def sweep(self, u, f, h):
        diag = self.coef(h - 1)[4]
        new = u[1:-1] + OMEGA * (f - self.operate(u, h)) / diag
        return self.mask(new, h - 1)

    def start(self, f, h):
        return self.mask(OMEGA * f / self.coef(h)[4], h)


def mode_table(mode_count, length, positions):
    frequency = length // 2 + jnp.arange(mode_count, dtype=jnp.int32)
    phases = frequency[:, None] * (2 * positions[None, :] + 1) % (4 * length)
    return jnp.cos(jnp.pi * phases.astype(jnp.float32) / (2 * length))


def on_device(coarse_states, accept_flags, owners, kl_coeffs, source):
    slabs = lax.axis_size("slab")
    chain_index = lax.axis_index("chain")
    s = lax.axis_index("slab")
    step_numbers = jnp.arange(1, STEPS, dtype=jnp.int32)
    chosen = jnp.max(jnp.where(accept_flags == 1, step_numbers[None, :], 0), axis=1)
    local_count = coarse_states.shape[0]
    accepted = coarse_states[jnp.arange(local_count, dtype=jnp.int32), chosen]
    every_field = lax.all_gather(accepted, "chain", axis=0, tiled=True)
    own = lax.dynamic_index_in_dim(every_field, owners[chain_index], 0, keepdims=False)

    cz, cy, cx = own.shape
    fz = source.shape[0]
    fy, fx = 2 * cy, 2 * cx
    coarse_total = cz * slabs
    fine_total = fz * slabs

    far = COARSE_HALO - cz
    parts = [shift_from(own[cz - far:], 2), shift_from(own, 1), own,
             shift_from(own, -1), shift_from(own[:far], -2)]
    ext = jnp.concatenate(parts, axis=0)
    n_ext = ext.shape[0]
    g0 = s * cz - COARSE_HALO
    gidx = g0 + jnp.arange(n_ext, dtype=jnp.int32)
    lo_plane = lax.dynamic_index_in_dim(ext, jnp.maximum(-g0, 0), 0, keepdims=True)
    hi_plane = lax.dynamic_index_in_dim(ext, jnp.minimum(coarse_total - 1 - g0, n_ext - 1), 0, keepdims=True)
    ext = jnp.where((gidx < 0)[:, None, None], lo_plane, ext)
    ext = jnp.where((gidx >= coarse_total)[:, None, None], hi_plane, ext)

    pro = along_x(ext, prolong_matrix(cx).astype(jnp.bfloat16), precision=lax.Precision.DEFAULT)
    pro = along_y(pro, prolong_matrix(cy))
    inner = pro[1:-1]
    even = 0.75 * inner + 0.25 * pro[:-2]
    odd = 0.75 * inner + 0.25 * pro[2:]
    log_perm = jnp.stack((even, odd), axis=1).reshape(2 * (n_ext - 2), fy, fx)
    k0_first = 2 * (g0 + 1)
    k0_planes = log_perm.shape[0]

    positions = k0_first + jnp.arange(k0_planes, dtype=jnp.int32)
    depth_table = mode_table(MZ, fine_total, positions)
    rows_table = mode_table(MY, fy, jnp.arange(fy, dtype=jnp.int32))
    cols_table = mode_table(MX, fx, jnp.arange(fx, dtype=jnp.int32))
    along_depth = jnp.einsum("abe,az->zbe", kl_coeffs[0], depth_table, precision=HI)
    along_rows = jnp.einsum("zbe,by->zye", along_depth, rows_table, precision=HI)
    kl = jnp.dot(along_rows.reshape(k0_planes * fy, MX), cols_table,
                 precision=HI).reshape(k0_planes, fy, fx)
    k0 = jnp.exp(log_perm + kl)
    k0 = jnp.where(plane_mask(k0_first, k0_planes, fine_total), k0, 0.0)
    k0_halo = (k0_planes - fz) // 2

    k1 = 0.125 * restrict_sum(k0)
    k1_halo = k0_halo // 2
    own1 = fz // 2
    k2_own = 0.125 * restrict_sum(k1[k1_halo:k1_halo + own1])

    h0k = F0_HALO + 1
    lvl0 = Level(k0[k0_halo - h0k: k0_halo + fz + h0k], h0k, fz, s * fz - h0k, fine_total)
    f0 = jnp.concatenate([shift_from(source[fz - F0_HALO:], 1), source,
                          shift_from(source[:F0_HALO], -1)], axis=0)
    u = lvl0.start(f0, F0_HALO)
    u1 = lvl0.sweep(u, lvl0.cut(f0, F0_HALO - 1, F0_HALO), F0_HALO)
    res0 = f0[F0_HALO:F0_HALO + fz] - lvl0.operate(u1[1:-1], 1)
    f1_own = 0.5 * restrict_sum(res0)

    h1k = F1_HALO + 1
    lvl1 = Level(k1[k1_halo - h1k: k1_halo + own1 + h1k], h1k, own1, s * own1 - h1k,
                 fine_total // 2)
    f1 = jnp.concatenate([shift_from(f1_own, 1), f1_own, shift_from(f1_own, -1)], axis=0)
    v = lvl1.start(f1, F1_HALO)
    v1 = lvl1.sweep(v, lvl1.cut(f1, F1_HALO - 1, F1_HALO), F1_HALO)
    res1 = f1_own - lvl1.operate(v1[2:-2], 1)
    both = gather_window(jnp.stack([0.5 * restrict_sum(res1), k2_own]))

    own2 = own1 // 2
    total2 = fine_total // 4
    k2_halo = 13
    f2_halo = k2_halo - 1
    reach = (both.shape[0] // 2) * own2
    f2w = both[:, 0].reshape((-1,) + both.shape[3:])[reach - f2_halo: reach + own2 + f2_halo]
    k2w = both[:, 1].reshape((-1,) + both.shape[3:])[reach - k2_halo: reach + own2 + k2_halo]
    lvl2 = Level(k2w, k2_halo, own2, s * own2 - k2_halo, total2)
    w = lvl2.start(f2w, f2_halo)
    w1 = lvl2.sweep(w, lvl2.cut(f2w, f2_halo - 1, f2_halo), f2_halo)
    res2 = lvl2.cut(f2w, f2_halo - 2, f2_halo) - lvl2.operate(w1, f2_halo - 1)
    f3 = 0.5 * restrict_sum(res2)
    f3_halo = (f2_halo - 2) // 2
    k3 = 0.125 * restrict_sum(k2w[1:-1])
    lvl3 = Level(k3, f3_halo + 1, own2 // 2, s * (own2 // 2) - f3_halo - 1, total2 // 2)
    b = lvl3.start(f3, f3_halo)
    for step in range(BOTTOM - 1):
        h = f3_halo - step
        b = lvl3.sweep(b, lvl3.cut(f3, h - 1, f3_halo), h)
    e3_halo = f3_halo - (BOTTOM - 1)
    cut2 = (f2_halo - 1) - 2 * e3_halo
    w = w1[cut2:w1.shape[0] - cut2] + copy_up(b)
    h = 2 * e3_halo
    for _ in range(SWEEPS):
        w = lvl2.sweep(w, lvl2.cut(f2w, h - 1, f2_halo), h)
        h -= 1
    e2 = w

    v = v1 + copy_up(e2)[1:-1]
    v = lvl1.sweep(v, lvl1.cut(f1, 2, F1_HALO), 3)
    e1 = lvl1.sweep(v, lvl1.cut(f1, 1, F1_HALO), 2)

    u = u1 + copy_up(e1)
    u = lvl0.sweep(u, lvl0.cut(f0, 1, F0_HALO), 2)
    u = lvl0.sweep(u, source, 1)
    return u[None]


def solution(mesh):
    return jax.shard_map(
        on_device,
        mesh=mesh,
        in_specs=(
            P("chain", None, "slab", None, None),
            P("chain", None),
            P(),
            P("chain", None, None, None),
            P("slab", None, None),
        ),
        out_specs=P("chain", "slab", None, None),
        check_vma=False,
    )
```

```python
import numpy as np
import jax
import jax.numpy as jnp
from jax import lax
from jax.sharding import PartitionSpec as P

STEPS = 4
MZ = 32
MY = 16
MX = 64
LEVELS = 4
SWEEPS = 2
BOTTOM = 4

OMEGA = 0.8
HI = lax.Precision.HIGHEST

K0_HALO = 10
F0_HALO = 3
F1_HALO = 4
COARSE_HALO = 6


def pair_sum_matrix(n):
    m = np.zeros((n, n // 2), np.float32)
    m[np.arange(n), np.arange(n) // 2] = 1.0
    return m


def repeat_matrix(n):
    return np.ascontiguousarray(pair_sum_matrix(2 * n).T)


def prolong_matrix(n):
    m = np.zeros((n, 2 * n), np.float32)
    for i in range(n):
        m[i, 2 * i] += 0.75
        m[max(i - 1, 0), 2 * i] += 0.25
        m[i, 2 * i + 1] += 0.75
        m[min(i + 1, n - 1), 2 * i + 1] += 0.25
    return m


def along_x(values, matrix, precision=HI):
    return jnp.einsum("zyx,xw->zyw", values, jnp.asarray(matrix), precision=precision,
                      preferred_element_type=jnp.float32)


def along_y(values, matrix, precision=HI):
    return jnp.einsum("zyx,yv->zvx", values, jnp.asarray(matrix), precision=precision,
                      preferred_element_type=jnp.float32)


def restrict_sum(values):
    nz, ny, nx = values.shape
    values = values.reshape(nz // 2, 2, ny, nx).sum(axis=1)
    values = along_y(values, pair_sum_matrix(ny))
    return along_x(values, pair_sum_matrix(nx))


def copy_up(values):
    nz, ny, nx = values.shape
    values = along_x(values, repeat_matrix(nx))
    values = along_y(values, repeat_matrix(ny))
    return jnp.repeat(values, 2, axis=0)


def shift_from(block, offset):
    count = lax.axis_size("slab")
    pairs = [(i, i + offset) for i in range(count) if 0 <= i + offset < count]
    return lax.ppermute(block, "slab", pairs)


def gather_window(block):
    got = jnp.concatenate([shift_from(block[None], 1), block[None], shift_from(block[None], -1)])
    got = jnp.concatenate([shift_from(got[:2], 2), got, shift_from(got[1:], -2)])
    return jnp.concatenate([shift_from(got[:4], 4), got, shift_from(got[3:], -4)])


def plane_mask(first_global, planes, total):
    g = first_global + jnp.arange(planes, dtype=jnp.int32)
    return ((g >= 0) & (g < total))[:, None, None]


class Level:
    def __init__(self, k, k_halo, own, first_global, total):
        self.own = own
        self.halo = k_halo - 1
        self.first = first_global + 1
        self.total = total
        faces_z = 0.5 * (k[1:] + k[:-1])
        kc = k[1:-1]
        rows = jnp.pad(kc, ((0, 0), (1, 1), (0, 0)))
        self.fy = 0.5 * (rows[:, 1:] + rows[:, :-1])
        cols = jnp.pad(kc, ((0, 0), (0, 0), (1, 1)))
        self.fx = 0.5 * (cols[:, :, 1:] + cols[:, :, :-1])
        self.fzl = faces_z[:-1]
        self.fzu = faces_z[1:]
        diag = self.fzl + self.fzu + self.fy[:, 1:] + self.fy[:, :-1]
        diag = diag + self.fx[:, :, 1:] + self.fx[:, :, :-1]
        inside = plane_mask(self.first, kc.shape[0], total)
        self.fzl = jnp.where(inside, self.fzl, 0.0)
        self.fzu = jnp.where(inside, self.fzu, 0.0)
        self.fy = jnp.where(inside, self.fy, 0.0)
        self.fx = jnp.where(inside, self.fx, 0.0)
        self.diag = jnp.where(inside, diag, 1.0)

    def cut(self, arr, h, have):
        n = self.own + 2 * h
        return arr[have - h: have - h + n]

    def coef(self, h):
        c = self.cut
        H = self.halo
        return c(self.fzl, h, H), c(self.fzu, h, H), c(self.fy, h, H), c(self.fx, h, H), c(self.diag, h, H)

    def operate(self, u, h):
        fzl, fzu, fy, fx, diag = self.coef(h - 1)
        uc = u[1:-1]
        rows = jnp.pad(uc, ((0, 0), (1, 1), (0, 0)))
        cols = jnp.pad(uc, ((0, 0), (0, 0), (1, 1)))
        nb = fzu * u[2:] + fzl * u[:-2]
        nb = nb + fy[:, 1:] * rows[:, 2:] + fy[:, :-1] * rows[:, :-2]
        nb = nb + fx[:, :, 1:] * cols[:, :, 2:] + fx[:, :, :-1] * cols[:, :, :-2]
        return diag * uc - nb

    def sweep(self, u, f, h):
        diag = self.coef(h - 1)[4]
        return u[1:-1] + OMEGA * (f - self.operate(u, h)) / diag

    def start(self, f, h):
        return OMEGA * f / self.coef(h)[4]


def mode_table(mode_count, length, positions):
    frequency = length // 2 + jnp.arange(mode_count, dtype=jnp.int32)
    phases = frequency[:, None] * (2 * positions[None, :] + 1) % (4 * length)
    return jnp.cos(jnp.pi * phases.astype(jnp.float32) / (2 * length))


def on_device(coarse_states, accept_flags, owners, kl_coeffs, source):
    slabs = lax.axis_size("slab")
    chain_index = lax.axis_index("chain")
    s = lax.axis_index("slab")
    step_numbers = jnp.arange(1, STEPS, dtype=jnp.int32)
    chosen = jnp.max(jnp.where(accept_flags == 1, step_numbers[None, :], 0), axis=1)
    local_count = coarse_states.shape[0]
    accepted = coarse_states[jnp.arange(local_count, dtype=jnp.int32), chosen]
    every_field = lax.all_gather(accepted, "chain", axis=0, tiled=True)
    own = lax.dynamic_index_in_dim(every_field, owners[chain_index], 0, keepdims=False)

    cz, cy, cx = own.shape
    fz = source.shape[0]
    fy, fx = 2 * cy, 2 * cx
    coarse_total = cz * slabs
    fine_total = fz * slabs

    far = COARSE_HALO - cz
    parts = [shift_from(own[cz - far:], 2), shift_from(own, 1), own,
             shift_from(own, -1), shift_from(own[:far], -2)]
    ext = jnp.concatenate(parts, axis=0)
    n_ext = ext.shape[0]
    g0 = s * cz - COARSE_HALO
    gidx = g0 + jnp.arange(n_ext, dtype=jnp.int32)
    lo_plane = lax.dynamic_index_in_dim(ext, jnp.maximum(-g0, 0), 0, keepdims=True)
    hi_plane = lax.dynamic_index_in_dim(ext, jnp.minimum(coarse_total - 1 - g0, n_ext - 1), 0, keepdims=True)
    ext = jnp.where((gidx < 0)[:, None, None], lo_plane, ext)
    ext = jnp.where((gidx >= coarse_total)[:, None, None], hi_plane, ext)

    pro = along_x(ext, prolong_matrix(cx).astype(jnp.bfloat16), precision=lax.Precision.DEFAULT)
    pro = along_y(pro, prolong_matrix(cy))
    inner = pro[1:-1]
    even = 0.75 * inner + 0.25 * pro[:-2]
    odd = 0.75 * inner + 0.25 * pro[2:]
    log_perm = jnp.stack((even, odd), axis=1).reshape(2 * (n_ext - 2), fy, fx)
    k0_first = 2 * (g0 + 1)
    k0_planes = log_perm.shape[0]

    positions = k0_first + jnp.arange(k0_planes, dtype=jnp.int32)
    depth_table = mode_table(MZ, fine_total, positions)
    rows_table = mode_table(MY, fy, jnp.arange(fy, dtype=jnp.int32))
    cols_table = mode_table(MX, fx, jnp.arange(fx, dtype=jnp.int32))
    along_depth = jnp.einsum("abe,az->zbe", kl_coeffs[0], depth_table, precision=HI)
    along_rows = jnp.einsum("zbe,by->zye", along_depth, rows_table, precision=HI)
    kl = jnp.dot(along_rows.reshape(k0_planes * fy, MX), cols_table,
                 precision=HI).reshape(k0_planes, fy, fx)
    k0 = jnp.exp(log_perm + kl)
    k0 = jnp.where(plane_mask(k0_first, k0_planes, fine_total), k0, 0.0)
    k0_halo = (k0_planes - fz) // 2

    k1 = 0.125 * restrict_sum(k0)
    k1_halo = k0_halo // 2
    own1 = fz // 2
    k2_own = 0.125 * restrict_sum(k1[k1_halo:k1_halo + own1])

    h0k = F0_HALO + 1
    lvl0 = Level(k0[k0_halo - h0k: k0_halo + fz + h0k], h0k, fz, s * fz - h0k, fine_total)
    f0 = jnp.concatenate([shift_from(source[fz - F0_HALO:], 1), source,
                          shift_from(source[:F0_HALO], -1)], axis=0)
    u = lvl0.start(f0, F0_HALO)
    u1 = lvl0.sweep(u, lvl0.cut(f0, F0_HALO - 1, F0_HALO), F0_HALO)
    res0 = f0[F0_HALO:F0_HALO + fz] - lvl0.operate(u1[1:-1], 1)
    f1_own = 0.5 * restrict_sum(res0)

    h1k = F1_HALO + 1
    lvl1 = Level(k1[k1_halo - h1k: k1_halo + own1 + h1k], h1k, own1, s * own1 - h1k,
                 fine_total // 2)
    f1 = jnp.concatenate([shift_from(f1_own, 1), f1_own, shift_from(f1_own, -1)], axis=0)
    v = lvl1.start(f1, F1_HALO)
    v1 = lvl1.sweep(v, lvl1.cut(f1, F1_HALO - 1, F1_HALO), F1_HALO)
    res1 = f1_own - lvl1.operate(v1[2:-2], 1)
    both = gather_window(jnp.stack([0.5 * restrict_sum(res1), k2_own]))

    own2 = own1 // 2
    total2 = fine_total // 4
    k2_halo = 13
    f2_halo = k2_halo - 1
    reach = (both.shape[0] // 2) * own2
    f2w = both[:, 0].reshape((-1,) + both.shape[3:])[reach - f2_halo: reach + own2 + f2_halo]
    k2w = both[:, 1].reshape((-1,) + both.shape[3:])[reach - k2_halo: reach + own2 + k2_halo]
    lvl2 = Level(k2w, k2_halo, own2, s * own2 - k2_halo, total2)
    w = lvl2.start(f2w, f2_halo)
    w1 = lvl2.sweep(w, lvl2.cut(f2w, f2_halo - 1, f2_halo), f2_halo)
    res2 = lvl2.cut(f2w, f2_halo - 2, f2_halo) - lvl2.operate(w1, f2_halo - 1)
    f3 = 0.5 * restrict_sum(res2)
    f3_halo = (f2_halo - 2) // 2
    k3 = 0.125 * restrict_sum(k2w[1:-1])
    lvl3 = Level(k3, f3_halo + 1, own2 // 2, s * (own2 // 2) - f3_halo - 1, total2 // 2)
    b = lvl3.start(f3, f3_halo)
    for step in range(BOTTOM - 1):
        h = f3_halo - step
        b = lvl3.sweep(b, lvl3.cut(f3, h - 1, f3_halo), h)
    e3_halo = f3_halo - (BOTTOM - 1)
    cut2 = (f2_halo - 1) - 2 * e3_halo
    w = w1[cut2:w1.shape[0] - cut2] + copy_up(b)
    h = 2 * e3_halo
    for _ in range(SWEEPS):
        w = lvl2.sweep(w, lvl2.cut(f2w, h - 1, f2_halo), h)
        h -= 1
    e2 = w

    v = v1 + copy_up(e2)[1:-1]
    v = lvl1.sweep(v, lvl1.cut(f1, 2, F1_HALO), 3)
    e1 = lvl1.sweep(v, lvl1.cut(f1, 1, F1_HALO), 2)

    u = u1 + copy_up(e1)
    u = lvl0.sweep(u, lvl0.cut(f0, 1, F0_HALO), 2)
    u = lvl0.sweep(u, source, 1)
    return u[None]


def solution(mesh):
    return jax.shard_map(
        on_device,
        mesh=mesh,
        in_specs=(
            P("chain", None, "slab", None, None),
            P("chain", None),
            P(),
            P("chain", None, None, None),
            P("slab", None, None),
        ),
        out_specs=P("chain", "slab", None, None),
        check_vma=False,
    )
```

```python
import numpy as np
import jax
import jax.numpy as jnp
from jax import lax
from jax.sharding import PartitionSpec as P

STEPS = 4
MZ = 32
MY = 16
MX = 64
LEVELS = 4
SWEEPS = 2
BOTTOM = 4

OMEGA = 0.8
HI = lax.Precision.HIGHEST

F0_HALO = 3
F1_HALO = 4
COARSE_HALO = 4


def pair_sum_matrix(n):
    m = np.zeros((n, n // 2), np.float32)
    m[np.arange(n), np.arange(n) // 2] = 1.0
    return m


def repeat_matrix(n):
    return np.ascontiguousarray(pair_sum_matrix(2 * n).T)


def prolong_matrix(n):
    m = np.zeros((n, 2 * n), np.float32)
    for i in range(n):
        m[i, 2 * i] += 0.75
        m[max(i - 1, 0), 2 * i] += 0.25
        m[i, 2 * i + 1] += 0.75
        m[min(i + 1, n - 1), 2 * i + 1] += 0.25
    return m


def along_x(values, matrix, precision=HI):
    return jnp.einsum("zyx,xw->zyw", values, jnp.asarray(matrix), precision=precision,
                      preferred_element_type=jnp.float32)


def along_y(values, matrix, precision=HI):
    return jnp.einsum("zyx,yv->zvx", values, jnp.asarray(matrix), precision=precision,
                      preferred_element_type=jnp.float32)


def restrict_sum(values):
    nz, ny, nx = values.shape
    values = values.reshape(nz // 2, 2, ny, nx).sum(axis=1)
    values = along_y(values, pair_sum_matrix(ny))
    return along_x(values, pair_sum_matrix(nx))


def copy_up(values):
    nz, ny, nx = values.shape
    values = along_x(values, repeat_matrix(nx))
    values = along_y(values, repeat_matrix(ny))
    return jnp.repeat(values, 2, axis=0)


def shift_from(block, offset):
    count = lax.axis_size("slab")
    pairs = [(i, i + offset) for i in range(count) if 0 <= i + offset < count]
    return lax.ppermute(block, "slab", pairs)


def gather_window(block):
    got = jnp.concatenate([shift_from(block[None], 1), block[None], shift_from(block[None], -1)])
    got = jnp.concatenate([shift_from(got[:2], 2), got, shift_from(got[1:], -2)])
    return jnp.concatenate([shift_from(got[:4], 4), got, shift_from(got[3:], -4)])


def plane_mask(first_global, planes, total):
    g = first_global + jnp.arange(planes, dtype=jnp.int32)
    return ((g >= 0) & (g < total))[:, None, None]


class Level:
    def __init__(self, k, k_halo, own, first_global, total):
        self.own = own
        self.halo = k_halo - 1
        self.first = first_global + 1
        self.total = total
        faces_z = 0.5 * (k[1:] + k[:-1])
        kc = k[1:-1]
        rows = jnp.pad(kc, ((0, 0), (1, 1), (0, 0)))
        self.fy = 0.5 * (rows[:, 1:] + rows[:, :-1])
        cols = jnp.pad(kc, ((0, 0), (0, 0), (1, 1)))
        self.fx = 0.5 * (cols[:, :, 1:] + cols[:, :, :-1])
        self.fzl = faces_z[:-1]
        self.fzu = faces_z[1:]
        diag = self.fzl + self.fzu + self.fy[:, 1:] + self.fy[:, :-1]
        self.diag = diag + self.fx[:, :, 1:] + self.fx[:, :, :-1]

    def cut(self, arr, h, have):
        n = self.own + 2 * h
        return arr[have - h: have - h + n]

    def coef(self, h):
        c = self.cut
        H = self.halo
        return c(self.fzl, h, H), c(self.fzu, h, H), c(self.fy, h, H), c(self.fx, h, H), c(self.diag, h, H)

    def mask(self, u, h):
        return jnp.where(plane_mask(self.first + self.halo - h, u.shape[0], self.total), u, 0.0)

    def operate(self, u, h):
        fzl, fzu, fy, fx, diag = self.coef(h - 1)
        uc = u[1:-1]
        rows = jnp.pad(uc, ((0, 0), (1, 1), (0, 0)))
        cols = jnp.pad(uc, ((0, 0), (0, 0), (1, 1)))
        nb = fzu * u[2:] + fzl * u[:-2]
        nb = nb + fy[:, 1:] * rows[:, 2:] + fy[:, :-1] * rows[:, :-2]
        nb = nb + fx[:, :, 1:] * cols[:, :, 2:] + fx[:, :, :-1] * cols[:, :, :-2]
        return diag * uc - nb

    def sweep(self, u, f, h):
        diag = self.coef(h - 1)[4]
        new = u[1:-1] + OMEGA * (f - self.operate(u, h)) / diag
        return self.mask(new, h - 1)

    def start(self, f, h):
        return self.mask(OMEGA * f / self.coef(h)[4], h)


def mode_table(mode_count, length, positions):
    frequency = length // 2 + jnp.arange(mode_count, dtype=jnp.int32)
    phases = frequency[:, None] * (2 * positions[None, :] + 1) % (4 * length)
    return jnp.cos(jnp.pi * phases.astype(jnp.float32) / (2 * length))


def on_device(coarse_states, accept_flags, owners, kl_coeffs, source):
    slabs = lax.axis_size("slab")
    chain_index = lax.axis_index("chain")
    s = lax.axis_index("slab")
    step_numbers = jnp.arange(1, STEPS, dtype=jnp.int32)
    chosen = jnp.max(jnp.where(accept_flags == 1, step_numbers[None, :], 0), axis=1)
    local_count = coarse_states.shape[0]
    accepted = coarse_states[jnp.arange(local_count, dtype=jnp.int32), chosen]
    every_field = lax.all_gather(accepted, "chain", axis=0, tiled=True)
    own = lax.dynamic_index_in_dim(every_field, owners[chain_index], 0, keepdims=False)

    cz, cy, cx = own.shape
    fz = source.shape[0]
    fy, fx = 2 * cy, 2 * cx
    coarse_total = cz * slabs
    fine_total = fz * slabs

    ext = jnp.concatenate([shift_from(own, 1), own, shift_from(own, -1)], axis=0)
    n_ext = ext.shape[0]
    g0 = s * cz - COARSE_HALO
    gidx = g0 + jnp.arange(n_ext, dtype=jnp.int32)
    lo_plane = lax.dynamic_index_in_dim(ext, jnp.maximum(-g0, 0), 0, keepdims=True)
    hi_plane = lax.dynamic_index_in_dim(ext, jnp.minimum(coarse_total - 1 - g0, n_ext - 1), 0, keepdims=True)
    ext = jnp.where((gidx < 0)[:, None, None], lo_plane, ext)
    ext = jnp.where((gidx >= coarse_total)[:, None, None], hi_plane, ext)

    pro = along_x(ext, prolong_matrix(cx).astype(jnp.bfloat16), precision=lax.Precision.DEFAULT)
    pro = along_y(pro, prolong_matrix(cy))
    inner = pro[1:-1]
    even = 0.75 * inner + 0.25 * pro[:-2]
    odd = 0.75 * inner + 0.25 * pro[2:]
    log_perm = jnp.stack((even, odd), axis=1).reshape(2 * (n_ext - 2), fy, fx)
    k0_first = 2 * (g0 + 1)
    k0_planes = log_perm.shape[0]

    positions = k0_first + jnp.arange(k0_planes, dtype=jnp.int32)
    depth_table = mode_table(MZ, fine_total, positions)
    rows_table = mode_table(MY, fy, jnp.arange(fy, dtype=jnp.int32))
    cols_table = mode_table(MX, fx, jnp.arange(fx, dtype=jnp.int32))
    along_depth = jnp.einsum("abe,az->zbe", kl_coeffs[0], depth_table, precision=HI)
    along_rows = jnp.einsum("zbe,by->zye", along_depth, rows_table, precision=HI)
    kl = jnp.dot(along_rows.reshape(k0_planes * fy, MX), cols_table,
                 precision=HI).reshape(k0_planes, fy, fx)
    k0 = jnp.exp(log_perm + kl)
    k0 = jnp.where(plane_mask(k0_first, k0_planes, fine_total), k0, 0.0)
    k0_halo = (k0_planes - fz) // 2

    k1 = 0.125 * restrict_sum(k0)
    k1_halo = k0_halo // 2
    own1 = fz // 2
    k2_own = 0.125 * restrict_sum(k1[k1_halo:k1_halo + own1])

    h0k = F0_HALO + 1
    lvl0 = Level(k0[k0_halo - h0k: k0_halo + fz + h0k], h0k, fz, s * fz - h0k, fine_total)
    f0 = jnp.concatenate([shift_from(source[fz - F0_HALO:], 1), source,
                          shift_from(source[:F0_HALO], -1)], axis=0)
    u = lvl0.start(f0, F0_HALO)
    u1 = lvl0.sweep(u, lvl0.cut(f0, F0_HALO - 1, F0_HALO), F0_HALO)
    res0 = f0[F0_HALO:F0_HALO + fz] - lvl0.operate(u1[1:-1], 1)
    f1_own = 0.5 * restrict_sum(res0)

    h1k = F1_HALO + 1
    extra = h1k - k1_halo
    from_left = shift_from(jnp.concatenate([k1[own1 - extra: own1], f1_own]), 1)
    from_right = shift_from(jnp.concatenate([f1_own, k1[2 * k1_halo: 2 * k1_halo + extra]]), -1)
    k1_ext = jnp.concatenate([from_left[:extra], k1, from_right[own1:]], axis=0)
    f1 = jnp.concatenate([from_left[extra:], f1_own, from_right[:own1]], axis=0)
    lvl1 = Level(k1_ext, h1k, own1, s * own1 - h1k, fine_total // 2)
    v = lvl1.start(f1, F1_HALO)
    v1 = lvl1.sweep(v, lvl1.cut(f1, F1_HALO - 1, F1_HALO), F1_HALO)
    res1 = f1_own - lvl1.operate(v1[2:-2], 1)
    both = gather_window(jnp.stack([0.5 * restrict_sum(res1), k2_own]))

    own2 = own1 // 2
    total2 = fine_total // 4
    k2_halo = 13
    f2_halo = k2_halo - 1
    reach = (both.shape[0] // 2) * own2
    f2w = both[:, 0].reshape((-1,) + both.shape[3:])[reach - f2_halo: reach + own2 + f2_halo]
    k2w = both[:, 1].reshape((-1,) + both.shape[3:])[reach - k2_halo: reach + own2 + k2_halo]
    lvl2 = Level(k2w, k2_halo, own2, s * own2 - k2_halo, total2)
    w = lvl2.start(f2w, f2_halo)
    w1 = lvl2.sweep(w, lvl2.cut(f2w, f2_halo - 1, f2_halo), f2_halo)
    res2 = lvl2.cut(f2w, f2_halo - 2, f2_halo) - lvl2.operate(w1, f2_halo - 1)
    f3 = 0.5 * restrict_sum(res2)
    f3_halo = (f2_halo - 2) // 2
    k3 = 0.125 * restrict_sum(k2w[1:-1])
    lvl3 = Level(k3, f3_halo + 1, own2 // 2, s * (own2 // 2) - f3_halo - 1, total2 // 2)
    b = lvl3.start(f3, f3_halo)
    for step in range(BOTTOM - 1):
        h = f3_halo - step
        b = lvl3.sweep(b, lvl3.cut(f3, h - 1, f3_halo), h)
    e3_halo = f3_halo - (BOTTOM - 1)
    cut2 = (f2_halo - 1) - 2 * e3_halo
    w = w1[cut2:w1.shape[0] - cut2] + copy_up(b)
    h = 2 * e3_halo
    for _ in range(SWEEPS):
        w = lvl2.sweep(w, lvl2.cut(f2w, h - 1, f2_halo), h)
        h -= 1
    e2 = w

    v = v1 + copy_up(e2)[1:-1]
    v = lvl1.sweep(v, lvl1.cut(f1, 2, F1_HALO), 3)
    e1 = lvl1.sweep(v, lvl1.cut(f1, 1, F1_HALO), 2)

    u = u1 + copy_up(e1)
    u = lvl0.sweep(u, lvl0.cut(f0, 1, F0_HALO), 2)
    u = lvl0.sweep(u, source, 1)
    return u[None]


def solution(mesh):
    return jax.shard_map(
        on_device,
        mesh=mesh,
        in_specs=(
            P("chain", None, "slab", None, None),
            P("chain", None),
            P(),
            P("chain", None, None, None),
            P("slab", None, None),
        ),
        out_specs=P("chain", "slab", None, None),
        check_vma=False,
    )
```

```python
import numpy as np
import jax
import jax.numpy as jnp
from jax import lax
from jax.sharding import PartitionSpec as P

STEPS = 4
MZ = 32
MY = 16
MX = 64
LEVELS = 4
SWEEPS = 2
BOTTOM = 4

OMEGA = 0.8
HI = lax.Precision.HIGHEST

F0_HALO = 3
F1_HALO = 4
COARSE_HALO = 4


def pair_sum_matrix(n):
    m = np.zeros((n, n // 2), np.float32)
    m[np.arange(n), np.arange(n) // 2] = 1.0
    return m


def repeat_matrix(n):
    return np.ascontiguousarray(pair_sum_matrix(2 * n).T)


def prolong_matrix(n):
    m = np.zeros((n, 2 * n), np.float32)
    for i in range(n):
        m[i, 2 * i] += 0.75
        m[max(i - 1, 0), 2 * i] += 0.25
        m[i, 2 * i + 1] += 0.75
        m[min(i + 1, n - 1), 2 * i + 1] += 0.25
    return m


def along_x(values, matrix, precision=HI):
    return jnp.einsum("zyx,xw->zyw", values, jnp.asarray(matrix), precision=precision,
                      preferred_element_type=jnp.float32)


def along_y(values, matrix, precision=HI):
    return jnp.einsum("zyx,yv->zvx", values, jnp.asarray(matrix), precision=precision,
                      preferred_element_type=jnp.float32)


def restrict_sum(values):
    nz, ny, nx = values.shape
    values = values.reshape(nz // 2, 2, ny, nx).sum(axis=1)
    values = along_y(values, pair_sum_matrix(ny))
    return along_x(values, pair_sum_matrix(nx))


def copy_up(values):
    nz, ny, nx = values.shape
    values = along_x(values, repeat_matrix(nx))
    values = along_y(values, repeat_matrix(ny))
    return jnp.repeat(values, 2, axis=0)


def shift_from(block, offset):
    count = lax.axis_size("slab")
    pairs = [(i, i + offset) for i in range(count) if 0 <= i + offset < count]
    return lax.ppermute(block, "slab", pairs)


def gather_window(block):
    got = jnp.concatenate([shift_from(block[None], 1), block[None], shift_from(block[None], -1)])
    got = jnp.concatenate([shift_from(got[:2], 2), got, shift_from(got[1:], -2)])
    return jnp.concatenate([shift_from(got[:4], 4), got, shift_from(got[3:], -4)])


def plane_mask(first_global, planes, total):
    g = first_global + jnp.arange(planes, dtype=jnp.int32)
    return ((g >= 0) & (g < total))[:, None, None]


class Level:
    def __init__(self, k, k_halo, own, first_global, total):
        self.own = own
        self.halo = k_halo - 1
        self.first = first_global + 1
        self.total = total
        faces_z = 0.5 * (k[1:] + k[:-1])
        kc = k[1:-1]
        rows = jnp.pad(kc, ((0, 0), (1, 1), (0, 0)))
        self.fy = 0.5 * (rows[:, 1:] + rows[:, :-1])
        cols = jnp.pad(kc, ((0, 0), (0, 0), (1, 1)))
        self.fx = 0.5 * (cols[:, :, 1:] + cols[:, :, :-1])
        self.fzl = faces_z[:-1]
        self.fzu = faces_z[1:]
        diag = self.fzl + self.fzu + self.fy[:, 1:] + self.fy[:, :-1]
        self.diag = diag + self.fx[:, :, 1:] + self.fx[:, :, :-1]

    def cut(self, arr, h, have):
        n = self.own + 2 * h
        return arr[have - h: have - h + n]

    def coef(self, h):
        c = self.cut
        H = self.halo
        return c(self.fzl, h, H), c(self.fzu, h, H), c(self.fy, h, H), c(self.fx, h, H), c(self.diag, h, H)

    def mask(self, u, h):
        return jnp.where(plane_mask(self.first + self.halo - h, u.shape[0], self.total), u, 0.0)

    def operate(self, u, h):
        fzl, fzu, fy, fx, diag = self.coef(h - 1)
        uc = u[1:-1]
        rows = jnp.pad(uc, ((0, 0), (1, 1), (0, 0)))
        cols = jnp.pad(uc, ((0, 0), (0, 0), (1, 1)))
        nb = fzu * u[2:] + fzl * u[:-2]
        nb = nb + fy[:, 1:] * rows[:, 2:] + fy[:, :-1] * rows[:, :-2]
        nb = nb + fx[:, :, 1:] * cols[:, :, 2:] + fx[:, :, :-1] * cols[:, :, :-2]
        return diag * uc - nb

    def sweep(self, u, f, h):
        diag = self.coef(h - 1)[4]
        new = u[1:-1] + OMEGA * (f - self.operate(u, h)) / diag
        return self.mask(new, h - 1)

    def start(self, f, h):
        return self.mask(OMEGA * f / self.coef(h)[4], h)


def mode_table(mode_count, length, positions):
    frequency = length // 2 + jnp.arange(mode_count, dtype=jnp.int32)
    phases = frequency[:, None] * (2 * positions[None, :] + 1) % (4 * length)
    return jnp.cos(jnp.pi * phases.astype(jnp.float32) / (2 * length))


def on_device(coarse_states, accept_flags, owners, kl_coeffs, source):
    slabs = lax.axis_size("slab")
    chain_index = lax.axis_index("chain")
    s = lax.axis_index("slab")
    step_numbers = jnp.arange(1, STEPS, dtype=jnp.int32)
    chosen = jnp.max(jnp.where(accept_flags == 1, step_numbers[None, :], 0), axis=1)
    local_count = coarse_states.shape[0]
    accepted = coarse_states[jnp.arange(local_count, dtype=jnp.int32), chosen]
    every_field = lax.all_gather(accepted, "chain", axis=0, tiled=True)
    own = lax.dynamic_index_in_dim(every_field, owners[chain_index], 0, keepdims=False)

    cz, cy, cx = own.shape
    fz = source.shape[0]
    fy, fx = 2 * cy, 2 * cx
    coarse_total = cz * slabs
    fine_total = fz * slabs

    crow = cz * cy * cx // fx

    def pack(source_part):
        return jnp.concatenate([own.astype(jnp.float32).reshape(crow, fx),
                                source_part.reshape(-1, fx)], axis=0)

    got_l = shift_from(pack(source[fz - F0_HALO:]), 1)
    got_r = shift_from(pack(source[:F0_HALO]), -1)
    coarse_l = got_l[:crow].reshape(cz, cy, cx).astype(own.dtype)
    coarse_r = got_r[:crow].reshape(cz, cy, cx).astype(own.dtype)
    ext = jnp.concatenate([coarse_l, own, coarse_r], axis=0)
    n_ext = ext.shape[0]
    g0 = s * cz - COARSE_HALO
    gidx = g0 + jnp.arange(n_ext, dtype=jnp.int32)
    lo_plane = lax.dynamic_index_in_dim(ext, jnp.maximum(-g0, 0), 0, keepdims=True)
    hi_plane = lax.dynamic_index_in_dim(ext, jnp.minimum(coarse_total - 1 - g0, n_ext - 1), 0, keepdims=True)
    ext = jnp.where((gidx < 0)[:, None, None], lo_plane, ext)
    ext = jnp.where((gidx >= coarse_total)[:, None, None], hi_plane, ext)

    pro = along_x(ext, prolong_matrix(cx).astype(jnp.bfloat16), precision=lax.Precision.DEFAULT)
    pro = along_y(pro, prolong_matrix(cy))
    inner = pro[1:-1]
    even = 0.75 * inner + 0.25 * pro[:-2]
    odd = 0.75 * inner + 0.25 * pro[2:]
    log_perm = jnp.stack((even, odd), axis=1).reshape(2 * (n_ext - 2), fy, fx)
    k0_first = 2 * (g0 + 1)
    k0_planes = log_perm.shape[0]

    positions = k0_first + jnp.arange(k0_planes, dtype=jnp.int32)
    depth_table = mode_table(MZ, fine_total, positions)
    rows_table = mode_table(MY, fy, jnp.arange(fy, dtype=jnp.int32))
    cols_table = mode_table(MX, fx, jnp.arange(fx, dtype=jnp.int32))
    along_depth = jnp.einsum("abe,az->zbe", kl_coeffs[0], depth_table, precision=HI)
    along_rows = jnp.einsum("zbe,by->zye", along_depth, rows_table, precision=HI)
    kl = jnp.dot(along_rows.reshape(k0_planes * fy, MX), cols_table,
                 precision=HI).reshape(k0_planes, fy, fx)
    k0 = jnp.exp(log_perm + kl)
    k0 = jnp.where(plane_mask(k0_first, k0_planes, fine_total), k0, 0.0)
    k0_halo = (k0_planes - fz) // 2

    k1 = 0.125 * restrict_sum(k0)
    k1_halo = k0_halo // 2
    own1 = fz // 2
    k2_own = 0.125 * restrict_sum(k1[k1_halo:k1_halo + own1])

    h0k = F0_HALO + 1
    lvl0 = Level(k0[k0_halo - h0k: k0_halo + fz + h0k], h0k, fz, s * fz - h0k, fine_total)
    f0 = jnp.concatenate([got_l[crow:].reshape(F0_HALO, fy, fx), source,
                          got_r[crow:].reshape(F0_HALO, fy, fx)], axis=0)
    u = lvl0.start(f0, F0_HALO)
    u1 = lvl0.sweep(u, lvl0.cut(f0, F0_HALO - 1, F0_HALO), F0_HALO)
    res0 = f0[F0_HALO:F0_HALO + fz] - lvl0.operate(u1[1:-1], 1)
    f1_own = 0.5 * restrict_sum(res0)

    h1k = F1_HALO + 1
    extra = h1k - k1_halo
    from_left = shift_from(jnp.concatenate([k1[own1 - extra: own1], f1_own]), 1)
    from_right = shift_from(jnp.concatenate([f1_own, k1[2 * k1_halo: 2 * k1_halo + extra]]), -1)
    k1_ext = jnp.concatenate([from_left[:extra], k1, from_right[own1:]], axis=0)
    f1 = jnp.concatenate([from_left[extra:], f1_own, from_right[:own1]], axis=0)
    lvl1 = Level(k1_ext, h1k, own1, s * own1 - h1k, fine_total // 2)
    v = lvl1.start(f1, F1_HALO)
    v1 = lvl1.sweep(v, lvl1.cut(f1, F1_HALO - 1, F1_HALO), F1_HALO)
    res1 = f1_own - lvl1.operate(v1[2:-2], 1)
    both = gather_window(jnp.stack([0.5 * restrict_sum(res1), k2_own]))

    own2 = own1 // 2
    total2 = fine_total // 4
    k2_halo = 13
    f2_halo = k2_halo - 1
    reach = (both.shape[0] // 2) * own2
    f2w = both[:, 0].reshape((-1,) + both.shape[3:])[reach - f2_halo: reach + own2 + f2_halo]
    k2w = both[:, 1].reshape((-1,) + both.shape[3:])[reach - k2_halo: reach + own2 + k2_halo]
    lvl2 = Level(k2w, k2_halo, own2, s * own2 - k2_halo, total2)
    w = lvl2.start(f2w, f2_halo)
    w1 = lvl2.sweep(w, lvl2.cut(f2w, f2_halo - 1, f2_halo), f2_halo)
    res2 = lvl2.cut(f2w, f2_halo - 2, f2_halo) - lvl2.operate(w1, f2_halo - 1)
    f3 = 0.5 * restrict_sum(res2)
    f3_halo = (f2_halo - 2) // 2
    k3 = 0.125 * restrict_sum(k2w[1:-1])
    lvl3 = Level(k3, f3_halo + 1, own2 // 2, s * (own2 // 2) - f3_halo - 1, total2 // 2)
    b = lvl3.start(f3, f3_halo)
    for step in range(BOTTOM - 1):
        h = f3_halo - step
        b = lvl3.sweep(b, lvl3.cut(f3, h - 1, f3_halo), h)
    e3_halo = f3_halo - (BOTTOM - 1)
    cut2 = (f2_halo - 1) - 2 * e3_halo
    w = w1[cut2:w1.shape[0] - cut2] + copy_up(b)
    h = 2 * e3_halo
    for _ in range(SWEEPS):
        w = lvl2.sweep(w, lvl2.cut(f2w, h - 1, f2_halo), h)
        h -= 1
    e2 = w

    v = v1 + copy_up(e2)[1:-1]
    v = lvl1.sweep(v, lvl1.cut(f1, 2, F1_HALO), 3)
    e1 = lvl1.sweep(v, lvl1.cut(f1, 1, F1_HALO), 2)

    u = u1 + copy_up(e1)
    u = lvl0.sweep(u, lvl0.cut(f0, 1, F0_HALO), 2)
    u = lvl0.sweep(u, source, 1)
    return u[None]


def solution(mesh):
    return jax.shard_map(
        on_device,
        mesh=mesh,
        in_specs=(
            P("chain", None, "slab", None, None),
            P("chain", None),
            P(),
            P("chain", None, None, None),
            P("slab", None, None),
        ),
        out_specs=P("chain", "slab", None, None),
        check_vma=False,
    )
```

```python
import numpy as np
import jax
import jax.numpy as jnp
from jax import lax
from jax.sharding import PartitionSpec as P

STEPS = 4
MZ = 32
MY = 16
MX = 64
LEVELS = 4
SWEEPS = 2
BOTTOM = 4

OMEGA = 0.8
HI = lax.Precision.HIGHEST

F0_HALO = 3
F1_HALO = 4
COARSE_HALO = 4


def pair_sum_matrix(n):
    m = np.zeros((n, n // 2), np.float32)
    m[np.arange(n), np.arange(n) // 2] = 1.0
    return m


def repeat_matrix(n):
    return np.ascontiguousarray(pair_sum_matrix(2 * n).T)


def prolong_matrix(n):
    m = np.zeros((n, 2 * n), np.float32)
    for i in range(n):
        m[i, 2 * i] += 0.75
        m[max(i - 1, 0), 2 * i] += 0.25
        m[i, 2 * i + 1] += 0.75
        m[min(i + 1, n - 1), 2 * i + 1] += 0.25
    return m


def along_x(values, matrix, precision=HI):
    return jnp.einsum("zyx,xw->zyw", values, jnp.asarray(matrix), precision=precision,
                      preferred_element_type=jnp.float32)


def along_y(values, matrix, precision=HI):
    return jnp.einsum("zyx,yv->zvx", values, jnp.asarray(matrix), precision=precision,
                      preferred_element_type=jnp.float32)


def restrict_sum(values):
    nz, ny, nx = values.shape
    values = values.reshape(nz // 2, 2, ny, nx).sum(axis=1)
    values = along_y(values, pair_sum_matrix(ny))
    return along_x(values, pair_sum_matrix(nx))


def copy_up(values):
    nz, ny, nx = values.shape
    values = along_x(values, repeat_matrix(nx))
    values = along_y(values, repeat_matrix(ny))
    return jnp.repeat(values, 2, axis=0)


def shift_from(block, offset):
    count = lax.axis_size("slab")
    pairs = [(i, i + offset) for i in range(count) if 0 <= i + offset < count]
    return lax.ppermute(block, "slab", pairs)


def gather_window(block):
    got = jnp.concatenate([shift_from(block[None], 1), block[None], shift_from(block[None], -1)])
    got = jnp.concatenate([shift_from(got[:2], 2), got, shift_from(got[1:], -2)])
    return jnp.concatenate([shift_from(got[:4], 4), got, shift_from(got[3:], -4)])


def plane_mask(first_global, planes, total):
    g = first_global + jnp.arange(planes, dtype=jnp.int32)
    return ((g >= 0) & (g < total))[:, None, None]


class Level:
    def __init__(self, k, k_halo, own, first_global, total):
        self.own = own
        self.halo = k_halo - 1
        self.first = first_global + 1
        self.total = total
        faces_z = 0.5 * (k[1:] + k[:-1])
        kc = k[1:-1]
        rows = jnp.pad(kc, ((0, 0), (1, 1), (0, 0)))
        self.fy = 0.5 * (rows[:, 1:] + rows[:, :-1])
        cols = jnp.pad(kc, ((0, 0), (0, 0), (1, 1)))
        self.fx = 0.5 * (cols[:, :, 1:] + cols[:, :, :-1])
        self.fzl = faces_z[:-1]
        self.fzu = faces_z[1:]
        diag = self.fzl + self.fzu + self.fy[:, 1:] + self.fy[:, :-1]
        self.diag = diag + self.fx[:, :, 1:] + self.fx[:, :, :-1]

    def cut(self, arr, h, have):
        n = self.own + 2 * h
        return arr[have - h: have - h + n]

    def coef(self, h):
        c = self.cut
        H = self.halo
        return c(self.fzl, h, H), c(self.fzu, h, H), c(self.fy, h, H), c(self.fx, h, H), c(self.diag, h, H)

    def mask(self, u, h):
        return jnp.where(plane_mask(self.first + self.halo - h, u.shape[0], self.total), u, 0.0)

    def operate(self, u, h):
        fzl, fzu, fy, fx, diag = self.coef(h - 1)
        uc = u[1:-1]
        rows = jnp.pad(uc, ((0, 0), (1, 1), (0, 0)))
        cols = jnp.pad(uc, ((0, 0), (0, 0), (1, 1)))
        nb = fzu * u[2:] + fzl * u[:-2]
        nb = nb + fy[:, 1:] * rows[:, 2:] + fy[:, :-1] * rows[:, :-2]
        nb = nb + fx[:, :, 1:] * cols[:, :, 2:] + fx[:, :, :-1] * cols[:, :, :-2]
        return diag * uc - nb

    def sweep(self, u, f, h):
        diag = self.coef(h - 1)[4]
        new = u[1:-1] + OMEGA * (f - self.operate(u, h)) / diag
        return self.mask(new, h - 1)

    def start(self, f, h):
        return self.mask(OMEGA * f / self.coef(h)[4], h)


def mode_table(mode_count, length, positions):
    frequency = length // 2 + jnp.arange(mode_count, dtype=jnp.int32)
    phases = frequency[:, None] * (2 * positions[None, :] + 1) % (4 * length)
    return jnp.cos(jnp.pi * phases.astype(jnp.float32) / (2 * length))


def on_device(coarse_states, accept_flags, owners, kl_coeffs, source):
    slabs = lax.axis_size("slab")
    chain_index = lax.axis_index("chain")
    s = lax.axis_index("slab")
    step_numbers = jnp.arange(1, STEPS, dtype=jnp.int32)
    chosen = jnp.max(jnp.where(accept_flags == 1, step_numbers[None, :], 0), axis=1)
    local_count = coarse_states.shape[0]
    accepted = coarse_states[jnp.arange(local_count, dtype=jnp.int32), chosen]
    every_field = lax.all_gather(accepted, "chain", axis=0, tiled=True)
    own = lax.dynamic_index_in_dim(every_field, owners[chain_index], 0, keepdims=False)

    cz, cy, cx = own.shape
    fz = source.shape[0]
    fy, fx = 2 * cy, 2 * cx
    coarse_total = cz * slabs
    fine_total = fz * slabs

    crow = cz * cy * cx // fx

    def pack(source_part):
        return jnp.concatenate([own.astype(jnp.float32).reshape(crow, fx),
                                source_part.reshape(-1, fx)], axis=0)

    got_l = shift_from(pack(source[fz - F0_HALO:]), 1)
    got_r = shift_from(pack(source[:F0_HALO]), -1)
    coarse_l = got_l[:crow].reshape(cz, cy, cx).astype(own.dtype)
    coarse_r = got_r[:crow].reshape(cz, cy, cx).astype(own.dtype)
    ext = jnp.concatenate([coarse_l, own, coarse_r], axis=0)
    n_ext = ext.shape[0]
    g0 = s * cz - COARSE_HALO
    gidx = g0 + jnp.arange(n_ext, dtype=jnp.int32)
    lo_plane = lax.dynamic_index_in_dim(ext, jnp.maximum(-g0, 0), 0, keepdims=True)
    hi_plane = lax.dynamic_index_in_dim(ext, jnp.minimum(coarse_total - 1 - g0, n_ext - 1), 0, keepdims=True)
    ext = jnp.where((gidx < 0)[:, None, None], lo_plane, ext)
    ext = jnp.where((gidx >= coarse_total)[:, None, None], hi_plane, ext)

    pro = along_x(ext, prolong_matrix(cx).astype(jnp.bfloat16), precision=lax.Precision.DEFAULT)
    pro = along_y(pro, prolong_matrix(cy))
    inner = pro[1:-1]
    even = 0.75 * inner + 0.25 * pro[:-2]
    odd = 0.75 * inner + 0.25 * pro[2:]
    log_perm = jnp.stack((even, odd), axis=1).reshape(2 * (n_ext - 2), fy, fx)
    k0_first = 2 * (g0 + 1)
    k0_planes = log_perm.shape[0]

    positions = k0_first + jnp.arange(k0_planes, dtype=jnp.int32)
    depth_table = mode_table(MZ, fine_total, positions)
    rows_table = mode_table(MY, fy, jnp.arange(fy, dtype=jnp.int32))
    cols_table = mode_table(MX, fx, jnp.arange(fx, dtype=jnp.int32))
    along_depth = jnp.einsum("abe,az->zbe", kl_coeffs[0], depth_table, precision=HI)
    along_rows = jnp.einsum("zbe,by->zye", along_depth, rows_table, precision=HI)
    kl = jnp.dot(along_rows.reshape(k0_planes * fy, MX), cols_table,
                 precision=HI).reshape(k0_planes, fy, fx)
    kl = lax.optimization_barrier(kl)
    k0 = jnp.exp(log_perm + kl)
    k0 = jnp.where(plane_mask(k0_first, k0_planes, fine_total), k0, 0.0)
    k0_halo = (k0_planes - fz) // 2

    k1 = 0.125 * restrict_sum(k0)
    k1_halo = k0_halo // 2
    own1 = fz // 2
    k2_own = 0.125 * restrict_sum(k1[k1_halo:k1_halo + own1])

    h0k = F0_HALO + 1
    lvl0 = Level(k0[k0_halo - h0k: k0_halo + fz + h0k], h0k, fz, s * fz - h0k, fine_total)
    f0 = jnp.concatenate([got_l[crow:].reshape(F0_HALO, fy, fx), source,
                          got_r[crow:].reshape(F0_HALO, fy, fx)], axis=0)
    u = lvl0.start(f0, F0_HALO)
    u1 = lvl0.sweep(u, lvl0.cut(f0, F0_HALO - 1, F0_HALO), F0_HALO)
    res0 = f0[F0_HALO:F0_HALO + fz] - lvl0.operate(u1[1:-1], 1)
    f1_own = 0.5 * restrict_sum(res0)

    h1k = F1_HALO + 1
    extra = h1k - k1_halo
    from_left = shift_from(jnp.concatenate([k1[own1 - extra: own1], f1_own]), 1)
    from_right = shift_from(jnp.concatenate([f1_own, k1[2 * k1_halo: 2 * k1_halo + extra]]), -1)
    k1_ext = jnp.concatenate([from_left[:extra], k1, from_right[own1:]], axis=0)
    f1 = jnp.concatenate([from_left[extra:], f1_own, from_right[:own1]], axis=0)
    lvl1 = Level(k1_ext, h1k, own1, s * own1 - h1k, fine_total // 2)
    v = lvl1.start(f1, F1_HALO)
    v1 = lvl1.sweep(v, lvl1.cut(f1, F1_HALO - 1, F1_HALO), F1_HALO)
    res1 = f1_own - lvl1.operate(v1[2:-2], 1)
    both = gather_window(jnp.stack([0.5 * restrict_sum(res1), k2_own]))

    own2 = own1 // 2
    total2 = fine_total // 4
    k2_halo = 13
    f2_halo = k2_halo - 1
    reach = (both.shape[0] // 2) * own2
    f2w = both[:, 0].reshape((-1,) + both.shape[3:])[reach - f2_halo: reach + own2 + f2_halo]
    k2w = both[:, 1].reshape((-1,) + both.shape[3:])[reach - k2_halo: reach + own2 + k2_halo]
    lvl2 = Level(k2w, k2_halo, own2, s * own2 - k2_halo, total2)
    w = lvl2.start(f2w, f2_halo)
    w1 = lvl2.sweep(w, lvl2.cut(f2w, f2_halo - 1, f2_halo), f2_halo)
    res2 = lvl2.cut(f2w, f2_halo - 2, f2_halo) - lvl2.operate(w1, f2_halo - 1)
    f3 = 0.5 * restrict_sum(res2)
    f3_halo = (f2_halo - 2) // 2
    k3 = 0.125 * restrict_sum(k2w[1:-1])
    lvl3 = Level(k3, f3_halo + 1, own2 // 2, s * (own2 // 2) - f3_halo - 1, total2 // 2)
    b = lvl3.start(f3, f3_halo)
    for step in range(BOTTOM - 1):
        h = f3_halo - step
        b = lvl3.sweep(b, lvl3.cut(f3, h - 1, f3_halo), h)
    e3_halo = f3_halo - (BOTTOM - 1)
    cut2 = (f2_halo - 1) - 2 * e3_halo
    w = w1[cut2:w1.shape[0] - cut2] + copy_up(b)
    h = 2 * e3_halo
    for _ in range(SWEEPS):
        w = lvl2.sweep(w, lvl2.cut(f2w, h - 1, f2_halo), h)
        h -= 1
    e2 = w

    v = v1 + copy_up(e2)[1:-1]
    v = lvl1.sweep(v, lvl1.cut(f1, 2, F1_HALO), 3)
    e1 = lvl1.sweep(v, lvl1.cut(f1, 1, F1_HALO), 2)

    u = u1 + copy_up(e1)
    u = lvl0.sweep(u, lvl0.cut(f0, 1, F0_HALO), 2)
    u = lvl0.sweep(u, source, 1)
    return u[None]


def solution(mesh):
    return jax.shard_map(
        on_device,
        mesh=mesh,
        in_specs=(
            P("chain", None, "slab", None, None),
            P("chain", None),
            P(),
            P("chain", None, None, None),
            P("slab", None, None),
        ),
        out_specs=P("chain", "slab", None, None),
        check_vma=False,
    )
```

```python
import numpy as np
import jax
import jax.numpy as jnp
from jax import lax
from jax.sharding import PartitionSpec as P

STEPS = 4
MZ = 32
MY = 16
MX = 64
LEVELS = 4
SWEEPS = 2
BOTTOM = 4

OMEGA = 0.8
HI = lax.Precision.HIGHEST

F0_HALO = 3
F1_HALO = 4
COARSE_HALO = 4


def pair_sum_matrix(n):
    m = np.zeros((n, n // 2), np.float32)
    m[np.arange(n), np.arange(n) // 2] = 1.0
    return m


def repeat_matrix(n):
    return np.ascontiguousarray(pair_sum_matrix(2 * n).T)


def prolong_matrix(n):
    m = np.zeros((n, 2 * n), np.float32)
    for i in range(n):
        m[i, 2 * i] += 0.75
        m[max(i - 1, 0), 2 * i] += 0.25
        m[i, 2 * i + 1] += 0.75
        m[min(i + 1, n - 1), 2 * i + 1] += 0.25
    return m


def along_x(values, matrix, precision=HI):
    return jnp.einsum("zyx,xw->zyw", values, jnp.asarray(matrix), precision=precision,
                      preferred_element_type=jnp.float32)


def along_y(values, matrix, precision=HI):
    return jnp.einsum("zyx,yv->zvx", values, jnp.asarray(matrix), precision=precision,
                      preferred_element_type=jnp.float32)


def restrict_sum(values):
    nz, ny, nx = values.shape
    values = values.reshape(nz // 2, 2, ny, nx).sum(axis=1)
    values = along_y(values, pair_sum_matrix(ny))
    return along_x(values, pair_sum_matrix(nx))


def copy_up(values):
    nz, ny, nx = values.shape
    values = along_x(values, repeat_matrix(nx))
    values = along_y(values, repeat_matrix(ny))
    return jnp.repeat(values, 2, axis=0)


def shift_from(block, offset):
    count = lax.axis_size("slab")
    pairs = [(i, i + offset) for i in range(count) if 0 <= i + offset < count]
    return lax.ppermute(block, "slab", pairs)


def gather_window(block):
    got = jnp.concatenate([shift_from(block[None], 1), block[None], shift_from(block[None], -1)])
    got = jnp.concatenate([shift_from(got[:2], 2), got, shift_from(got[1:], -2)])
    return jnp.concatenate([shift_from(got[:4], 4), got, shift_from(got[3:], -4)])


def plane_mask(first_global, planes, total):
    g = first_global + jnp.arange(planes, dtype=jnp.int32)
    return ((g >= 0) & (g < total))[:, None, None]


class Level:
    def __init__(self, k, k_halo, own, first_global, total):
        self.own = own
        self.halo = k_halo - 1
        self.first = first_global + 1
        self.total = total
        faces_z = 0.5 * (k[1:] + k[:-1])
        kc = k[1:-1]
        rows = jnp.pad(kc, ((0, 0), (1, 1), (0, 0)))
        self.fy = 0.5 * (rows[:, 1:] + rows[:, :-1])
        cols = jnp.pad(kc, ((0, 0), (0, 0), (1, 1)))
        self.fx = 0.5 * (cols[:, :, 1:] + cols[:, :, :-1])
        self.fzl = faces_z[:-1]
        self.fzu = faces_z[1:]
        diag = self.fzl + self.fzu + self.fy[:, 1:] + self.fy[:, :-1]
        self.diag = diag + self.fx[:, :, 1:] + self.fx[:, :, :-1]

    def cut(self, arr, h, have):
        n = self.own + 2 * h
        return arr[have - h: have - h + n]

    def coef(self, h):
        c = self.cut
        H = self.halo
        return c(self.fzl, h, H), c(self.fzu, h, H), c(self.fy, h, H), c(self.fx, h, H), c(self.diag, h, H)

    def mask(self, u, h):
        return jnp.where(plane_mask(self.first + self.halo - h, u.shape[0], self.total), u, 0.0)

    def operate(self, u, h):
        fzl, fzu, fy, fx, diag = self.coef(h - 1)
        uc = u[1:-1]
        rows = jnp.pad(uc, ((0, 0), (1, 1), (0, 0)))
        cols = jnp.pad(uc, ((0, 0), (0, 0), (1, 1)))
        nb = fzu * u[2:] + fzl * u[:-2]
        nb = nb + fy[:, 1:] * rows[:, 2:] + fy[:, :-1] * rows[:, :-2]
        nb = nb + fx[:, :, 1:] * cols[:, :, 2:] + fx[:, :, :-1] * cols[:, :, :-2]
        return diag * uc - nb

    def sweep(self, u, f, h):
        diag = self.coef(h - 1)[4]
        new = u[1:-1] + OMEGA * (f - self.operate(u, h)) / diag
        return self.mask(new, h - 1)

    def start(self, f, h):
        return self.mask(OMEGA * f / self.coef(h)[4], h)


def mode_table(mode_count, length, positions):
    frequency = length // 2 + jnp.arange(mode_count, dtype=jnp.int32)
    phases = frequency[:, None] * (2 * positions[None, :] + 1) % (4 * length)
    return jnp.cos(jnp.pi * phases.astype(jnp.float32) / (2 * length))


def on_device(coarse_states, accept_flags, owners, kl_coeffs, source):
    slabs = lax.axis_size("slab")
    chain_index = lax.axis_index("chain")
    s = lax.axis_index("slab")
    step_numbers = jnp.arange(1, STEPS, dtype=jnp.int32)
    chosen = jnp.max(jnp.where(accept_flags == 1, step_numbers[None, :], 0), axis=1)
    local_count = coarse_states.shape[0]
    def local_state(owner):
        pick = owner % local_count
        return coarse_states[pick, chosen[pick]]

    other = owners[1 - chain_index]
    sent = lax.ppermute(local_state(other), "chain", [(0, 1), (1, 0)])
    target = owners[chain_index]
    own = jnp.where(target // local_count == chain_index, local_state(target), sent)

    cz, cy, cx = own.shape
    fz = source.shape[0]
    fy, fx = 2 * cy, 2 * cx
    coarse_total = cz * slabs
    fine_total = fz * slabs

    crow = cz * cy * cx // fx

    def pack(source_part):
        return jnp.concatenate([own.astype(jnp.float32).reshape(crow, fx),
                                source_part.reshape(-1, fx)], axis=0)

    got_l = shift_from(pack(source[fz - F0_HALO:]), 1)
    got_r = shift_from(pack(source[:F0_HALO]), -1)
    coarse_l = got_l[:crow].reshape(cz, cy, cx).astype(own.dtype)
    coarse_r = got_r[:crow].reshape(cz, cy, cx).astype(own.dtype)
    ext = jnp.concatenate([coarse_l, own, coarse_r], axis=0)
    n_ext = ext.shape[0]
    g0 = s * cz - COARSE_HALO
    gidx = g0 + jnp.arange(n_ext, dtype=jnp.int32)
    lo_plane = lax.dynamic_index_in_dim(ext, jnp.maximum(-g0, 0), 0, keepdims=True)
    hi_plane = lax.dynamic_index_in_dim(ext, jnp.minimum(coarse_total - 1 - g0, n_ext - 1), 0, keepdims=True)
    ext = jnp.where((gidx < 0)[:, None, None], lo_plane, ext)
    ext = jnp.where((gidx >= coarse_total)[:, None, None], hi_plane, ext)

    pro = along_x(ext, prolong_matrix(cx).astype(jnp.bfloat16), precision=lax.Precision.DEFAULT)
    pro = along_y(pro, prolong_matrix(cy))
    inner = pro[1:-1]
    even = 0.75 * inner + 0.25 * pro[:-2]
    odd = 0.75 * inner + 0.25 * pro[2:]
    log_perm = jnp.stack((even, odd), axis=1).reshape(2 * (n_ext - 2), fy, fx)
    k0_first = 2 * (g0 + 1)
    k0_planes = log_perm.shape[0]

    positions = k0_first + jnp.arange(k0_planes, dtype=jnp.int32)
    depth_table = mode_table(MZ, fine_total, positions)
    rows_table = mode_table(MY, fy, jnp.arange(fy, dtype=jnp.int32))
    cols_table = mode_table(MX, fx, jnp.arange(fx, dtype=jnp.int32))
    along_depth = jnp.einsum("abe,az->zbe", kl_coeffs[0], depth_table, precision=HI)
    along_rows = jnp.einsum("zbe,by->zye", along_depth, rows_table, precision=HI)
    kl = jnp.dot(along_rows.reshape(k0_planes * fy, MX), cols_table,
                 precision=HI).reshape(k0_planes, fy, fx)
    k0 = jnp.exp(log_perm + kl)
    k0 = jnp.where(plane_mask(k0_first, k0_planes, fine_total), k0, 0.0)
    k0_halo = (k0_planes - fz) // 2

    k1 = 0.125 * restrict_sum(k0)
    k1_halo = k0_halo // 2
    own1 = fz // 2
    k2_own = 0.125 * restrict_sum(k1[k1_halo:k1_halo + own1])

    h0k = F0_HALO + 1
    lvl0 = Level(k0[k0_halo - h0k: k0_halo + fz + h0k], h0k, fz, s * fz - h0k, fine_total)
    f0 = jnp.concatenate([got_l[crow:].reshape(F0_HALO, fy, fx), source,
                          got_r[crow:].reshape(F0_HALO, fy, fx)], axis=0)
    u = lvl0.start(f0, F0_HALO)
    u1 = lvl0.sweep(u, lvl0.cut(f0, F0_HALO - 1, F0_HALO), F0_HALO)
    res0 = f0[F0_HALO:F0_HALO + fz] - lvl0.operate(u1[1:-1], 1)
    f1_own = 0.5 * restrict_sum(res0)

    h1k = F1_HALO + 1
    extra = h1k - k1_halo
    from_left = shift_from(jnp.concatenate([k1[own1 - extra: own1], f1_own]), 1)
    from_right = shift_from(jnp.concatenate([f1_own, k1[2 * k1_halo: 2 * k1_halo + extra]]), -1)
    k1_ext = jnp.concatenate([from_left[:extra], k1, from_right[own1:]], axis=0)
    f1 = jnp.concatenate([from_left[extra:], f1_own, from_right[:own1]], axis=0)
    lvl1 = Level(k1_ext, h1k, own1, s * own1 - h1k, fine_total // 2)
    v = lvl1.start(f1, F1_HALO)
    v1 = lvl1.sweep(v, lvl1.cut(f1, F1_HALO - 1, F1_HALO), F1_HALO)
    res1 = f1_own - lvl1.operate(v1[2:-2], 1)
    both = gather_window(jnp.stack([0.5 * restrict_sum(res1), k2_own]))

    own2 = own1 // 2
    total2 = fine_total // 4
    k2_halo = 13
    f2_halo = k2_halo - 1
    reach = (both.shape[0] // 2) * own2
    f2w = both[:, 0].reshape((-1,) + both.shape[3:])[reach - f2_halo: reach + own2 + f2_halo]
    k2w = both[:, 1].reshape((-1,) + both.shape[3:])[reach - k2_halo: reach + own2 + k2_halo]
    lvl2 = Level(k2w, k2_halo, own2, s * own2 - k2_halo, total2)
    w = lvl2.start(f2w, f2_halo)
    w1 = lvl2.sweep(w, lvl2.cut(f2w, f2_halo - 1, f2_halo), f2_halo)
    res2 = lvl2.cut(f2w, f2_halo - 2, f2_halo) - lvl2.operate(w1, f2_halo - 1)
    f3 = 0.5 * restrict_sum(res2)
    f3_halo = (f2_halo - 2) // 2
    k3 = 0.125 * restrict_sum(k2w[1:-1])
    lvl3 = Level(k3, f3_halo + 1, own2 // 2, s * (own2 // 2) - f3_halo - 1, total2 // 2)
    b = lvl3.start(f3, f3_halo)
    for step in range(BOTTOM - 1):
        h = f3_halo - step
        b = lvl3.sweep(b, lvl3.cut(f3, h - 1, f3_halo), h)
    e3_halo = f3_halo - (BOTTOM - 1)
    cut2 = (f2_halo - 1) - 2 * e3_halo
    w = w1[cut2:w1.shape[0] - cut2] + copy_up(b)
    h = 2 * e3_halo
    for _ in range(SWEEPS):
        w = lvl2.sweep(w, lvl2.cut(f2w, h - 1, f2_halo), h)
        h -= 1
    e2 = w

    v = v1 + copy_up(e2)[1:-1]
    v = lvl1.sweep(v, lvl1.cut(f1, 2, F1_HALO), 3)
    e1 = lvl1.sweep(v, lvl1.cut(f1, 1, F1_HALO), 2)

    u = u1 + copy_up(e1)
    u = lvl0.sweep(u, lvl0.cut(f0, 1, F0_HALO), 2)
    u = lvl0.sweep(u, source, 1)
    return u[None]


def solution(mesh):
    return jax.shard_map(
        on_device,
        mesh=mesh,
        in_specs=(
            P("chain", None, "slab", None, None),
            P("chain", None),
            P(),
            P("chain", None, None, None),
            P("slab", None, None),
        ),
        out_specs=P("chain", "slab", None, None),
        check_vma=False,
    )
```

```python
import numpy as np
import jax
import jax.numpy as jnp
from jax import lax
from jax.sharding import PartitionSpec as P

STEPS = 4
MZ = 32
MY = 16
MX = 64
LEVELS = 4
SWEEPS = 2
BOTTOM = 4

OMEGA = 0.8
HI = lax.Precision.HIGHEST

F0_HALO = 3
F1_HALO = 4
COARSE_HALO = 4


def pair_sum_matrix(n):
    m = np.zeros((n, n // 2), np.float32)
    m[np.arange(n), np.arange(n) // 2] = 1.0
    return m


def repeat_matrix(n):
    return np.ascontiguousarray(pair_sum_matrix(2 * n).T)


def prolong_matrix(n):
    m = np.zeros((n, 2 * n), np.float32)
    for i in range(n):
        m[i, 2 * i] += 0.75
        m[max(i - 1, 0), 2 * i] += 0.25
        m[i, 2 * i + 1] += 0.75
        m[min(i + 1, n - 1), 2 * i + 1] += 0.25
    return m


def along_x(values, matrix, precision=HI):
    return jnp.einsum("zyx,xw->zyw", values, jnp.asarray(matrix), precision=precision,
                      preferred_element_type=jnp.float32)


def along_y(values, matrix, precision=HI):
    return jnp.einsum("zyx,yv->zvx", values, jnp.asarray(matrix), precision=precision,
                      preferred_element_type=jnp.float32)


def restrict_sum(values):
    nz, ny, nx = values.shape
    values = values.reshape(nz // 2, 2, ny, nx).sum(axis=1)
    values = along_y(values, pair_sum_matrix(ny))
    return along_x(values, pair_sum_matrix(nx))


def copy_up(values):
    nz, ny, nx = values.shape
    values = along_x(values, repeat_matrix(nx))
    values = along_y(values, repeat_matrix(ny))
    return jnp.repeat(values, 2, axis=0)


def shift_from(block, offset):
    count = lax.axis_size("slab")
    pairs = [(i, i + offset) for i in range(count) if 0 <= i + offset < count]
    return lax.ppermute(block, "slab", pairs)


def gather_window(block):
    got = jnp.concatenate([shift_from(block[None], 1), block[None], shift_from(block[None], -1)])
    got = jnp.concatenate([shift_from(got[:2], 2), got, shift_from(got[1:], -2)])
    return jnp.concatenate([shift_from(got[:4], 4), got, shift_from(got[3:], -4)])


def plane_mask(first_global, planes, total):
    g = first_global + jnp.arange(planes, dtype=jnp.int32)
    return ((g >= 0) & (g < total))[:, None, None]


class Level:
    def __init__(self, k, k_halo, own, first_global, total):
        self.own = own
        self.halo = k_halo - 1
        self.first = first_global + 1
        self.total = total
        faces_z = 0.5 * (k[1:] + k[:-1])
        kc = k[1:-1]
        rows = jnp.pad(kc, ((0, 0), (1, 1), (0, 0)))
        self.fy = 0.5 * (rows[:, 1:] + rows[:, :-1])
        cols = jnp.pad(kc, ((0, 0), (0, 0), (1, 1)))
        self.fx = 0.5 * (cols[:, :, 1:] + cols[:, :, :-1])
        self.fzl = faces_z[:-1]
        self.fzu = faces_z[1:]
        diag = self.fzl + self.fzu + self.fy[:, 1:] + self.fy[:, :-1]
        self.diag = diag + self.fx[:, :, 1:] + self.fx[:, :, :-1]
        self.valid = plane_mask(self.first, kc.shape[0], total)

    def cut(self, arr, h, have):
        n = self.own + 2 * h
        return arr[have - h: have - h + n]

    def coef(self, h):
        c = self.cut
        H = self.halo
        return c(self.fzl, h, H), c(self.fzu, h, H), c(self.fy, h, H), c(self.fx, h, H), c(self.diag, h, H)

    def mask(self, u, h):
        return jnp.where(self.cut(self.valid, h, self.halo), u, 0.0)

    def operate(self, u, h):
        fzl, fzu, fy, fx, diag = self.coef(h - 1)
        uc = u[1:-1]
        rows = jnp.pad(uc, ((0, 0), (1, 1), (0, 0)))
        cols = jnp.pad(uc, ((0, 0), (0, 0), (1, 1)))
        nb = fzu * u[2:] + fzl * u[:-2]
        nb = nb + fy[:, 1:] * rows[:, 2:] + fy[:, :-1] * rows[:, :-2]
        nb = nb + fx[:, :, 1:] * cols[:, :, 2:] + fx[:, :, :-1] * cols[:, :, :-2]
        return diag * uc - nb

    def sweep(self, u, f, h):
        diag = self.coef(h - 1)[4]
        new = u[1:-1] + OMEGA * (f - self.operate(u, h)) / diag
        return self.mask(new, h - 1)

    def start(self, f, h):
        return self.mask(OMEGA * f / self.coef(h)[4], h)


def mode_table(mode_count, length, positions):
    frequency = length // 2 + jnp.arange(mode_count, dtype=jnp.int32)
    phases = frequency[:, None] * (2 * positions[None, :] + 1) % (4 * length)
    return jnp.cos(jnp.pi * phases.astype(jnp.float32) / (2 * length))


def on_device(coarse_states, accept_flags, owners, kl_coeffs, source):
    slabs = lax.axis_size("slab")
    chain_index = lax.axis_index("chain")
    s = lax.axis_index("slab")
    step_numbers = jnp.arange(1, STEPS, dtype=jnp.int32)
    chosen = jnp.max(jnp.where(accept_flags == 1, step_numbers[None, :], 0), axis=1)
    local_count = coarse_states.shape[0]
    accepted = coarse_states[jnp.arange(local_count, dtype=jnp.int32), chosen]
    every_field = lax.all_gather(accepted, "chain", axis=0, tiled=True)
    own = lax.dynamic_index_in_dim(every_field, owners[chain_index], 0, keepdims=False)

    cz, cy, cx = own.shape
    fz = source.shape[0]
    fy, fx = 2 * cy, 2 * cx
    coarse_total = cz * slabs
    fine_total = fz * slabs

    crow = cz * cy * cx // fx

    def pack(source_part):
        return jnp.concatenate([own.astype(jnp.float32).reshape(crow, fx),
                                source_part.reshape(-1, fx)], axis=0)

    got_l = shift_from(pack(source[fz - F0_HALO:]), 1)
    got_r = shift_from(pack(source[:F0_HALO]), -1)
    coarse_l = got_l[:crow].reshape(cz, cy, cx).astype(own.dtype)
    coarse_r = got_r[:crow].reshape(cz, cy, cx).astype(own.dtype)
    ext = jnp.concatenate([coarse_l, own, coarse_r], axis=0)
    n_ext = ext.shape[0]
    g0 = s * cz - COARSE_HALO
    gidx = g0 + jnp.arange(n_ext, dtype=jnp.int32)
    lo_plane = lax.dynamic_index_in_dim(ext, jnp.maximum(-g0, 0), 0, keepdims=True)
    hi_plane = lax.dynamic_index_in_dim(ext, jnp.minimum(coarse_total - 1 - g0, n_ext - 1), 0, keepdims=True)
    ext = jnp.where((gidx < 0)[:, None, None], lo_plane, ext)
    ext = jnp.where((gidx >= coarse_total)[:, None, None], hi_plane, ext)

    pro = along_x(ext, prolong_matrix(cx).astype(jnp.bfloat16), precision=lax.Precision.DEFAULT)
    pro = along_y(pro, prolong_matrix(cy))
    inner = pro[1:-1]
    even = 0.75 * inner + 0.25 * pro[:-2]
    odd = 0.75 * inner + 0.25 * pro[2:]
    log_perm = jnp.stack((even, odd), axis=1).reshape(2 * (n_ext - 2), fy, fx)
    k0_first = 2 * (g0 + 1)
    k0_planes = log_perm.shape[0]

    positions = k0_first + jnp.arange(k0_planes, dtype=jnp.int32)
    depth_table = mode_table(MZ, fine_total, positions)
    rows_table = mode_table(MY, fy, jnp.arange(fy, dtype=jnp.int32))
    cols_table = mode_table(MX, fx, jnp.arange(fx, dtype=jnp.int32))
    along_depth = jnp.einsum("abe,az->zbe", kl_coeffs[0], depth_table, precision=HI)
    along_rows = jnp.einsum("zbe,by->zye", along_depth, rows_table, precision=HI)
    kl = jnp.dot(along_rows.reshape(k0_planes * fy, MX), cols_table,
                 precision=HI).reshape(k0_planes, fy, fx)
    k0 = jnp.exp(log_perm + kl)
    k0 = jnp.where(plane_mask(k0_first, k0_planes, fine_total), k0, 0.0)
    k0_halo = (k0_planes - fz) // 2

    k1 = 0.125 * restrict_sum(k0)
    k1_halo = k0_halo // 2
    own1 = fz // 2
    k2_own = 0.125 * restrict_sum(k1[k1_halo:k1_halo + own1])

    h0k = F0_HALO + 1
    lvl0 = Level(k0[k0_halo - h0k: k0_halo + fz + h0k], h0k, fz, s * fz - h0k, fine_total)
    f0 = jnp.concatenate([got_l[crow:].reshape(F0_HALO, fy, fx), source,
                          got_r[crow:].reshape(F0_HALO, fy, fx)], axis=0)
    u = lvl0.start(f0, F0_HALO)
    u1 = lvl0.sweep(u, lvl0.cut(f0, F0_HALO - 1, F0_HALO), F0_HALO)
    res0 = f0[F0_HALO:F0_HALO + fz] - lvl0.operate(u1[1:-1], 1)
    f1_own = 0.5 * restrict_sum(res0)

    h1k = F1_HALO + 1
    extra = h1k - k1_halo
    from_left = shift_from(jnp.concatenate([k1[own1 - extra: own1], f1_own]), 1)
    from_right = shift_from(jnp.concatenate([f1_own, k1[2 * k1_halo: 2 * k1_halo + extra]]), -1)
    k1_ext = jnp.concatenate([from_left[:extra], k1, from_right[own1:]], axis=0)
    f1 = jnp.concatenate([from_left[extra:], f1_own, from_right[:own1]], axis=0)
    lvl1 = Level(k1_ext, h1k, own1, s * own1 - h1k, fine_total // 2)
    v = lvl1.start(f1, F1_HALO)
    v1 = lvl1.sweep(v, lvl1.cut(f1, F1_HALO - 1, F1_HALO), F1_HALO)
    res1 = f1_own - lvl1.operate(v1[2:-2], 1)
    both = gather_window(jnp.stack([0.5 * restrict_sum(res1), k2_own]))

    own2 = own1 // 2
    total2 = fine_total // 4
    k2_halo = 13
    f2_halo = k2_halo - 1
    reach = (both.shape[0] // 2) * own2
    f2w = both[:, 0].reshape((-1,) + both.shape[3:])[reach - f2_halo: reach + own2 + f2_halo]
    k2w = both[:, 1].reshape((-1,) + both.shape[3:])[reach - k2_halo: reach + own2 + k2_halo]
    lvl2 = Level(k2w, k2_halo, own2, s * own2 - k2_halo, total2)
    w = lvl2.start(f2w, f2_halo)
    w1 = lvl2.sweep(w, lvl2.cut(f2w, f2_halo - 1, f2_halo), f2_halo)
    res2 = lvl2.cut(f2w, f2_halo - 2, f2_halo) - lvl2.operate(w1, f2_halo - 1)
    f3 = 0.5 * restrict_sum(res2)
    f3_halo = (f2_halo - 2) // 2
    k3 = 0.125 * restrict_sum(k2w[1:-1])
    lvl3 = Level(k3, f3_halo + 1, own2 // 2, s * (own2 // 2) - f3_halo - 1, total2 // 2)
    b = lvl3.start(f3, f3_halo)
    for step in range(BOTTOM - 1):
        h = f3_halo - step
        b = lvl3.sweep(b, lvl3.cut(f3, h - 1, f3_halo), h)
    e3_halo = f3_halo - (BOTTOM - 1)
    cut2 = (f2_halo - 1) - 2 * e3_halo
    w = w1[cut2:w1.shape[0] - cut2] + copy_up(b)
    h = 2 * e3_halo
    for _ in range(SWEEPS):
        w = lvl2.sweep(w, lvl2.cut(f2w, h - 1, f2_halo), h)
        h -= 1
    e2 = w

    v = v1 + copy_up(e2)[1:-1]
    v = lvl1.sweep(v, lvl1.cut(f1, 2, F1_HALO), 3)
    e1 = lvl1.sweep(v, lvl1.cut(f1, 1, F1_HALO), 2)

    u = u1 + copy_up(e1)
    u = lvl0.sweep(u, lvl0.cut(f0, 1, F0_HALO), 2)
    u = lvl0.sweep(u, source, 1)
    return u[None]


def solution(mesh):
    return jax.shard_map(
        on_device,
        mesh=mesh,
        in_specs=(
            P("chain", None, "slab", None, None),
            P("chain", None),
            P(),
            P("chain", None, None, None),
            P("slab", None, None),
        ),
        out_specs=P("chain", "slab", None, None),
        check_vma=False,
    )
```

```python
import numpy as np
import jax
import jax.numpy as jnp
from jax import lax
from jax.sharding import PartitionSpec as P

STEPS = 4
MZ = 32
MY = 16
MX = 64
LEVELS = 4
SWEEPS = 2
BOTTOM = 4

OMEGA = 0.8
HI = lax.Precision.HIGHEST
GRID = lax.Precision.HIGH

F0_HALO = 3
F1_HALO = 4
COARSE_HALO = 4


def pair_sum_matrix(n):
    m = np.zeros((n, n // 2), np.float32)
    m[np.arange(n), np.arange(n) // 2] = 1.0
    return m


def repeat_matrix(n):
    return np.ascontiguousarray(pair_sum_matrix(2 * n).T)


def prolong_matrix(n):
    m = np.zeros((n, 2 * n), np.float32)
    for i in range(n):
        m[i, 2 * i] += 0.75
        m[max(i - 1, 0), 2 * i] += 0.25
        m[i, 2 * i + 1] += 0.75
        m[min(i + 1, n - 1), 2 * i + 1] += 0.25
    return m


def along_x(values, matrix, precision=HI):
    return jnp.einsum("zyx,xw->zyw", values, jnp.asarray(matrix), precision=precision,
                      preferred_element_type=jnp.float32)


def along_y(values, matrix, precision=HI):
    return jnp.einsum("zyx,yv->zvx", values, jnp.asarray(matrix), precision=precision,
                      preferred_element_type=jnp.float32)


def restrict_sum(values):
    nz, ny, nx = values.shape
    values = values.reshape(nz // 2, 2, ny, nx).sum(axis=1)
    values = along_y(values, pair_sum_matrix(ny), GRID)
    return along_x(values, pair_sum_matrix(nx), GRID)


def copy_up(values):
    nz, ny, nx = values.shape
    values = along_x(values, repeat_matrix(nx), GRID)
    values = along_y(values, repeat_matrix(ny), GRID)
    return jnp.repeat(values, 2, axis=0)


def shift_from(block, offset):
    count = lax.axis_size("slab")
    pairs = [(i, i + offset) for i in range(count) if 0 <= i + offset < count]
    return lax.ppermute(block, "slab", pairs)


def gather_window(block):
    got = jnp.concatenate([shift_from(block[None], 1), block[None], shift_from(block[None], -1)])
    got = jnp.concatenate([shift_from(got[:2], 2), got, shift_from(got[1:], -2)])
    return jnp.concatenate([shift_from(got[:4], 4), got, shift_from(got[3:], -4)])


def plane_mask(first_global, planes, total):
    g = first_global + jnp.arange(planes, dtype=jnp.int32)
    return ((g >= 0) & (g < total))[:, None, None]


class Level:
    def __init__(self, k, k_halo, own, first_global, total):
        self.own = own
        self.halo = k_halo - 1
        self.first = first_global + 1
        self.total = total
        faces_z = 0.5 * (k[1:] + k[:-1])
        kc = k[1:-1]
        rows = jnp.pad(kc, ((0, 0), (1, 1), (0, 0)))
        self.fy = 0.5 * (rows[:, 1:] + rows[:, :-1])
        cols = jnp.pad(kc, ((0, 0), (0, 0), (1, 1)))
        self.fx = 0.5 * (cols[:, :, 1:] + cols[:, :, :-1])
        self.fzl = faces_z[:-1]
        self.fzu = faces_z[1:]
        diag = self.fzl + self.fzu + self.fy[:, 1:] + self.fy[:, :-1]
        self.diag = diag + self.fx[:, :, 1:] + self.fx[:, :, :-1]

    def cut(self, arr, h, have):
        n = self.own + 2 * h
        return arr[have - h: have - h + n]

    def coef(self, h):
        c = self.cut
        H = self.halo
        return c(self.fzl, h, H), c(self.fzu, h, H), c(self.fy, h, H), c(self.fx, h, H), c(self.diag, h, H)

    def mask(self, u, h):
        return jnp.where(plane_mask(self.first + self.halo - h, u.shape[0], self.total), u, 0.0)

    def operate(self, u, h):
        fzl, fzu, fy, fx, diag = self.coef(h - 1)
        uc = u[1:-1]
        rows = jnp.pad(uc, ((0, 0), (1, 1), (0, 0)))
        cols = jnp.pad(uc, ((0, 0), (0, 0), (1, 1)))
        nb = fzu * u[2:] + fzl * u[:-2]
        nb = nb + fy[:, 1:] * rows[:, 2:] + fy[:, :-1] * rows[:, :-2]
        nb = nb + fx[:, :, 1:] * cols[:, :, 2:] + fx[:, :, :-1] * cols[:, :, :-2]
        return diag * uc - nb

    def sweep(self, u, f, h):
        diag = self.coef(h - 1)[4]
        new = u[1:-1] + OMEGA * (f - self.operate(u, h)) / diag
        return self.mask(new, h - 1)

    def start(self, f, h):
        return self.mask(OMEGA * f / self.coef(h)[4], h)


def mode_table(mode_count, length, positions):
    frequency = length // 2 + jnp.arange(mode_count, dtype=jnp.int32)
    phases = frequency[:, None] * (2 * positions[None, :] + 1) % (4 * length)
    return jnp.cos(jnp.pi * phases.astype(jnp.float32) / (2 * length))


def on_device(coarse_states, accept_flags, owners, kl_coeffs, source):
    slabs = lax.axis_size("slab")
    chain_index = lax.axis_index("chain")
    s = lax.axis_index("slab")
    step_numbers = jnp.arange(1, STEPS, dtype=jnp.int32)
    chosen = jnp.max(jnp.where(accept_flags == 1, step_numbers[None, :], 0), axis=1)
    local_count = coarse_states.shape[0]
    accepted = coarse_states[jnp.arange(local_count, dtype=jnp.int32), chosen]
    every_field = lax.all_gather(accepted, "chain", axis=0, tiled=True)
    own = lax.dynamic_index_in_dim(every_field, owners[chain_index], 0, keepdims=False)

    cz, cy, cx = own.shape
    fz = source.shape[0]
    fy, fx = 2 * cy, 2 * cx
    coarse_total = cz * slabs
    fine_total = fz * slabs

    crow = cz * cy * cx // fx

    def pack(source_part):
        return jnp.concatenate([own.astype(jnp.float32).reshape(crow, fx),
                                source_part.reshape(-1, fx)], axis=0)

    got_l = shift_from(pack(source[fz - F0_HALO:]), 1)
    got_r = shift_from(pack(source[:F0_HALO]), -1)
    coarse_l = got_l[:crow].reshape(cz, cy, cx).astype(own.dtype)
    coarse_r = got_r[:crow].reshape(cz, cy, cx).astype(own.dtype)
    ext = jnp.concatenate([coarse_l, own, coarse_r], axis=0)
    n_ext = ext.shape[0]
    g0 = s * cz - COARSE_HALO
    gidx = g0 + jnp.arange(n_ext, dtype=jnp.int32)
    lo_plane = lax.dynamic_index_in_dim(ext, jnp.maximum(-g0, 0), 0, keepdims=True)
    hi_plane = lax.dynamic_index_in_dim(ext, jnp.minimum(coarse_total - 1 - g0, n_ext - 1), 0, keepdims=True)
    ext = jnp.where((gidx < 0)[:, None, None], lo_plane, ext)
    ext = jnp.where((gidx >= coarse_total)[:, None, None], hi_plane, ext)

    pro = along_x(ext, prolong_matrix(cx).astype(jnp.bfloat16), precision=lax.Precision.DEFAULT)
    pro = along_y(pro, prolong_matrix(cy), GRID)
    inner = pro[1:-1]
    even = 0.75 * inner + 0.25 * pro[:-2]
    odd = 0.75 * inner + 0.25 * pro[2:]
    log_perm = jnp.stack((even, odd), axis=1).reshape(2 * (n_ext - 2), fy, fx)
    k0_first = 2 * (g0 + 1)
    k0_planes = log_perm.shape[0]

    positions = k0_first + jnp.arange(k0_planes, dtype=jnp.int32)
    depth_table = mode_table(MZ, fine_total, positions)
    rows_table = mode_table(MY, fy, jnp.arange(fy, dtype=jnp.int32))
    cols_table = mode_table(MX, fx, jnp.arange(fx, dtype=jnp.int32))
    along_depth = jnp.einsum("abe,az->zbe", kl_coeffs[0], depth_table, precision=HI)
    along_rows = jnp.einsum("zbe,by->zye", along_depth, rows_table, precision=HI)
    kl = jnp.dot(along_rows.reshape(k0_planes * fy, MX), cols_table,
                 precision=HI).reshape(k0_planes, fy, fx)
    k0 = jnp.exp(log_perm + kl)
    k0 = jnp.where(plane_mask(k0_first, k0_planes, fine_total), k0, 0.0)
    k0_halo = (k0_planes - fz) // 2

    k1 = 0.125 * restrict_sum(k0)
    k1_halo = k0_halo // 2
    own1 = fz // 2
    k2_own = 0.125 * restrict_sum(k1[k1_halo:k1_halo + own1])

    h0k = F0_HALO + 1
    lvl0 = Level(k0[k0_halo - h0k: k0_halo + fz + h0k], h0k, fz, s * fz - h0k, fine_total)
    f0 = jnp.concatenate([got_l[crow:].reshape(F0_HALO, fy, fx), source,
                          got_r[crow:].reshape(F0_HALO, fy, fx)], axis=0)
    u = lvl0.start(f0, F0_HALO)
    u1 = lvl0.sweep(u, lvl0.cut(f0, F0_HALO - 1, F0_HALO), F0_HALO)
    res0 = f0[F0_HALO:F0_HALO + fz] - lvl0.operate(u1[1:-1], 1)
    f1_own = 0.5 * restrict_sum(res0)

    h1k = F1_HALO + 1
    extra = h1k - k1_halo
    from_left = shift_from(jnp.concatenate([k1[own1 - extra: own1], f1_own]), 1)
    from_right = shift_from(jnp.concatenate([f1_own, k1[2 * k1_halo: 2 * k1_halo + extra]]), -1)
    k1_ext = jnp.concatenate([from_left[:extra], k1, from_right[own1:]], axis=0)
    f1 = jnp.concatenate([from_left[extra:], f1_own, from_right[:own1]], axis=0)
    lvl1 = Level(k1_ext, h1k, own1, s * own1 - h1k, fine_total // 2)
    v = lvl1.start(f1, F1_HALO)
    v1 = lvl1.sweep(v, lvl1.cut(f1, F1_HALO - 1, F1_HALO), F1_HALO)
    res1 = f1_own - lvl1.operate(v1[2:-2], 1)
    both = gather_window(jnp.stack([0.5 * restrict_sum(res1), k2_own]))

    own2 = own1 // 2
    total2 = fine_total // 4
    k2_halo = 13
    f2_halo = k2_halo - 1
    reach = (both.shape[0] // 2) * own2
    f2w = both[:, 0].reshape((-1,) + both.shape[3:])[reach - f2_halo: reach + own2 + f2_halo]
    k2w = both[:, 1].reshape((-1,) + both.shape[3:])[reach - k2_halo: reach + own2 + k2_halo]
    lvl2 = Level(k2w, k2_halo, own2, s * own2 - k2_halo, total2)
    w = lvl2.start(f2w, f2_halo)
    w1 = lvl2.sweep(w, lvl2.cut(f2w, f2_halo - 1, f2_halo), f2_halo)
    res2 = lvl2.cut(f2w, f2_halo - 2, f2_halo) - lvl2.operate(w1, f2_halo - 1)
    f3 = 0.5 * restrict_sum(res2)
    f3_halo = (f2_halo - 2) // 2
    k3 = 0.125 * restrict_sum(k2w[1:-1])
    lvl3 = Level(k3, f3_halo + 1, own2 // 2, s * (own2 // 2) - f3_halo - 1, total2 // 2)
    b = lvl3.start(f3, f3_halo)
    for step in range(BOTTOM - 1):
        h = f3_halo - step
        b = lvl3.sweep(b, lvl3.cut(f3, h - 1, f3_halo), h)
    e3_halo = f3_halo - (BOTTOM - 1)
    cut2 = (f2_halo - 1) - 2 * e3_halo
    w = w1[cut2:w1.shape[0] - cut2] + copy_up(b)
    h = 2 * e3_halo
    for _ in range(SWEEPS):
        w = lvl2.sweep(w, lvl2.cut(f2w, h - 1, f2_halo), h)
        h -= 1
    e2 = w

    v = v1 + copy_up(e2)[1:-1]
    v = lvl1.sweep(v, lvl1.cut(f1, 2, F1_HALO), 3)
    e1 = lvl1.sweep(v, lvl1.cut(f1, 1, F1_HALO), 2)

    u = u1 + copy_up(e1)
    u = lvl0.sweep(u, lvl0.cut(f0, 1, F0_HALO), 2)
    u = lvl0.sweep(u, source, 1)
    return u[None]


def solution(mesh):
    return jax.shard_map(
        on_device,
        mesh=mesh,
        in_specs=(
            P("chain", None, "slab", None, None),
            P("chain", None),
            P(),
            P("chain", None, None, None),
            P("slab", None, None),
        ),
        out_specs=P("chain", "slab", None, None),
        check_vma=False,
    )
```

```python
import numpy as np
import jax
import jax.numpy as jnp
from jax import lax
from jax.sharding import PartitionSpec as P

STEPS = 4
MZ = 32
MY = 16
MX = 64
LEVELS = 4
SWEEPS = 2
BOTTOM = 4

OMEGA = 0.8
HI = lax.Precision.HIGHEST
GRID = lax.Precision.HIGH

F0_HALO = 3
F1_HALO = 4
COARSE_HALO = 4


def pair_sum_matrix(n):
    m = np.zeros((n, n // 2), np.float32)
    m[np.arange(n), np.arange(n) // 2] = 1.0
    return m


def repeat_matrix(n):
    return np.ascontiguousarray(pair_sum_matrix(2 * n).T)


def prolong_matrix(n):
    m = np.zeros((n, 2 * n), np.float32)
    for i in range(n):
        m[i, 2 * i] += 0.75
        m[max(i - 1, 0), 2 * i] += 0.25
        m[i, 2 * i + 1] += 0.75
        m[min(i + 1, n - 1), 2 * i + 1] += 0.25
    return m


def along_x(values, matrix, precision=HI):
    return jnp.einsum("zyx,xw->zyw", values, jnp.asarray(matrix), precision=precision,
                      preferred_element_type=jnp.float32)


def along_y(values, matrix, precision=HI):
    return jnp.einsum("zyx,yv->zvx", values, jnp.asarray(matrix), precision=precision,
                      preferred_element_type=jnp.float32)


def restrict_sum(values):
    nz, ny, nx = values.shape
    values = values.reshape(nz // 2, 2, ny, nx).sum(axis=1)
    values = along_y(values, pair_sum_matrix(ny), GRID)
    return along_x(values, pair_sum_matrix(nx), GRID)


def copy_up(values):
    nz, ny, nx = values.shape
    values = along_x(values, repeat_matrix(nx), GRID)
    values = along_y(values, repeat_matrix(ny), GRID)
    return jnp.repeat(values, 2, axis=0)


def shift_from(block, offset):
    count = lax.axis_size("slab")
    pairs = [(i, i + offset) for i in range(count) if 0 <= i + offset < count]
    return lax.ppermute(block, "slab", pairs)


def gather_window(block):
    got = jnp.concatenate([shift_from(block[None], 1), block[None], shift_from(block[None], -1)])
    got = jnp.concatenate([shift_from(got[:2], 2), got, shift_from(got[1:], -2)])
    return jnp.concatenate([shift_from(got[:4], 4), got, shift_from(got[3:], -4)])


def plane_mask(first_global, planes, total):
    g = first_global + jnp.arange(planes, dtype=jnp.int32)
    return ((g >= 0) & (g < total))[:, None, None]


class Level:
    def __init__(self, k, k_halo, own, first_global, total):
        self.own = own
        self.halo = k_halo - 1
        self.first = first_global + 1
        self.total = total
        faces_z = 0.5 * (k[1:] + k[:-1])
        kc = k[1:-1]
        rows = jnp.pad(kc, ((0, 0), (1, 1), (0, 0)))
        self.fy = 0.5 * (rows[:, 1:] + rows[:, :-1])
        cols = jnp.pad(kc, ((0, 0), (0, 0), (1, 1)))
        self.fx = 0.5 * (cols[:, :, 1:] + cols[:, :, :-1])
        self.fzl = faces_z[:-1]
        self.fzu = faces_z[1:]
        diag = self.fzl + self.fzu + self.fy[:, 1:] + self.fy[:, :-1]
        self.diag = diag + self.fx[:, :, 1:] + self.fx[:, :, :-1]

    def cut(self, arr, h, have):
        n = self.own + 2 * h
        return arr[have - h: have - h + n]

    def coef(self, h):
        c = self.cut
        H = self.halo
        return c(self.fzl, h, H), c(self.fzu, h, H), c(self.fy, h, H), c(self.fx, h, H), c(self.diag, h, H)

    def mask(self, u, h):
        return jnp.where(plane_mask(self.first + self.halo - h, u.shape[0], self.total), u, 0.0)

    def operate(self, u, h):
        fzl, fzu, fy, fx, diag = self.coef(h - 1)
        uc = u[1:-1]
        rows = jnp.pad(uc, ((0, 0), (1, 1), (0, 0)))
        cols = jnp.pad(uc, ((0, 0), (0, 0), (1, 1)))
        nb = fzu * u[2:] + fzl * u[:-2]
        nb = nb + fy[:, 1:] * rows[:, 2:] + fy[:, :-1] * rows[:, :-2]
        nb = nb + fx[:, :, 1:] * cols[:, :, 2:] + fx[:, :, :-1] * cols[:, :, :-2]
        return diag * uc - nb

    def sweep(self, u, f, h):
        diag = self.coef(h - 1)[4]
        new = u[1:-1] + OMEGA * (f - self.operate(u, h)) / diag
        return self.mask(new, h - 1)

    def start(self, f, h):
        return self.mask(OMEGA * f / self.coef(h)[4], h)


def mode_table(mode_count, length, positions):
    frequency = length // 2 + jnp.arange(mode_count, dtype=jnp.int32)
    phases = frequency[:, None] * (2 * positions[None, :] + 1) % (4 * length)
    return jnp.cos(jnp.pi * phases.astype(jnp.float32) / (2 * length))


def on_device(coarse_states, accept_flags, owners, kl_coeffs, source):
    slabs = lax.axis_size("slab")
    chain_index = lax.axis_index("chain")
    s = lax.axis_index("slab")
    step_numbers = jnp.arange(1, STEPS, dtype=jnp.int32)
    chosen = jnp.max(jnp.where(accept_flags == 1, step_numbers[None, :], 0), axis=1)
    local_count = coarse_states.shape[0]
    accepted = coarse_states[jnp.arange(local_count, dtype=jnp.int32), chosen]
    every_field = lax.all_gather(accepted, "chain", axis=0, tiled=True)
    own = lax.dynamic_index_in_dim(every_field, owners[chain_index], 0, keepdims=False)

    cz, cy, cx = own.shape
    fz = source.shape[0]
    fy, fx = 2 * cy, 2 * cx
    coarse_total = cz * slabs
    fine_total = fz * slabs

    crow = cz * cy * cx // fx

    def pack(source_part):
        return jnp.concatenate([own.astype(jnp.float32).reshape(crow, fx),
                                source_part.reshape(-1, fx)], axis=0)

    got_l = shift_from(pack(source[fz - F0_HALO:]), 1)
    got_r = shift_from(pack(source[:F0_HALO]), -1)
    coarse_l = got_l[:crow].reshape(cz, cy, cx).astype(own.dtype)
    coarse_r = got_r[:crow].reshape(cz, cy, cx).astype(own.dtype)
    ext = jnp.concatenate([coarse_l, own, coarse_r], axis=0)
    n_ext = ext.shape[0]
    g0 = s * cz - COARSE_HALO
    gidx = g0 + jnp.arange(n_ext, dtype=jnp.int32)
    lo_plane = lax.dynamic_index_in_dim(ext, jnp.maximum(-g0, 0), 0, keepdims=True)
    hi_plane = lax.dynamic_index_in_dim(ext, jnp.minimum(coarse_total - 1 - g0, n_ext - 1), 0, keepdims=True)
    ext = jnp.where((gidx < 0)[:, None, None], lo_plane, ext)
    ext = jnp.where((gidx >= coarse_total)[:, None, None], hi_plane, ext)

    pro = along_x(ext, prolong_matrix(cx).astype(jnp.bfloat16), precision=lax.Precision.DEFAULT)
    pro = along_y(pro, prolong_matrix(cy), GRID)
    inner = pro[1:-1]
    even = 0.75 * inner + 0.25 * pro[:-2]
    odd = 0.75 * inner + 0.25 * pro[2:]
    log_perm = jnp.stack((even, odd), axis=1).reshape(2 * (n_ext - 2), fy, fx)
    k0_first = 2 * (g0 + 1)
    k0_planes = log_perm.shape[0]

    positions = k0_first + jnp.arange(k0_planes, dtype=jnp.int32)
    depth_table = mode_table(MZ, fine_total, positions)
    rows_table = mode_table(MY, fy, jnp.arange(fy, dtype=jnp.int32))
    cols_table = mode_table(MX, fx, jnp.arange(fx, dtype=jnp.int32))
    along_depth = jnp.einsum("abe,az->zbe", kl_coeffs[0], depth_table, precision=GRID)
    along_rows = jnp.einsum("zbe,by->zye", along_depth, rows_table, precision=GRID)
    kl = jnp.dot(along_rows.reshape(k0_planes * fy, MX), cols_table,
                 precision=GRID).reshape(k0_planes, fy, fx)
    k0 = jnp.exp(log_perm + kl)
    k0 = jnp.where(plane_mask(k0_first, k0_planes, fine_total), k0, 0.0)
    k0_halo = (k0_planes - fz) // 2

    k1 = 0.125 * restrict_sum(k0)
    k1_halo = k0_halo // 2
    own1 = fz // 2
    k2_own = 0.125 * restrict_sum(k1[k1_halo:k1_halo + own1])

    h0k = F0_HALO + 1
    lvl0 = Level(k0[k0_halo - h0k: k0_halo + fz + h0k], h0k, fz, s * fz - h0k, fine_total)
    f0 = jnp.concatenate([got_l[crow:].reshape(F0_HALO, fy, fx), source,
                          got_r[crow:].reshape(F0_HALO, fy, fx)], axis=0)
    u = lvl0.start(f0, F0_HALO)
    u1 = lvl0.sweep(u, lvl0.cut(f0, F0_HALO - 1, F0_HALO), F0_HALO)
    res0 = f0[F0_HALO:F0_HALO + fz] - lvl0.operate(u1[1:-1], 1)
    f1_own = 0.5 * restrict_sum(res0)

    h1k = F1_HALO + 1
    extra = h1k - k1_halo
    from_left = shift_from(jnp.concatenate([k1[own1 - extra: own1], f1_own]), 1)
    from_right = shift_from(jnp.concatenate([f1_own, k1[2 * k1_halo: 2 * k1_halo + extra]]), -1)
    k1_ext = jnp.concatenate([from_left[:extra], k1, from_right[own1:]], axis=0)
    f1 = jnp.concatenate([from_left[extra:], f1_own, from_right[:own1]], axis=0)
    lvl1 = Level(k1_ext, h1k, own1, s * own1 - h1k, fine_total // 2)
    v = lvl1.start(f1, F1_HALO)
    v1 = lvl1.sweep(v, lvl1.cut(f1, F1_HALO - 1, F1_HALO), F1_HALO)
    res1 = f1_own - lvl1.operate(v1[2:-2], 1)
    both = gather_window(jnp.stack([0.5 * restrict_sum(res1), k2_own]))

    own2 = own1 // 2
    total2 = fine_total // 4
    k2_halo = 13
    f2_halo = k2_halo - 1
    reach = (both.shape[0] // 2) * own2
    f2w = both[:, 0].reshape((-1,) + both.shape[3:])[reach - f2_halo: reach + own2 + f2_halo]
    k2w = both[:, 1].reshape((-1,) + both.shape[3:])[reach - k2_halo: reach + own2 + k2_halo]
    lvl2 = Level(k2w, k2_halo, own2, s * own2 - k2_halo, total2)
    w = lvl2.start(f2w, f2_halo)
    w1 = lvl2.sweep(w, lvl2.cut(f2w, f2_halo - 1, f2_halo), f2_halo)
    res2 = lvl2.cut(f2w, f2_halo - 2, f2_halo) - lvl2.operate(w1, f2_halo - 1)
    f3 = 0.5 * restrict_sum(res2)
    f3_halo = (f2_halo - 2) // 2
    k3 = 0.125 * restrict_sum(k2w[1:-1])
    lvl3 = Level(k3, f3_halo + 1, own2 // 2, s * (own2 // 2) - f3_halo - 1, total2 // 2)
    b = lvl3.start(f3, f3_halo)
    for step in range(BOTTOM - 1):
        h = f3_halo - step
        b = lvl3.sweep(b, lvl3.cut(f3, h - 1, f3_halo), h)
    e3_halo = f3_halo - (BOTTOM - 1)
    cut2 = (f2_halo - 1) - 2 * e3_halo
    w = w1[cut2:w1.shape[0] - cut2] + copy_up(b)
    h = 2 * e3_halo
    for _ in range(SWEEPS):
        w = lvl2.sweep(w, lvl2.cut(f2w, h - 1, f2_halo), h)
        h -= 1
    e2 = w

    v = v1 + copy_up(e2)[1:-1]
    v = lvl1.sweep(v, lvl1.cut(f1, 2, F1_HALO), 3)
    e1 = lvl1.sweep(v, lvl1.cut(f1, 1, F1_HALO), 2)

    u = u1 + copy_up(e1)
    u = lvl0.sweep(u, lvl0.cut(f0, 1, F0_HALO), 2)
    u = lvl0.sweep(u, source, 1)
    return u[None]


def solution(mesh):
    return jax.shard_map(
        on_device,
        mesh=mesh,
        in_specs=(
            P("chain", None, "slab", None, None),
            P("chain", None),
            P(),
            P("chain", None, None, None),
            P("slab", None, None),
        ),
        out_specs=P("chain", "slab", None, None),
        check_vma=False,
    )
```

```python
import numpy as np
import jax
import jax.numpy as jnp
from jax import lax
from jax.sharding import PartitionSpec as P

STEPS = 4
MZ = 32
MY = 16
MX = 64
LEVELS = 4
SWEEPS = 2
BOTTOM = 4

OMEGA = 0.8
HI = lax.Precision.HIGHEST
GRID = lax.Precision.HIGH

F0_HALO = 3
F1_HALO = 4
COARSE_HALO = 4


def pair_sum_matrix(n):
    m = np.zeros((n, n // 2), np.float32)
    m[np.arange(n), np.arange(n) // 2] = 1.0
    return m


def repeat_matrix(n):
    return np.ascontiguousarray(pair_sum_matrix(2 * n).T)


def prolong_matrix(n):
    m = np.zeros((n, 2 * n), np.float32)
    for i in range(n):
        m[i, 2 * i] += 0.75
        m[max(i - 1, 0), 2 * i] += 0.25
        m[i, 2 * i + 1] += 0.75
        m[min(i + 1, n - 1), 2 * i + 1] += 0.25
    return m


def along_x(values, matrix, precision=HI):
    return jnp.einsum("zyx,xw->zyw", values, jnp.asarray(matrix), precision=precision,
                      preferred_element_type=jnp.float32)


def along_y(values, matrix, precision=HI):
    return jnp.einsum("zyx,yv->zvx", values, jnp.asarray(matrix), precision=precision,
                      preferred_element_type=jnp.float32)


def restrict_sum(values):
    nz, ny, nx = values.shape
    values = values.reshape(nz // 2, 2, ny, nx).sum(axis=1)
    values = along_x(values, pair_sum_matrix(nx), GRID)
    return along_y(values, pair_sum_matrix(ny), GRID)


def copy_up(values):
    nz, ny, nx = values.shape
    values = along_y(values, repeat_matrix(ny), GRID)
    values = along_x(values, repeat_matrix(nx), GRID)
    return jnp.repeat(values, 2, axis=0)


def shift_from(block, offset):
    count = lax.axis_size("slab")
    pairs = [(i, i + offset) for i in range(count) if 0 <= i + offset < count]
    return lax.ppermute(block, "slab", pairs)


def gather_window(block):
    got = jnp.concatenate([shift_from(block[None], 1), block[None], shift_from(block[None], -1)])
    got = jnp.concatenate([shift_from(got[:2], 2), got, shift_from(got[1:], -2)])
    return jnp.concatenate([shift_from(got[:4], 4), got, shift_from(got[3:], -4)])


def plane_mask(first_global, planes, total):
    g = first_global + jnp.arange(planes, dtype=jnp.int32)
    return ((g >= 0) & (g < total))[:, None, None]


class Level:
    def __init__(self, k, k_halo, own, first_global, total):
        self.own = own
        self.halo = k_halo - 1
        self.first = first_global + 1
        self.total = total
        faces_z = 0.5 * (k[1:] + k[:-1])
        kc = k[1:-1]
        rows = jnp.pad(kc, ((0, 0), (1, 1), (0, 0)))
        self.fy = 0.5 * (rows[:, 1:] + rows[:, :-1])
        cols = jnp.pad(kc, ((0, 0), (0, 0), (1, 1)))
        self.fx = 0.5 * (cols[:, :, 1:] + cols[:, :, :-1])
        self.fzl = faces_z[:-1]
        self.fzu = faces_z[1:]
        diag = self.fzl + self.fzu + self.fy[:, 1:] + self.fy[:, :-1]
        self.diag = diag + self.fx[:, :, 1:] + self.fx[:, :, :-1]

    def cut(self, arr, h, have):
        n = self.own + 2 * h
        return arr[have - h: have - h + n]

    def coef(self, h):
        c = self.cut
        H = self.halo
        return c(self.fzl, h, H), c(self.fzu, h, H), c(self.fy, h, H), c(self.fx, h, H), c(self.diag, h, H)

    def mask(self, u, h):
        return jnp.where(plane_mask(self.first + self.halo - h, u.shape[0], self.total), u, 0.0)

    def operate(self, u, h):
        fzl, fzu, fy, fx, diag = self.coef(h - 1)
        uc = u[1:-1]
        rows = jnp.pad(uc, ((0, 0), (1, 1), (0, 0)))
        cols = jnp.pad(uc, ((0, 0), (0, 0), (1, 1)))
        nb = fzu * u[2:] + fzl * u[:-2]
        nb = nb + fy[:, 1:] * rows[:, 2:] + fy[:, :-1] * rows[:, :-2]
        nb = nb + fx[:, :, 1:] * cols[:, :, 2:] + fx[:, :, :-1] * cols[:, :, :-2]
        return diag * uc - nb

    def sweep(self, u, f, h):
        diag = self.coef(h - 1)[4]
        new = u[1:-1] + OMEGA * (f - self.operate(u, h)) / diag
        return self.mask(new, h - 1)

    def start(self, f, h):
        return self.mask(OMEGA * f / self.coef(h)[4], h)


def mode_table(mode_count, length, positions):
    frequency = length // 2 + jnp.arange(mode_count, dtype=jnp.int32)
    phases = frequency[:, None] * (2 * positions[None, :] + 1) % (4 * length)
    return jnp.cos(jnp.pi * phases.astype(jnp.float32) / (2 * length))


def on_device(coarse_states, accept_flags, owners, kl_coeffs, source):
    slabs = lax.axis_size("slab")
    chain_index = lax.axis_index("chain")
    s = lax.axis_index("slab")
    step_numbers = jnp.arange(1, STEPS, dtype=jnp.int32)
    chosen = jnp.max(jnp.where(accept_flags == 1, step_numbers[None, :], 0), axis=1)
    local_count = coarse_states.shape[0]
    accepted = coarse_states[jnp.arange(local_count, dtype=jnp.int32), chosen]
    every_field = lax.all_gather(accepted, "chain", axis=0, tiled=True)
    own = lax.dynamic_index_in_dim(every_field, owners[chain_index], 0, keepdims=False)

    cz, cy, cx = own.shape
    fz = source.shape[0]
    fy, fx = 2 * cy, 2 * cx
    coarse_total = cz * slabs
    fine_total = fz * slabs

    crow = cz * cy * cx // fx

    def pack(source_part):
        return jnp.concatenate([own.astype(jnp.float32).reshape(crow, fx),
                                source_part.reshape(-1, fx)], axis=0)

    got_l = shift_from(pack(source[fz - F0_HALO:]), 1)
    got_r = shift_from(pack(source[:F0_HALO]), -1)
    coarse_l = got_l[:crow].reshape(cz, cy, cx).astype(own.dtype)
    coarse_r = got_r[:crow].reshape(cz, cy, cx).astype(own.dtype)
    ext = jnp.concatenate([coarse_l, own, coarse_r], axis=0)
    n_ext = ext.shape[0]
    g0 = s * cz - COARSE_HALO
    gidx = g0 + jnp.arange(n_ext, dtype=jnp.int32)
    lo_plane = lax.dynamic_index_in_dim(ext, jnp.maximum(-g0, 0), 0, keepdims=True)
    hi_plane = lax.dynamic_index_in_dim(ext, jnp.minimum(coarse_total - 1 - g0, n_ext - 1), 0, keepdims=True)
    ext = jnp.where((gidx < 0)[:, None, None], lo_plane, ext)
    ext = jnp.where((gidx >= coarse_total)[:, None, None], hi_plane, ext)

    pro = along_x(ext, prolong_matrix(cx).astype(jnp.bfloat16), precision=lax.Precision.DEFAULT)
    pro = along_y(pro, prolong_matrix(cy), GRID)
    inner = pro[1:-1]
    even = 0.75 * inner + 0.25 * pro[:-2]
    odd = 0.75 * inner + 0.25 * pro[2:]
    log_perm = jnp.stack((even, odd), axis=1).reshape(2 * (n_ext - 2), fy, fx)
    k0_first = 2 * (g0 + 1)
    k0_planes = log_perm.shape[0]

    positions = k0_first + jnp.arange(k0_planes, dtype=jnp.int32)
    depth_table = mode_table(MZ, fine_total, positions)
    rows_table = mode_table(MY, fy, jnp.arange(fy, dtype=jnp.int32))
    cols_table = mode_table(MX, fx, jnp.arange(fx, dtype=jnp.int32))
    along_depth = jnp.einsum("abe,az->zbe", kl_coeffs[0], depth_table, precision=GRID)
    along_rows = jnp.einsum("zbe,by->zye", along_depth, rows_table, precision=GRID)
    kl = jnp.dot(along_rows.reshape(k0_planes * fy, MX), cols_table,
                 precision=GRID).reshape(k0_planes, fy, fx)
    k0 = jnp.exp(log_perm + kl)
    k0 = jnp.where(plane_mask(k0_first, k0_planes, fine_total), k0, 0.0)
    k0_halo = (k0_planes - fz) // 2

    k1 = 0.125 * restrict_sum(k0)
    k1_halo = k0_halo // 2
    own1 = fz // 2
    k2_own = 0.125 * restrict_sum(k1[k1_halo:k1_halo + own1])

    h0k = F0_HALO + 1
    lvl0 = Level(k0[k0_halo - h0k: k0_halo + fz + h0k], h0k, fz, s * fz - h0k, fine_total)
    f0 = jnp.concatenate([got_l[crow:].reshape(F0_HALO, fy, fx), source,
                          got_r[crow:].reshape(F0_HALO, fy, fx)], axis=0)
    u = lvl0.start(f0, F0_HALO)
    u1 = lvl0.sweep(u, lvl0.cut(f0, F0_HALO - 1, F0_HALO), F0_HALO)
    res0 = f0[F0_HALO:F0_HALO + fz] - lvl0.operate(u1[1:-1], 1)
    f1_own = 0.5 * restrict_sum(res0)

    h1k = F1_HALO + 1
    extra = h1k - k1_halo
    from_left = shift_from(jnp.concatenate([k1[own1 - extra: own1], f1_own]), 1)
    from_right = shift_from(jnp.concatenate([f1_own, k1[2 * k1_halo: 2 * k1_halo + extra]]), -1)
    k1_ext = jnp.concatenate([from_left[:extra], k1, from_right[own1:]], axis=0)
    f1 = jnp.concatenate([from_left[extra:], f1_own, from_right[:own1]], axis=0)
    lvl1 = Level(k1_ext, h1k, own1, s * own1 - h1k, fine_total // 2)
    v = lvl1.start(f1, F1_HALO)
    v1 = lvl1.sweep(v, lvl1.cut(f1, F1_HALO - 1, F1_HALO), F1_HALO)
    res1 = f1_own - lvl1.operate(v1[2:-2], 1)
    both = gather_window(jnp.stack([0.5 * restrict_sum(res1), k2_own]))

    own2 = own1 // 2
    total2 = fine_total // 4
    k2_halo = 13
    f2_halo = k2_halo - 1
    reach = (both.shape[0] // 2) * own2
    f2w = both[:, 0].reshape((-1,) + both.shape[3:])[reach - f2_halo: reach + own2 + f2_halo]
    k2w = both[:, 1].reshape((-1,) + both.shape[3:])[reach - k2_halo: reach + own2 + k2_halo]
    lvl2 = Level(k2w, k2_halo, own2, s * own2 - k2_halo, total2)
    w = lvl2.start(f2w, f2_halo)
    w1 = lvl2.sweep(w, lvl2.cut(f2w, f2_halo - 1, f2_halo), f2_halo)
    res2 = lvl2.cut(f2w, f2_halo - 2, f2_halo) - lvl2.operate(w1, f2_halo - 1)
    f3 = 0.5 * restrict_sum(res2)
    f3_halo = (f2_halo - 2) // 2
    k3 = 0.125 * restrict_sum(k2w[1:-1])
    lvl3 = Level(k3, f3_halo + 1, own2 // 2, s * (own2 // 2) - f3_halo - 1, total2 // 2)
    b = lvl3.start(f3, f3_halo)
    for step in range(BOTTOM - 1):
        h = f3_halo - step
        b = lvl3.sweep(b, lvl3.cut(f3, h - 1, f3_halo), h)
    e3_halo = f3_halo - (BOTTOM - 1)
    cut2 = (f2_halo - 1) - 2 * e3_halo
    w = w1[cut2:w1.shape[0] - cut2] + copy_up(b)
    h = 2 * e3_halo
    for _ in range(SWEEPS):
        w = lvl2.sweep(w, lvl2.cut(f2w, h - 1, f2_halo), h)
        h -= 1
    e2 = w

    v = v1 + copy_up(e2)[1:-1]
    v = lvl1.sweep(v, lvl1.cut(f1, 2, F1_HALO), 3)
    e1 = lvl1.sweep(v, lvl1.cut(f1, 1, F1_HALO), 2)

    u = u1 + copy_up(e1)
    u = lvl0.sweep(u, lvl0.cut(f0, 1, F0_HALO), 2)
    u = lvl0.sweep(u, source, 1)
    return u[None]


def solution(mesh):
    return jax.shard_map(
        on_device,
        mesh=mesh,
        in_specs=(
            P("chain", None, "slab", None, None),
            P("chain", None),
            P(),
            P("chain", None, None, None),
            P("slab", None, None),
        ),
        out_specs=P("chain", "slab", None, None),
        check_vma=False,
    )
```

```python
import numpy as np
import jax
import jax.numpy as jnp
from jax import lax
from jax.sharding import PartitionSpec as P

STEPS = 4
MZ = 32
MY = 16
MX = 64
LEVELS = 4
SWEEPS = 2
BOTTOM = 4

OMEGA = 0.8
HI = lax.Precision.HIGHEST
GRID = lax.Precision.HIGH

F0_HALO = 3
F1_HALO = 4
COARSE_HALO = 4


def pair_sum_matrix(n):
    m = np.zeros((n, n // 2), np.float32)
    m[np.arange(n), np.arange(n) // 2] = 1.0
    return m


def repeat_matrix(n):
    return np.ascontiguousarray(pair_sum_matrix(2 * n).T)


def prolong_matrix(n):
    m = np.zeros((n, 2 * n), np.float32)
    for i in range(n):
        m[i, 2 * i] += 0.75
        m[max(i - 1, 0), 2 * i] += 0.25
        m[i, 2 * i + 1] += 0.75
        m[min(i + 1, n - 1), 2 * i + 1] += 0.25
    return m


def along_x(values, matrix, precision=HI):
    return jnp.einsum("zyx,xw->zyw", values, jnp.asarray(matrix), precision=precision,
                      preferred_element_type=jnp.float32)


def along_y(values, matrix, precision=HI):
    return jnp.einsum("zyx,yv->zvx", values, jnp.asarray(matrix), precision=precision,
                      preferred_element_type=jnp.float32)


def restrict_sum(values):
    nz, ny, nx = values.shape
    values = values.reshape(nz // 2, 2, ny, nx).sum(axis=1)
    values = along_x(values, pair_sum_matrix(nx), GRID)
    return along_y(values, pair_sum_matrix(ny), GRID)


def copy_up(values):
    nz, ny, nx = values.shape
    values = along_y(values, repeat_matrix(ny), GRID)
    values = along_x(values, repeat_matrix(nx), GRID)
    return jnp.repeat(values, 2, axis=0)


def shift_from(block, offset):
    count = lax.axis_size("slab")
    pairs = [(i, i + offset) for i in range(count) if 0 <= i + offset < count]
    return lax.ppermute(block, "slab", pairs)


def gather_window(block):
    got = jnp.concatenate([shift_from(block[None], 1), block[None], shift_from(block[None], -1)])
    got = jnp.concatenate([shift_from(got[:2], 2), got, shift_from(got[1:], -2)])
    return jnp.concatenate([shift_from(got[:4], 4), got, shift_from(got[3:], -4)])


def plane_mask(first_global, planes, total):
    g = first_global + jnp.arange(planes, dtype=jnp.int32)
    return ((g >= 0) & (g < total))[:, None, None]


class Level:
    def __init__(self, k, k_halo, own, first_global, total):
        self.own = own
        self.halo = k_halo - 1
        self.first = first_global + 1
        self.total = total
        faces_z = 0.5 * (k[1:] + k[:-1])
        kc = k[1:-1]
        rows = jnp.pad(kc, ((0, 0), (1, 1), (0, 0)))
        self.fy = 0.5 * (rows[:, 1:] + rows[:, :-1])
        cols = jnp.pad(kc, ((0, 0), (0, 0), (1, 1)))
        self.fx = 0.5 * (cols[:, :, 1:] + cols[:, :, :-1])
        self.fzl = faces_z[:-1]
        self.fzu = faces_z[1:]
        diag = self.fzl + self.fzu + self.fy[:, 1:] + self.fy[:, :-1]
        self.diag = diag + self.fx[:, :, 1:] + self.fx[:, :, :-1]

    def cut(self, arr, h, have):
        n = self.own + 2 * h
        return arr[have - h: have - h + n]

    def coef(self, h):
        c = self.cut
        H = self.halo
        return c(self.fzl, h, H), c(self.fzu, h, H), c(self.fy, h, H), c(self.fx, h, H), c(self.diag, h, H)

    def mask(self, u, h):
        return jnp.where(plane_mask(self.first + self.halo - h, u.shape[0], self.total), u, 0.0)

    def operate(self, u, h):
        fzl, fzu, fy, fx, diag = self.coef(h - 1)
        uc = u[1:-1]
        rows = jnp.pad(uc, ((0, 0), (1, 1), (0, 0)))
        cols = jnp.pad(uc, ((0, 0), (0, 0), (1, 1)))
        nb = fzu * u[2:] + fzl * u[:-2]
        nb = nb + fy[:, 1:] * rows[:, 2:] + fy[:, :-1] * rows[:, :-2]
        nb = nb + fx[:, :, 1:] * cols[:, :, 2:] + fx[:, :, :-1] * cols[:, :, :-2]
        return diag * uc - nb

    def sweep(self, u, f, h):
        diag = self.coef(h - 1)[4]
        new = u[1:-1] + OMEGA * (f - self.operate(u, h)) / diag
        return self.mask(new, h - 1)

    def start(self, f, h):
        return self.mask(OMEGA * f / self.coef(h)[4], h)


def mode_table(mode_count, length, positions):
    frequency = length // 2 + jnp.arange(mode_count, dtype=jnp.int32)
    phases = frequency[:, None] * (2 * positions[None, :] + 1) % (4 * length)
    return jnp.cos(jnp.pi * phases.astype(jnp.float32) / (2 * length))


def on_device(coarse_states, accept_flags, owners, kl_coeffs, source):
    slabs = lax.axis_size("slab")
    chain_index = lax.axis_index("chain")
    s = lax.axis_index("slab")
    step_numbers = jnp.arange(1, STEPS, dtype=jnp.int32)
    chosen = jnp.max(jnp.where(accept_flags == 1, step_numbers[None, :], 0), axis=1)
    local_count = coarse_states.shape[0]
    accepted = coarse_states[jnp.arange(local_count, dtype=jnp.int32), chosen]
    every_field = lax.all_gather(accepted, "chain", axis=0, tiled=True)
    own = lax.dynamic_index_in_dim(every_field, owners[chain_index], 0, keepdims=False)

    cz, cy, cx = own.shape
    fz = source.shape[0]
    fy, fx = 2 * cy, 2 * cx
    coarse_total = cz * slabs
    fine_total = fz * slabs

    crow = cz * cy * cx // fx

    def pack(source_part):
        return jnp.concatenate([own.astype(jnp.float32).reshape(crow, fx),
                                source_part.reshape(-1, fx)], axis=0)

    got_l = shift_from(pack(source[fz - F0_HALO:]), 1)
    got_r = shift_from(pack(source[:F0_HALO]), -1)
    coarse_l = got_l[:crow].reshape(cz, cy, cx).astype(own.dtype)
    coarse_r = got_r[:crow].reshape(cz, cy, cx).astype(own.dtype)
    ext = jnp.concatenate([coarse_l, own, coarse_r], axis=0)
    n_ext = ext.shape[0]
    g0 = s * cz - COARSE_HALO
    gidx = g0 + jnp.arange(n_ext, dtype=jnp.int32)
    lo_plane = lax.dynamic_index_in_dim(ext, jnp.maximum(-g0, 0), 0, keepdims=True)
    hi_plane = lax.dynamic_index_in_dim(ext, jnp.minimum(coarse_total - 1 - g0, n_ext - 1), 0, keepdims=True)
    ext = jnp.where((gidx < 0)[:, None, None], lo_plane, ext)
    ext = jnp.where((gidx >= coarse_total)[:, None, None], hi_plane, ext)

    pro = along_y(ext, prolong_matrix(cy).astype(jnp.bfloat16), precision=lax.Precision.DEFAULT)
    pro = along_x(pro, prolong_matrix(cx), GRID)
    inner = pro[1:-1]
    even = 0.75 * inner + 0.25 * pro[:-2]
    odd = 0.75 * inner + 0.25 * pro[2:]
    log_perm = jnp.stack((even, odd), axis=1).reshape(2 * (n_ext - 2), fy, fx)
    k0_first = 2 * (g0 + 1)
    k0_planes = log_perm.shape[0]

    positions = k0_first + jnp.arange(k0_planes, dtype=jnp.int32)
    depth_table = mode_table(MZ, fine_total, positions)
    rows_table = mode_table(MY, fy, jnp.arange(fy, dtype=jnp.int32))
    cols_table = mode_table(MX, fx, jnp.arange(fx, dtype=jnp.int32))
    along_depth = jnp.einsum("abe,az->zbe", kl_coeffs[0], depth_table, precision=GRID)
    along_rows = jnp.einsum("zbe,by->zye", along_depth, rows_table, precision=GRID)
    kl = jnp.dot(along_rows.reshape(k0_planes * fy, MX), cols_table,
                 precision=GRID).reshape(k0_planes, fy, fx)
    k0 = jnp.exp(log_perm + kl)
    k0 = jnp.where(plane_mask(k0_first, k0_planes, fine_total), k0, 0.0)
    k0_halo = (k0_planes - fz) // 2

    k1 = 0.125 * restrict_sum(k0)
    k1_halo = k0_halo // 2
    own1 = fz // 2
    k2_own = 0.125 * restrict_sum(k1[k1_halo:k1_halo + own1])

    h0k = F0_HALO + 1
    lvl0 = Level(k0[k0_halo - h0k: k0_halo + fz + h0k], h0k, fz, s * fz - h0k, fine_total)
    f0 = jnp.concatenate([got_l[crow:].reshape(F0_HALO, fy, fx), source,
                          got_r[crow:].reshape(F0_HALO, fy, fx)], axis=0)
    u = lvl0.start(f0, F0_HALO)
    u1 = lvl0.sweep(u, lvl0.cut(f0, F0_HALO - 1, F0_HALO), F0_HALO)
    res0 = f0[F0_HALO:F0_HALO + fz] - lvl0.operate(u1[1:-1], 1)
    f1_own = 0.5 * restrict_sum(res0)

    h1k = F1_HALO + 1
    extra = h1k - k1_halo
    from_left = shift_from(jnp.concatenate([k1[own1 - extra: own1], f1_own]), 1)
    from_right = shift_from(jnp.concatenate([f1_own, k1[2 * k1_halo: 2 * k1_halo + extra]]), -1)
    k1_ext = jnp.concatenate([from_left[:extra], k1, from_right[own1:]], axis=0)
    f1 = jnp.concatenate([from_left[extra:], f1_own, from_right[:own1]], axis=0)
    lvl1 = Level(k1_ext, h1k, own1, s * own1 - h1k, fine_total // 2)
    v = lvl1.start(f1, F1_HALO)
    v1 = lvl1.sweep(v, lvl1.cut(f1, F1_HALO - 1, F1_HALO), F1_HALO)
    res1 = f1_own - lvl1.operate(v1[2:-2], 1)
    both = gather_window(jnp.stack([0.5 * restrict_sum(res1), k2_own]))

    own2 = own1 // 2
    total2 = fine_total // 4
    k2_halo = 13
    f2_halo = k2_halo - 1
    reach = (both.shape[0] // 2) * own2
    f2w = both[:, 0].reshape((-1,) + both.shape[3:])[reach - f2_halo: reach + own2 + f2_halo]
    k2w = both[:, 1].reshape((-1,) + both.shape[3:])[reach - k2_halo: reach + own2 + k2_halo]
    lvl2 = Level(k2w, k2_halo, own2, s * own2 - k2_halo, total2)
    w = lvl2.start(f2w, f2_halo)
    w1 = lvl2.sweep(w, lvl2.cut(f2w, f2_halo - 1, f2_halo), f2_halo)
    res2 = lvl2.cut(f2w, f2_halo - 2, f2_halo) - lvl2.operate(w1, f2_halo - 1)
    f3 = 0.5 * restrict_sum(res2)
    f3_halo = (f2_halo - 2) // 2
    k3 = 0.125 * restrict_sum(k2w[1:-1])
    lvl3 = Level(k3, f3_halo + 1, own2 // 2, s * (own2 // 2) - f3_halo - 1, total2 // 2)
    b = lvl3.start(f3, f3_halo)
    for step in range(BOTTOM - 1):
        h = f3_halo - step
        b = lvl3.sweep(b, lvl3.cut(f3, h - 1, f3_halo), h)
    e3_halo = f3_halo - (BOTTOM - 1)
    cut2 = (f2_halo - 1) - 2 * e3_halo
    w = w1[cut2:w1.shape[0] - cut2] + copy_up(b)
    h = 2 * e3_halo
    for _ in range(SWEEPS):
        w = lvl2.sweep(w, lvl2.cut(f2w, h - 1, f2_halo), h)
        h -= 1
    e2 = w

    v = v1 + copy_up(e2)[1:-1]
    v = lvl1.sweep(v, lvl1.cut(f1, 2, F1_HALO), 3)
    e1 = lvl1.sweep(v, lvl1.cut(f1, 1, F1_HALO), 2)

    u = u1 + copy_up(e1)
    u = lvl0.sweep(u, lvl0.cut(f0, 1, F0_HALO), 2)
    u = lvl0.sweep(u, source, 1)
    return u[None]


def solution(mesh):
    return jax.shard_map(
        on_device,
        mesh=mesh,
        in_specs=(
            P("chain", None, "slab", None, None),
            P("chain", None),
            P(),
            P("chain", None, None, None),
            P("slab", None, None),
        ),
        out_specs=P("chain", "slab", None, None),
        check_vma=False,
    )
```

```python
import numpy as np
import jax
import jax.numpy as jnp
from jax import lax
from jax.sharding import PartitionSpec as P

STEPS = 4
MZ = 32
MY = 16
MX = 64
LEVELS = 4
SWEEPS = 2
BOTTOM = 4

OMEGA = 0.8
HI = lax.Precision.HIGHEST
GRID = lax.Precision.HIGH

F0_HALO = 3
F1_HALO = 4
COARSE_HALO = 4


def pair_sum_matrix(n):
    m = np.zeros((n, n // 2), np.float32)
    m[np.arange(n), np.arange(n) // 2] = 1.0
    return m


def repeat_matrix(n):
    return np.ascontiguousarray(pair_sum_matrix(2 * n).T)


def prolong_matrix(n):
    m = np.zeros((n, 2 * n), np.float32)
    for i in range(n):
        m[i, 2 * i] += 0.75
        m[max(i - 1, 0), 2 * i] += 0.25
        m[i, 2 * i + 1] += 0.75
        m[min(i + 1, n - 1), 2 * i + 1] += 0.25
    return m


def along_x(values, matrix, precision=HI):
    return jnp.einsum("zyx,xw->zyw", values, jnp.asarray(matrix), precision=precision,
                      preferred_element_type=jnp.float32)


def along_y(values, matrix, precision=HI):
    return jnp.einsum("zyx,yv->zvx", values, jnp.asarray(matrix), precision=precision,
                      preferred_element_type=jnp.float32)


def restrict_sum(values):
    nz, ny, nx = values.shape
    values = values.reshape(nz // 2, 2, ny, nx).sum(axis=1)
    values = along_x(values, pair_sum_matrix(nx), GRID)
    return along_y(values, pair_sum_matrix(ny), GRID)


def copy_up(values):
    nz, ny, nx = values.shape
    values = along_y(values, repeat_matrix(ny), GRID)
    values = along_x(values, repeat_matrix(nx), GRID)
    return jnp.repeat(values, 2, axis=0)


def shift_from(block, offset):
    count = lax.axis_size("slab")
    pairs = [(i, i + offset) for i in range(count) if 0 <= i + offset < count]
    return lax.ppermute(block, "slab", pairs)


def gather_window(block):
    got = jnp.concatenate([shift_from(block[None], 1), block[None], shift_from(block[None], -1)])
    got = jnp.concatenate([shift_from(got[:2], 2), got, shift_from(got[1:], -2)])
    return jnp.concatenate([shift_from(got[:4], 4), got, shift_from(got[3:], -4)])


def plane_mask(first_global, planes, total):
    g = first_global + jnp.arange(planes, dtype=jnp.int32)
    return ((g >= 0) & (g < total))[:, None, None]


class Level:
    def __init__(self, k, k_halo, own, first_global, total):
        self.own = own
        self.halo = k_halo - 1
        self.first = first_global + 1
        self.total = total
        faces_z = 0.5 * (k[1:] + k[:-1])
        kc = k[1:-1]
        rows = jnp.pad(kc, ((0, 0), (1, 1), (0, 0)))
        self.fy = 0.5 * (rows[:, 1:] + rows[:, :-1])
        cols = jnp.pad(kc, ((0, 0), (0, 0), (1, 1)))
        self.fx = 0.5 * (cols[:, :, 1:] + cols[:, :, :-1])
        self.fzl = faces_z[:-1]
        self.fzu = faces_z[1:]
        diag = self.fzl + self.fzu + self.fy[:, 1:] + self.fy[:, :-1]
        self.diag = diag + self.fx[:, :, 1:] + self.fx[:, :, :-1]

    def cut(self, arr, h, have):
        n = self.own + 2 * h
        return arr[have - h: have - h + n]

    def coef(self, h):
        c = self.cut
        H = self.halo
        return c(self.fzl, h, H), c(self.fzu, h, H), c(self.fy, h, H), c(self.fx, h, H), c(self.diag, h, H)

    def mask(self, u, h):
        return jnp.where(plane_mask(self.first + self.halo - h, u.shape[0], self.total), u, 0.0)

    def operate(self, u, h):
        fzl, fzu, fy, fx, diag = self.coef(h - 1)
        uc = u[1:-1]
        rows = jnp.pad(uc, ((0, 0), (1, 1), (0, 0)))
        cols = jnp.pad(uc, ((0, 0), (0, 0), (1, 1)))
        nb = fzu * u[2:] + fzl * u[:-2]
        nb = nb + fy[:, 1:] * rows[:, 2:] + fy[:, :-1] * rows[:, :-2]
        nb = nb + fx[:, :, 1:] * cols[:, :, 2:] + fx[:, :, :-1] * cols[:, :, :-2]
        return diag * uc - nb

    def sweep(self, u, f, h):
        diag = self.coef(h - 1)[4]
        new = u[1:-1] + OMEGA * (f - self.operate(u, h)) / diag
        return self.mask(new, h - 1)

    def start(self, f, h):
        return self.mask(OMEGA * f / self.coef(h)[4], h)


def mode_table(mode_count, length, positions):
    frequency = length // 2 + jnp.arange(mode_count, dtype=jnp.int32)
    phases = frequency[:, None] * (2 * positions[None, :] + 1) % (4 * length)
    return jnp.cos(jnp.pi * phases.astype(jnp.float32) / (2 * length))


def on_device(coarse_states, accept_flags, owners, kl_coeffs, source):
    slabs = lax.axis_size("slab")
    chain_index = lax.axis_index("chain")
    s = lax.axis_index("slab")
    step_numbers = jnp.arange(1, STEPS, dtype=jnp.int32)
    chosen = jnp.max(jnp.where(accept_flags == 1, step_numbers[None, :], 0), axis=1)
    local_count = coarse_states.shape[0]
    accepted = coarse_states[jnp.arange(local_count, dtype=jnp.int32), chosen]
    every_field = lax.all_gather(accepted, "chain", axis=0, tiled=True)
    own = lax.dynamic_index_in_dim(every_field, owners[chain_index], 0, keepdims=False)

    cz, cy, cx = own.shape
    fz = source.shape[0]
    fy, fx = 2 * cy, 2 * cx
    coarse_total = cz * slabs
    fine_total = fz * slabs

    crow = cz * cy * cx // fx

    def pack(source_part):
        return jnp.concatenate([own.astype(jnp.float32).reshape(crow, fx),
                                source_part.reshape(-1, fx)], axis=0)

    got_l = shift_from(pack(source[fz - F0_HALO:]), 1)
    got_r = shift_from(pack(source[:F0_HALO]), -1)
    coarse_l = got_l[:crow].reshape(cz, cy, cx).astype(own.dtype)
    coarse_r = got_r[:crow].reshape(cz, cy, cx).astype(own.dtype)
    ext = jnp.concatenate([coarse_l, own, coarse_r], axis=0)
    n_ext = ext.shape[0]
    g0 = s * cz - COARSE_HALO
    gidx = g0 + jnp.arange(n_ext, dtype=jnp.int32)
    lo_plane = lax.dynamic_index_in_dim(ext, jnp.maximum(-g0, 0), 0, keepdims=True)
    hi_plane = lax.dynamic_index_in_dim(ext, jnp.minimum(coarse_total - 1 - g0, n_ext - 1), 0, keepdims=True)
    ext = jnp.where((gidx < 0)[:, None, None], lo_plane, ext)
    ext = jnp.where((gidx >= coarse_total)[:, None, None], hi_plane, ext)

    wide = ext.astype(jnp.float32)
    inner = wide[1:-1]
    even = 0.75 * inner + 0.25 * wide[:-2]
    odd = 0.75 * inner + 0.25 * wide[2:]
    pro = jnp.stack((even, odd), axis=1).reshape(2 * (n_ext - 2), cy, cx)
    pro = along_y(pro, prolong_matrix(cy), GRID)
    log_perm = along_x(pro, prolong_matrix(cx), GRID)
    k0_first = 2 * (g0 + 1)
    k0_planes = log_perm.shape[0]

    positions = k0_first + jnp.arange(k0_planes, dtype=jnp.int32)
    depth_table = mode_table(MZ, fine_total, positions)
    rows_table = mode_table(MY, fy, jnp.arange(fy, dtype=jnp.int32))
    cols_table = mode_table(MX, fx, jnp.arange(fx, dtype=jnp.int32))
    along_depth = jnp.einsum("abe,az->zbe", kl_coeffs[0], depth_table, precision=GRID)
    along_rows = jnp.einsum("zbe,by->zye", along_depth, rows_table, precision=GRID)
    kl = jnp.dot(along_rows.reshape(k0_planes * fy, MX), cols_table,
                 precision=GRID).reshape(k0_planes, fy, fx)
    k0 = jnp.exp(log_perm + kl)
    k0 = jnp.where(plane_mask(k0_first, k0_planes, fine_total), k0, 0.0)
    k0_halo = (k0_planes - fz) // 2

    k1 = 0.125 * restrict_sum(k0)
    k1_halo = k0_halo // 2
    own1 = fz // 2
    k2_own = 0.125 * restrict_sum(k1[k1_halo:k1_halo + own1])

    h0k = F0_HALO + 1
    lvl0 = Level(k0[k0_halo - h0k: k0_halo + fz + h0k], h0k, fz, s * fz - h0k, fine_total)
    f0 = jnp.concatenate([got_l[crow:].reshape(F0_HALO, fy, fx), source,
                          got_r[crow:].reshape(F0_HALO, fy, fx)], axis=0)
    u = lvl0.start(f0, F0_HALO)
    u1 = lvl0.sweep(u, lvl0.cut(f0, F0_HALO - 1, F0_HALO), F0_HALO)
    res0 = f0[F0_HALO:F0_HALO + fz] - lvl0.operate(u1[1:-1], 1)
    f1_own = 0.5 * restrict_sum(res0)

    h1k = F1_HALO + 1
    extra = h1k - k1_halo
    from_left = shift_from(jnp.concatenate([k1[own1 - extra: own1], f1_own]), 1)
    from_right = shift_from(jnp.concatenate([f1_own, k1[2 * k1_halo: 2 * k1_halo + extra]]), -1)
    k1_ext = jnp.concatenate([from_left[:extra], k1, from_right[own1:]], axis=0)
    f1 = jnp.concatenate([from_left[extra:], f1_own, from_right[:own1]], axis=0)
    lvl1 = Level(k1_ext, h1k, own1, s * own1 - h1k, fine_total // 2)
    v = lvl1.start(f1, F1_HALO)
    v1 = lvl1.sweep(v, lvl1.cut(f1, F1_HALO - 1, F1_HALO), F1_HALO)
    res1 = f1_own - lvl1.operate(v1[2:-2], 1)
    both = gather_window(jnp.stack([0.5 * restrict_sum(res1), k2_own]))

    own2 = own1 // 2
    total2 = fine_total // 4
    k2_halo = 13
    f2_halo = k2_halo - 1
    reach = (both.shape[0] // 2) * own2
    f2w = both[:, 0].reshape((-1,) + both.shape[3:])[reach - f2_halo: reach + own2 + f2_halo]
    k2w = both[:, 1].reshape((-1,) + both.shape[3:])[reach - k2_halo: reach + own2 + k2_halo]
    lvl2 = Level(k2w, k2_halo, own2, s * own2 - k2_halo, total2)
    w = lvl2.start(f2w, f2_halo)
    w1 = lvl2.sweep(w, lvl2.cut(f2w, f2_halo - 1, f2_halo), f2_halo)
    res2 = lvl2.cut(f2w, f2_halo - 2, f2_halo) - lvl2.operate(w1, f2_halo - 1)
    f3 = 0.5 * restrict_sum(res2)
    f3_halo = (f2_halo - 2) // 2
    k3 = 0.125 * restrict_sum(k2w[1:-1])
    lvl3 = Level(k3, f3_halo + 1, own2 // 2, s * (own2 // 2) - f3_halo - 1, total2 // 2)
    b = lvl3.start(f3, f3_halo)
    for step in range(BOTTOM - 1):
        h = f3_halo - step
        b = lvl3.sweep(b, lvl3.cut(f3, h - 1, f3_halo), h)
    e3_halo = f3_halo - (BOTTOM - 1)
    cut2 = (f2_halo - 1) - 2 * e3_halo
    w = w1[cut2:w1.shape[0] - cut2] + copy_up(b)
    h = 2 * e3_halo
    for _ in range(SWEEPS):
        w = lvl2.sweep(w, lvl2.cut(f2w, h - 1, f2_halo), h)
        h -= 1
    e2 = w

    v = v1 + copy_up(e2)[1:-1]
    v = lvl1.sweep(v, lvl1.cut(f1, 2, F1_HALO), 3)
    e1 = lvl1.sweep(v, lvl1.cut(f1, 1, F1_HALO), 2)

    u = u1 + copy_up(e1)
    u = lvl0.sweep(u, lvl0.cut(f0, 1, F0_HALO), 2)
    u = lvl0.sweep(u, source, 1)
    return u[None]


def solution(mesh):
    return jax.shard_map(
        on_device,
        mesh=mesh,
        in_specs=(
            P("chain", None, "slab", None, None),
            P("chain", None),
            P(),
            P("chain", None, None, None),
            P("slab", None, None),
        ),
        out_specs=P("chain", "slab", None, None),
        check_vma=False,
    )
```
